32 devices in a mesh: space: 4 (over y, x), scen: 8 (over z, core).
Axes of the slice: x: 2, y: 2, z: 4, core: 2. Of those that a mesh axis runs over, the one named last changes fastest.
Arguments:
- tracers: float32 [8, 2, 20, 32, 512], P('scen', None, None, None, 'space'), may hold values from -6 to 6
- diffusivity: float32 [2, 20, 32, 512], P(None, None, 'scen', 'space'), may hold values from 0.02 to 0.16
- level_count: int32 [32, 512], P(None, 'space'), may hold values from 0 to 20
- shelf_mask: int32 [32, 512], P(None, 'space'), may hold values 0 or 1
- cotangent: float32 [8, 2, 20, 32, 512], P('scen', None, None, None, 'space'), may hold values from -6 to 6
Outputs:
- final_tracers: float32 [8, 2, 20, 32, 512], P('scen', None, None, None, 'space')
- adjoint_tracers: float32 [8, 2, 20, 32, 512], P('scen', None, None, None, 'space')
- kappa_grad: float32 [2, 20, 32, 512], P(None, None, 'scen', 'space')
The draws below stay inside these ranges and needn't reach their ends.
Inputs may be any that keep to these rules, and one draw needn't show every extreme that they name: `level_count`: wet levels of a column, counted from the surface; 0 marks land.
All inputs are finite; a program needn't handle non-finite values. No bound on the sum of `shelf_mask` on one device may be relied on, other than what follows from the above.
Results may differ from the reference program's by a relative error of at most 0.00002.
Values sent between devices are 32-bit elements; how exact they have to be, the bound alone decides.
No kernel may reach another device: no remote copies, remote signals or barrier semaphores. Data moves between devices by JAX's collectives and lax.ppermute only.
A program may use at most 64 MiB of HBM per device.

```python
import math
import jax
import jax.numpy as jnp
from jax import lax

NY = 32
LEV = 20
STEPS = 2
NX = 512
SCEN = 8


def set_ends(entries, stream_key, smallest, top_value):
    longest = entries.shape.index(max(entries.shape))
    spots = []
    for shift in (0, 1):
        where = [jax.random.randint(jax.random.fold_in(stream_key, axis), (), 0, length) for axis, length in enumerate(entries.shape)]
        where[longest] = (where[longest] + shift) % entries.shape[longest]
        spots.append(tuple(where))
    return entries.at[spots[0]].set(smallest).at[spots[1]].set(top_value)


def spiked(entries, key, source, target, shards_of, factor):
    def block_of(dim):
        return (jnp.arange(entries.shape[dim]) // (entries.shape[dim] // shards_of)).reshape((-1,) + (1,) * (entries.ndim - 1 - dim))

    near = jax.random.permutation(key, shards_of)[block_of(target)]
    other_side = (block_of(target) + shards_of // 2) % shards_of
    return jnp.where((block_of(source) == near) | (block_of(source) == other_side), factor * entries, entries)


def block_levels(stream_key, dims, split, low, largest):
    def one(position, shards_of):
        steps = jax.random.uniform(jax.random.fold_in(jax.random.fold_in(stream_key, 6), position), (shards_of,), jnp.float32, low / len(split), largest / len(split))
        return jnp.repeat(jnp.exp(steps), dims[position] // shards_of).reshape((-1,) + (1,) * (len(dims) - position - 1))

    level = one(*split[0])
    for cut in split[1:]:
        level = level * one(*cut)
    return level


def bell_draw(key, dims, spread, bound, split=(), kind=jnp.bfloat16):
    drawn = jax.random.normal(key, dims, jnp.float32) * spread
    if len(split) > 0:
        drawn = block_levels(key, dims, split, -0.22, 0.18) * drawn
    return jnp.clip(drawn, min=-bound, max=bound).astype(kind)


def bell_draw_with(rng, shape, deviation, limit, cuts, heavy, kind=jnp.bfloat16):
    result = deviation * jax.random.normal(rng, shape, jnp.float32)
    if cuts:
        result = result * block_levels(rng, shape, cuts, -0.22, 0.18)
    return jnp.clip(spiked(result, jax.random.fold_in(rng, 3), *heavy), -limit, limit).astype(kind)


def setup_inputs(seed: int = 0) -> dict:
    keys = jax.random.split(jax.random.key(seed), 6)
    return {
        "tracers": bell_draw(keys[0], (SCEN, 2, LEV, NY, NX), 1.0, 6.0, ((0, 8), (4, 4)), jnp.float32),
        "diffusivity": jnp.clip(jnp.exp(math.log(0.16) - 2.0794415 * jax.random.uniform(keys[1], (2, LEV, NY, NX), jnp.float32) ** block_levels(keys[1], (2, LEV, NY, NX), ((2, 8), (3, 4)), -0.2, 0.2)), 0.02, 0.16),
        "level_count": set_ends(jax.random.randint(keys[2], (NY, NX), 0, LEV + 1), jax.random.fold_in(keys[2], 1), 0, LEV).astype(jnp.int32),
        "shelf_mask": set_ends((jax.random.randint(keys[3], (NY, NX), 0, 2) < 1).astype(jnp.int32), jax.random.fold_in(keys[3], 1), 0, 1),
        "cotangent": bell_draw_with(keys[4], (SCEN, 2, LEV, NY, NX), 1.0, 6.0, ((0, 8), (4, 4)), (0, 3, 8, 2.0), jnp.float32),
    }


vertical_rate = 0.1
thaw_rate = 0.3

def wetness_of(level_count):
    levels = jnp.arange(LEV)[:, None, None]
    return (levels < level_count[None]).astype(jnp.float32)

def sources_of(wetness, shelf_mask):
    below_wet = jnp.concatenate([wetness[1:], jnp.zeros_like(wetness[:1])], axis=0)
    heat_source = thaw_rate * shelf_mask.astype(wetness.dtype)[None] * wetness * (1.0 - below_wet)
    return jnp.stack([heat_source, jnp.zeros_like(heat_source)])

def operate(tracer_now, diffusivity, wetness):
    east_kappa = diffusivity[0]
    north_kappa = diffusivity[1]
    east_coeff = east_kappa * wetness * jnp.roll(wetness, -1, axis=2)
    east_flux = east_coeff * (jnp.roll(tracer_now, -1, axis=3) - tracer_now)
    across_x = east_flux - jnp.roll(east_flux, 1, axis=3)
    north_coeff = north_kappa[:, :-1] * wetness[:, :-1] * wetness[:, 1:]
    north_flux = north_coeff * (tracer_now[:, :, 1:] - tracer_now[:, :, :-1])
    top_wet = wetness[:, -1]
    top_kappa = north_kappa[:, -1]
    fold_coeff = 0.5 * (top_kappa + top_kappa[:, ::-1]) * top_wet * top_wet[:, ::-1]
    top_row = tracer_now[:, :, -1]
    fold_flux = fold_coeff * (top_row[:, :, ::-1] - top_row)
    all_north = jnp.concatenate([north_flux, fold_flux[:, :, None]], axis=2)
    zero_row = jnp.zeros_like(all_north[:, :, :1])
    across_y = all_north - jnp.concatenate([zero_row, all_north[:, :, :-1]], axis=2)
    down_coeff = vertical_rate * wetness[:-1] * wetness[1:]
    down_flux = down_coeff * (tracer_now[:, 1:] - tracer_now[:, :-1])
    zero_level = jnp.zeros_like(down_flux[:, :1])
    across_z = jnp.concatenate([down_flux, zero_level], axis=1) - jnp.concatenate([zero_level, down_flux], axis=1)
    return across_x + across_y + across_z

def forward(tracer_now, diffusivity, wetness, sources):
    for substep in range(STEPS):
        tracer_now = wetness * (tracer_now + operate(tracer_now, diffusivity, wetness) + sources)
    return tracer_now

def reference(tracers, diffusivity, level_count, shelf_mask, cotangent):
    wetness = wetness_of(level_count)
    sources = sources_of(wetness, shelf_mask)

    def advance(initial, field_kappa):
        return forward(initial, field_kappa, wetness, sources)

    def one_scenario(summed, scenario_pair):
        initial, seed_cot = scenario_pair
        final_field, pull_back = jax.vjp(advance, initial, diffusivity)
        adjoint, kappa_part = pull_back(seed_cot)
        return (summed + kappa_part, (final_field, adjoint))
    summed, (finals, adjoints) = lax.scan(one_scenario, jnp.zeros_like(diffusivity), (tracers, cotangent))
    return (finals, adjoints, summed)
```

```python
import jax
import jax.numpy as jnp
from jax import lax
from jax.experimental import pallas as pl
from jax.experimental.pallas import tpu as pltpu
from jax.sharding import PartitionSpec as P

STEPS = 2
HALO = 2

vertical_rate = 0.1
thaw_rate = 0.3

INTERPRET = False


def shifted(x, perm):
    return lax.ppermute(x, "space", perm)


def extended(fields, lanes, rows):
    n = lax.axis_size("space")
    count, ny, width = fields.shape
    west = shifted(fields[..., width - HALO:], [(q, (q + 1) % n) for q in range(n)])
    east = shifted(fields[..., :HALO], [(q, (q - 1) % n) for q in range(n)])
    mirrored = fields[:, ny - 1:ny - 3:-1, ::-1]
    ghost = shifted(mirrored, [(q, n - 1 - q) for q in range(n)])
    ghost_east = shifted(mirrored[..., :HALO], [(q, (n - 2 - q) % n) for q in range(n)])
    ghost_west = shifted(mirrored[..., width - HALO:], [(q, (n - q) % n) for q in range(n)])
    gap = lanes - width - 2 * HALO
    top = jnp.concatenate(
        [fields, east, jnp.zeros((count, ny, gap), fields.dtype), west], axis=-1
    )
    folded = jnp.concatenate(
        [ghost, ghost_east, jnp.zeros((count, 2, gap), fields.dtype), ghost_west], axis=-1
    )
    pad = jnp.zeros((count, rows - ny - 2, lanes), fields.dtype)
    return jnp.concatenate([top, folded, pad], axis=1)


def roll(x, shift, axis):
    return pltpu.roll(x, shift % x.shape[axis], axis)


def diffusion_kernel(
    ue_ref, ve_ref, ke_ref, kn_ref, lev_ref, shelf_ref,
    fin_ref, adj_ref, grad_ref,
    wet_ref, ce_ref, cn_ref, cz_ref, src_ref, gem_ref, gnm_ref, u1_ref, a_ref, b_ref,
):
    levels, rows, lanes = wet_ref.shape
    ny, width = fin_ref.shape[2:]
    row = lax.broadcasted_iota(jnp.int32, (rows, lanes), 0)
    lane = lax.broadcasted_iota(jnp.int32, (rows, lanes), 1)
    owned = (row < ny) & (lane < width)
    lev = lev_ref[...]
    shelf = shelf_ref[...]

    def wet_of(k):
        return (lev > k.astype(jnp.float32)).astype(jnp.float32)

    cz_ref[0] = jnp.zeros((rows, lanes), jnp.float32)

    def setup(k, carry):
        w = wet_of(k)
        w_next = jnp.where(k + 1 < levels, wet_of(k + 1), 0.0)
        w_east = roll(w, -1, 1)
        w_north = roll(w, -1, 0)
        ke = ke_ref[k]
        ke_sel = jnp.where(row >= ny, roll(ke, -1, 1), ke)
        east_mask = w * w_east
        ce_ref[k] = ke_sel * east_mask
        kn = kn_ref[k]
        kn_up = roll(kn, -1, 0)
        kn_sel = jnp.where(
            row < ny - 1, kn, jnp.where(row == ny - 1, 0.5 * (kn + kn_up), jnp.where(row == ny, kn_up, 0.0))
        )
        north_mask = w * w_north
        cn_ref[k] = kn_sel * north_mask
        cz_ref[k + 1] = vertical_rate * w * w_next
        src_ref[k] = thaw_rate * shelf * w * (1.0 - w_next)
        wet_ref[k] = w
        gem_ref[k] = jnp.where(owned, east_mask, 0.0)
        gnm_ref[k] = jnp.where(
            owned, jnp.where(row < ny - 1, north_mask, jnp.where(row == ny - 1, 0.5 * north_mask, 0.0)), 0.0
        )
        return carry

    lax.fori_loop(0, levels, setup, 0)

    def operate(x_ref, c, k):
        x = x_ref[c, k]
        above = x_ref[c, jnp.minimum(k + 1, levels - 1)]
        below = x_ref[c, jnp.maximum(k - 1, 0)]
        east = ce_ref[k] * (roll(x, -1, 1) - x)
        north = cn_ref[k] * (roll(x, -1, 0) - x)
        change = (east - roll(east, 1, 1)) + (north - roll(north, 1, 0))
        change = change + (cz_ref[k + 1] * (above - x) - cz_ref[k] * (x - below))
        return x, change

    planes = 2 * levels

    def forward_first(ck, carry):
        c = ck // levels
        k = ck % levels
        x, change = operate(ue_ref, c, k)
        heat = jnp.where(c == 0, 1.0, 0.0)
        u1_ref[c, k] = wet_ref[k] * (x + change + heat * src_ref[k])
        return carry

    lax.fori_loop(0, planes, forward_first, 0)

    def forward_second(ck, carry):
        c = ck // levels
        k = ck % levels
        x, change = operate(u1_ref, c, k)
        heat = jnp.where(c == 0, 1.0, 0.0)
        out = wet_ref[k] * (x + change + heat * src_ref[k])
        fin_ref[c, k] = out[:ny, :width]
        return carry

    lax.fori_loop(0, planes, forward_second, 0)

    def weigh(ck, carry):
        c = ck // levels
        k = ck % levels
        a_ref[c, k] = wet_ref[k] * ve_ref[c, k]
        return carry

    lax.fori_loop(0, planes, weigh, 0)

    def backward_second(ck, carry):
        c = ck // levels
        k = ck % levels
        x, change = operate(a_ref, c, k)
        b_ref[c, k] = wet_ref[k] * (x + change)
        return carry

    lax.fori_loop(0, planes, backward_second, 0)

    def backward_first(ck, carry):
        c = ck // levels
        k = ck % levels
        x, change = operate(b_ref, c, k)
        adj_ref[c, k] = (x + change)[:ny, :width]
        return carry

    lax.fori_loop(0, planes, backward_first, 0)

    def gradient(k, carry):
        gem = gem_ref[k]
        gnm = gnm_ref[k]
        g_east = jnp.zeros((rows, lanes), jnp.float32)
        g_north = jnp.zeros((rows, lanes), jnp.float32)
        for c in range(2):
            for u_ref, v_ref in ((ue_ref, b_ref), (u1_ref, a_ref)):
                u = u_ref[c, k]
                v = v_ref[c, k]
                g_east = g_east + (roll(u, -1, 1) - u) * (v - roll(v, -1, 1))
                g_north = g_north + (roll(u, -1, 0) - u) * (v - roll(v, -1, 0))
        grad_ref[0, k] = (gem * g_east)[:ny, :width]
        grad_ref[1, k] = (gnm * g_north)[:ny, :width]
        return carry

    lax.fori_loop(0, levels, gradient, 0)


def on_device(tracers, diffusivity, level_count, shelf_mask, cotangent):
    _, chans, levels, ny, width = tracers.shape
    lanes = width + 128
    rows = -(-(ny + 2) // 8) * 8
    first = jnp.concatenate(
        [
            tracers[0].reshape(chans * levels, ny, width),
            cotangent[0].reshape(chans * levels, ny, width),
            level_count.astype(jnp.float32)[None],
            shelf_mask.astype(jnp.float32)[None],
        ]
    )
    first_ext = extended(first, lanes, rows)
    full_kappa = lax.all_gather(diffusivity, "scen", axis=2, tiled=True)
    kappa_ext = extended(full_kappa.reshape(2 * levels, ny, width), lanes, rows)
    planes = chans * levels
    ue = first_ext[:planes].reshape(chans, levels, rows, lanes)
    ve = first_ext[planes:2 * planes].reshape(chans, levels, rows, lanes)
    lev = first_ext[2 * planes]
    shelf = first_ext[2 * planes + 1]
    ke = kappa_ext[:levels]
    kn = kappa_ext[levels:]
    field = jax.ShapeDtypeStruct((chans, levels, ny, width), jnp.float32)
    plane = pltpu.VMEM((levels, rows, lanes), jnp.float32)
    planes_c = pltpu.VMEM((chans, levels, rows, lanes), jnp.float32)
    final, adjoint, grad = pl.pallas_call(
        diffusion_kernel,
        out_shape=(field, field, jax.ShapeDtypeStruct((2, levels, ny, width), jnp.float32)),
        scratch_shapes=[
            plane,
            plane,
            plane,
            pltpu.VMEM((levels + 1, rows, lanes), jnp.float32),
            plane,
            plane,
            plane,
            planes_c,
            planes_c,
            planes_c,
        ],
        compiler_params=pltpu.CompilerParams(vmem_limit_bytes=48 * 1024 * 1024),
        interpret=INTERPRET,
    )(ue, ve, ke, kn, lev, shelf)
    kappa_grad = lax.psum_scatter(grad, "scen", scatter_dimension=2, tiled=True)
    return (final[None], adjoint[None], kappa_grad)


def solution(mesh):
    placed = (
        P("scen", None, None, None, "space"),
        P(None, None, "scen", "space"),
        P(None, "space"),
        P(None, "space"),
        P("scen", None, None, None, "space"),
    )
    return jax.shard_map(
        on_device,
        mesh=mesh,
        in_specs=placed,
        out_specs=(
            P("scen", None, None, None, "space"),
            P("scen", None, None, None, "space"),
            P(None, None, "scen", "space"),
        ),
        check_vma=False,
    )
```

```python
import jax
import jax.numpy as jnp
from jax import lax
from jax.experimental import pallas as pl
from jax.experimental.pallas import tpu as pltpu
from jax.sharding import PartitionSpec as P

STEPS = 2
HALO = 2

vertical_rate = 0.1
thaw_rate = 0.3

INTERPRET = False


def shifted(x, perm):
    return lax.ppermute(x, "space", perm)


def extended(fields, lanes, rows):
    n = lax.axis_size("space")
    count, ny, width = fields.shape
    west = shifted(fields[..., width - HALO:], [(q, (q + 1) % n) for q in range(n)])
    east = shifted(fields[..., :HALO], [(q, (q - 1) % n) for q in range(n)])
    mirrored = fields[:, ny - 1:ny - 3:-1, ::-1]
    ghost = shifted(mirrored, [(q, n - 1 - q) for q in range(n)])
    ghost_east = shifted(mirrored[..., :HALO], [(q, (n - 2 - q) % n) for q in range(n)])
    ghost_west = shifted(mirrored[..., width - HALO:], [(q, (n - q) % n) for q in range(n)])
    gap = lanes - width - 2 * HALO
    top = jnp.concatenate(
        [fields, east, jnp.zeros((count, ny, gap), fields.dtype), west], axis=-1
    )
    folded = jnp.concatenate(
        [ghost, ghost_east, jnp.zeros((count, 2, gap), fields.dtype), ghost_west], axis=-1
    )
    pad = jnp.zeros((count, rows - ny - 2, lanes), fields.dtype)
    return jnp.concatenate([top, folded, pad], axis=1)


def roll(x, shift, axis):
    return pltpu.roll(x, shift % x.shape[axis], axis)


class Planes:
    def __init__(self, ref, start, levels):
        self.ref = ref
        self.start = start
        self.levels = levels

    def __getitem__(self, index):
        c, k = index
        return self.ref[self.start + c * self.levels + k]


def diffusion_kernel(
    x_ref,
    fin_ref, adj_ref, grad_ref,
    wet_ref, ce_ref, cn_ref, cz_ref, src_ref, gem_ref, gnm_ref, u1_ref, a_ref, b_ref,
):
    levels, rows, lanes = wet_ref.shape
    chans, _, ny, width = fin_ref.shape
    row = lax.broadcasted_iota(jnp.int32, (rows, lanes), 0)
    lane = lax.broadcasted_iota(jnp.int32, (rows, lanes), 1)
    owned = (row < ny) & (lane < width)
    planes = chans * levels
    ue_ref = Planes(x_ref, 0, levels)
    ve_ref = Planes(x_ref, planes, levels)
    ke_ref = Planes(x_ref, 2 * planes, levels)
    lev = x_ref[2 * planes + 2 * levels]
    shelf = x_ref[2 * planes + 2 * levels + 1]

    def wet_of(k):
        return (lev > k.astype(jnp.float32)).astype(jnp.float32)

    cz_ref[0] = jnp.zeros((rows, lanes), jnp.float32)

    def setup(k, carry):
        w = wet_of(k)
        w_next = jnp.where(k + 1 < levels, wet_of(k + 1), 0.0)
        w_east = roll(w, -1, 1)
        w_north = roll(w, -1, 0)
        ke = ke_ref[0, k]
        ke_sel = jnp.where(row >= ny, roll(ke, -1, 1), ke)
        east_mask = w * w_east
        ce_ref[k] = ke_sel * east_mask
        kn = ke_ref[1, k]
        kn_up = roll(kn, -1, 0)
        kn_sel = jnp.where(
            row < ny - 1, kn, jnp.where(row == ny - 1, 0.5 * (kn + kn_up), jnp.where(row == ny, kn_up, 0.0))
        )
        north_mask = w * w_north
        cn_ref[k] = kn_sel * north_mask
        cz_ref[k + 1] = vertical_rate * w * w_next
        src_ref[k] = thaw_rate * shelf * w * (1.0 - w_next)
        wet_ref[k] = w
        gem_ref[k] = jnp.where(owned, east_mask, 0.0)
        gnm_ref[k] = jnp.where(
            owned, jnp.where(row < ny - 1, north_mask, jnp.where(row == ny - 1, 0.5 * north_mask, 0.0)), 0.0
        )
        return carry

    lax.fori_loop(0, levels, setup, 0)

    def operate(x_ref, c, k):
        x = x_ref[c, k]
        above = x_ref[c, jnp.minimum(k + 1, levels - 1)]
        below = x_ref[c, jnp.maximum(k - 1, 0)]
        east = ce_ref[k] * (roll(x, -1, 1) - x)
        north = cn_ref[k] * (roll(x, -1, 0) - x)
        change = (east - roll(east, 1, 1)) + (north - roll(north, 1, 0))
        change = change + (cz_ref[k + 1] * (above - x) - cz_ref[k] * (x - below))
        return x, change

    def forward_first(ck, carry):
        c = ck // levels
        k = ck % levels
        x, change = operate(ue_ref, c, k)
        heat = jnp.where(c == 0, 1.0, 0.0)
        u1_ref[c, k] = wet_ref[k] * (x + change + heat * src_ref[k])
        return carry

    lax.fori_loop(0, planes, forward_first, 0)

    def forward_second(ck, carry):
        c = ck // levels
        k = ck % levels
        x, change = operate(u1_ref, c, k)
        heat = jnp.where(c == 0, 1.0, 0.0)
        out = wet_ref[k] * (x + change + heat * src_ref[k])
        fin_ref[c, k] = out[:ny, :width]
        return carry

    lax.fori_loop(0, planes, forward_second, 0)

    def weigh(ck, carry):
        c = ck // levels
        k = ck % levels
        a_ref[c, k] = wet_ref[k] * ve_ref[c, k]
        return carry

    lax.fori_loop(0, planes, weigh, 0)

    def backward_second(ck, carry):
        c = ck // levels
        k = ck % levels
        x, change = operate(a_ref, c, k)
        b_ref[c, k] = wet_ref[k] * (x + change)
        return carry

    lax.fori_loop(0, planes, backward_second, 0)

    def backward_first(ck, carry):
        c = ck // levels
        k = ck % levels
        x, change = operate(b_ref, c, k)
        adj_ref[c, k] = (x + change)[:ny, :width]
        return carry

    lax.fori_loop(0, planes, backward_first, 0)

    def gradient(k, carry):
        gem = gem_ref[k]
        gnm = gnm_ref[k]
        g_east = jnp.zeros((rows, lanes), jnp.float32)
        g_north = jnp.zeros((rows, lanes), jnp.float32)
        for c in range(2):
            for u_ref, v_ref in ((ue_ref, b_ref), (u1_ref, a_ref)):
                u = u_ref[c, k]
                v = v_ref[c, k]
                g_east = g_east + (roll(u, -1, 1) - u) * (v - roll(v, -1, 1))
                g_north = g_north + (roll(u, -1, 0) - u) * (v - roll(v, -1, 0))
        grad_ref[0, k] = (gem * g_east)[:ny, :width]
        grad_ref[1, k] = (gnm * g_north)[:ny, :width]
        return carry

    lax.fori_loop(0, levels, gradient, 0)


def on_device(tracers, diffusivity, level_count, shelf_mask, cotangent):
    _, chans, levels, ny, width = tracers.shape
    lanes = width + 128
    rows = -(-(ny + 2) // 8) * 8
    full_kappa = lax.all_gather(diffusivity, "scen", axis=2, tiled=True)
    fields = jnp.concatenate(
        [
            tracers[0].reshape(chans * levels, ny, width),
            cotangent[0].reshape(chans * levels, ny, width),
            full_kappa.reshape(2 * levels, ny, width),
            level_count.astype(jnp.float32)[None],
            shelf_mask.astype(jnp.float32)[None],
        ]
    )
    ext = extended(fields, lanes, rows)
    field = jax.ShapeDtypeStruct((chans, levels, ny, width), jnp.float32)
    plane = pltpu.VMEM((levels, rows, lanes), jnp.float32)
    planes_c = pltpu.VMEM((chans, levels, rows, lanes), jnp.float32)
    final, adjoint, grad = pl.pallas_call(
        diffusion_kernel,
        out_shape=(field, field, jax.ShapeDtypeStruct((2, levels, ny, width), jnp.float32)),
        scratch_shapes=[
            plane,
            plane,
            plane,
            pltpu.VMEM((levels + 1, rows, lanes), jnp.float32),
            plane,
            plane,
            plane,
            planes_c,
            planes_c,
            planes_c,
        ],
        compiler_params=pltpu.CompilerParams(vmem_limit_bytes=48 * 1024 * 1024),
        interpret=INTERPRET,
    )(ext)
    parts = lax.axis_size("scen")
    split = grad.reshape(2, levels, parts, ny // parts, width)
    gathered = lax.all_to_all(split, "scen", 2, 2, tiled=True)
    kappa_grad = gathered.sum(axis=2)
    return (final[None], adjoint[None], kappa_grad)


def solution(mesh):
    placed = (
        P("scen", None, None, None, "space"),
        P(None, None, "scen", "space"),
        P(None, "space"),
        P(None, "space"),
        P("scen", None, None, None, "space"),
    )
    return jax.shard_map(
        on_device,
        mesh=mesh,
        in_specs=placed,
        out_specs=(
            P("scen", None, None, None, "space"),
            P("scen", None, None, None, "space"),
            P(None, None, "scen", "space"),
        ),
        check_vma=False,
    )
```

```python
import jax
import jax.numpy as jnp
from jax import lax
from jax.experimental import pallas as pl
from jax.experimental.pallas import tpu as pltpu
from jax.sharding import PartitionSpec as P

STEPS = 2
HALO = 2

vertical_rate = 0.1
thaw_rate = 0.3

INTERPRET = False


def shifted(x, perm):
    return lax.ppermute(x, "space", perm)


def picker(size, positions):
    where = lax.broadcasted_iota(jnp.int32, (size, len(positions)), 0)
    slot = lax.broadcasted_iota(jnp.int32, (size, len(positions)), 1)
    hit = jnp.zeros((size, len(positions)), jnp.bool_)
    for p, at in enumerate(positions):
        hit = hit | ((slot == p) & (where == at))
    return hit.astype(jnp.float32)


def contract(a, b, dims):
    return lax.dot_general(
        a, b, (dims, ((), ())), precision=lax.Precision.HIGHEST, preferred_element_type=jnp.float32
    )


def extended(fields, lanes, rows):
    n = lax.axis_size("space")
    count, ny, width = fields.shape
    spare = lanes - width
    flat = fields.reshape(count * ny, width)
    edges = contract(picker(width, [width - 2, width - 1, 0, 1]), flat, ((0,), (1,)))
    west = shifted(edges[0:2], [(q, (q + 1) % n) for q in range(n)])
    east = shifted(edges[2:4], [(q, (q - 1) % n) for q in range(n)])
    mirrored = fields[:, ny - 1:ny - 3:-1, ::-1]
    ghost = shifted(mirrored, [(q, n - 1 - q) for q in range(n)])
    top_edges = edges.reshape(4, count, ny)[:, :, ny - 1:ny - 3:-1]
    ghost_east = shifted(top_edges[1::-1], [(q, (n - 2 - q) % n) for q in range(n)])
    ghost_west = shifted(top_edges[3:1:-1], [(q, (n - q) % n) for q in range(n)])
    place = picker(spare, [0, 1, spare - 2, spare - 1]).T
    side = contract(jnp.concatenate([east, west]), place, ((0,), (0,))).reshape(count, ny, spare)
    ghost_halo = jnp.concatenate([ghost_east, ghost_west]).reshape(4, count * 2)
    ghost_side = contract(ghost_halo, place, ((0,), (0,))).reshape(count, 2, spare)
    top = jnp.concatenate([fields, side], axis=-1)
    folded = jnp.concatenate([ghost, ghost_side], axis=-1)
    pad = jnp.zeros((count, rows - ny - 2, lanes), fields.dtype)
    return jnp.concatenate([top, folded, pad], axis=1)


def roll(x, shift, axis):
    return pltpu.roll(x, shift % x.shape[axis], axis)


class Planes:
    def __init__(self, ref, start, levels):
        self.ref = ref
        self.start = start
        self.levels = levels

    def __getitem__(self, index):
        c, k = index
        return self.ref[self.start + c * self.levels + k]


def diffusion_kernel(
    x_ref,
    fin_ref, adj_ref, grad_ref,
    wet_ref, ce_ref, cn_ref, cz_ref, src_ref, gem_ref, gnm_ref, u1_ref, a_ref, b_ref,
):
    levels, rows, lanes = wet_ref.shape
    chans, _, ny, width = fin_ref.shape
    row = lax.broadcasted_iota(jnp.int32, (rows, lanes), 0)
    lane = lax.broadcasted_iota(jnp.int32, (rows, lanes), 1)
    owned = (row < ny) & (lane < width)
    planes = chans * levels
    ue_ref = Planes(x_ref, 0, levels)
    ve_ref = Planes(x_ref, planes, levels)
    ke_ref = Planes(x_ref, 2 * planes, levels)
    lev = x_ref[2 * planes + 2 * levels]
    shelf = x_ref[2 * planes + 2 * levels + 1]

    def wet_of(k):
        return (lev > k.astype(jnp.float32)).astype(jnp.float32)

    cz_ref[0] = jnp.zeros((rows, lanes), jnp.float32)

    def setup(k, carry):
        w = wet_of(k)
        w_next = jnp.where(k + 1 < levels, wet_of(k + 1), 0.0)
        w_east = roll(w, -1, 1)
        w_north = roll(w, -1, 0)
        ke = ke_ref[0, k]
        ke_sel = jnp.where(row >= ny, roll(ke, -1, 1), ke)
        east_mask = w * w_east
        ce_ref[k] = ke_sel * east_mask
        kn = ke_ref[1, k]
        kn_up = roll(kn, -1, 0)
        kn_sel = jnp.where(
            row < ny - 1, kn, jnp.where(row == ny - 1, 0.5 * (kn + kn_up), jnp.where(row == ny, kn_up, 0.0))
        )
        north_mask = w * w_north
        cn_ref[k] = kn_sel * north_mask
        cz_ref[k + 1] = vertical_rate * w * w_next
        src_ref[k] = thaw_rate * shelf * w * (1.0 - w_next)
        wet_ref[k] = w
        gem_ref[k] = jnp.where(owned, east_mask, 0.0)
        gnm_ref[k] = jnp.where(
            owned, jnp.where(row < ny - 1, north_mask, jnp.where(row == ny - 1, 0.5 * north_mask, 0.0)), 0.0
        )
        return carry

    lax.fori_loop(0, levels, setup, 0)

    def operate(x_ref, c, k):
        x = x_ref[c, k]
        above = x_ref[c, jnp.minimum(k + 1, levels - 1)]
        below = x_ref[c, jnp.maximum(k - 1, 0)]
        east = ce_ref[k] * (roll(x, -1, 1) - x)
        north = cn_ref[k] * (roll(x, -1, 0) - x)
        change = (east - roll(east, 1, 1)) + (north - roll(north, 1, 0))
        change = change + (cz_ref[k + 1] * (above - x) - cz_ref[k] * (x - below))
        return x, change

    def forward_first(ck, carry):
        c = ck // levels
        k = ck % levels
        x, change = operate(ue_ref, c, k)
        heat = jnp.where(c == 0, 1.0, 0.0)
        u1_ref[c, k] = wet_ref[k] * (x + change + heat * src_ref[k])
        return carry

    lax.fori_loop(0, planes, forward_first, 0)

    def forward_second(ck, carry):
        c = ck // levels
        k = ck % levels
        x, change = operate(u1_ref, c, k)
        heat = jnp.where(c == 0, 1.0, 0.0)
        out = wet_ref[k] * (x + change + heat * src_ref[k])
        fin_ref[c, k] = out[:ny, :width]
        return carry

    lax.fori_loop(0, planes, forward_second, 0)

    def weigh(ck, carry):
        c = ck // levels
        k = ck % levels
        a_ref[c, k] = wet_ref[k] * ve_ref[c, k]
        return carry

    lax.fori_loop(0, planes, weigh, 0)

    def backward_second(ck, carry):
        c = ck // levels
        k = ck % levels
        x, change = operate(a_ref, c, k)
        b_ref[c, k] = wet_ref[k] * (x + change)
        return carry

    lax.fori_loop(0, planes, backward_second, 0)

    def backward_first(ck, carry):
        c = ck // levels
        k = ck % levels
        x, change = operate(b_ref, c, k)
        adj_ref[c, k] = (x + change)[:ny, :width]
        return carry

    lax.fori_loop(0, planes, backward_first, 0)

    def gradient(k, carry):
        gem = gem_ref[k]
        gnm = gnm_ref[k]
        g_east = jnp.zeros((rows, lanes), jnp.float32)
        g_north = jnp.zeros((rows, lanes), jnp.float32)
        for c in range(2):
            for u_ref, v_ref in ((ue_ref, b_ref), (u1_ref, a_ref)):
                u = u_ref[c, k]
                v = v_ref[c, k]
                g_east = g_east + (roll(u, -1, 1) - u) * (v - roll(v, -1, 1))
                g_north = g_north + (roll(u, -1, 0) - u) * (v - roll(v, -1, 0))
        grad_ref[0, k] = (gem * g_east)[:ny, :width]
        grad_ref[1, k] = (gnm * g_north)[:ny, :width]
        return carry

    lax.fori_loop(0, levels, gradient, 0)


def on_device(tracers, diffusivity, level_count, shelf_mask, cotangent):
    _, chans, levels, ny, width = tracers.shape
    lanes = width + 128
    rows = -(-(ny + 2) // 8) * 8
    full_kappa = lax.all_gather(diffusivity, "scen", axis=2, tiled=True)
    fields = jnp.concatenate(
        [
            tracers[0].reshape(chans * levels, ny, width),
            cotangent[0].reshape(chans * levels, ny, width),
            full_kappa.reshape(2 * levels, ny, width),
            level_count.astype(jnp.float32)[None],
            shelf_mask.astype(jnp.float32)[None],
        ]
    )
    ext = extended(fields, lanes, rows)
    field = jax.ShapeDtypeStruct((chans, levels, ny, width), jnp.float32)
    plane = pltpu.VMEM((levels, rows, lanes), jnp.float32)
    planes_c = pltpu.VMEM((chans, levels, rows, lanes), jnp.float32)
    final, adjoint, grad = pl.pallas_call(
        diffusion_kernel,
        out_shape=(field, field, jax.ShapeDtypeStruct((2, levels, ny, width), jnp.float32)),
        scratch_shapes=[
            plane,
            plane,
            plane,
            pltpu.VMEM((levels + 1, rows, lanes), jnp.float32),
            plane,
            plane,
            plane,
            planes_c,
            planes_c,
            planes_c,
        ],
        compiler_params=pltpu.CompilerParams(vmem_limit_bytes=48 * 1024 * 1024),
        interpret=INTERPRET,
    )(ext)
    parts = lax.axis_size("scen")
    split = grad.reshape(2, levels, parts, ny // parts, width)
    gathered = lax.all_to_all(split, "scen", 2, 2, tiled=True)
    kappa_grad = gathered.sum(axis=2)
    return (final[None], adjoint[None], kappa_grad)


def solution(mesh):
    placed = (
        P("scen", None, None, None, "space"),
        P(None, None, "scen", "space"),
        P(None, "space"),
        P(None, "space"),
        P("scen", None, None, None, "space"),
    )
    return jax.shard_map(
        on_device,
        mesh=mesh,
        in_specs=placed,
        out_specs=(
            P("scen", None, None, None, "space"),
            P("scen", None, None, None, "space"),
            P(None, None, "scen", "space"),
        ),
        check_vma=False,
    )
```

```python
import jax
import jax.numpy as jnp
from jax import lax
from jax.experimental import pallas as pl
from jax.experimental.pallas import tpu as pltpu
from jax.sharding import PartitionSpec as P

STEPS = 2
HALO = 2

vertical_rate = 0.1
thaw_rate = 0.3

INTERPRET = False


def shifted(x, perm):
    return lax.ppermute(x, "space", perm)


def picker(size, positions):
    where = lax.broadcasted_iota(jnp.int32, (size, len(positions)), 0)
    slot = lax.broadcasted_iota(jnp.int32, (size, len(positions)), 1)
    hit = jnp.zeros((size, len(positions)), jnp.bool_)
    for p, at in enumerate(positions):
        hit = hit | ((slot == p) & (where == at))
    return hit.astype(jnp.float32)


def contract(a, b, dims):
    return lax.dot_general(
        a, b, (dims, ((), ())), precision=lax.Precision.HIGHEST, preferred_element_type=jnp.float32
    )


def extended(fields, lanes, rows):
    n = lax.axis_size("space")
    count, ny, width = fields.shape
    spare = lanes - width
    flat = fields.reshape(count * ny, width)
    edges = contract(picker(width, [width - 2, width - 1, 0, 1]), flat, ((0,), (1,)))
    west = shifted(edges[0:2], [(q, (q + 1) % n) for q in range(n)])
    east = shifted(edges[2:4], [(q, (q - 1) % n) for q in range(n)])
    mirrored = fields[:, ny - 1:ny - 3:-1, ::-1]
    ghost = shifted(mirrored, [(q, n - 1 - q) for q in range(n)])
    top_edges = edges.reshape(4, count, ny)[:, :, ny - 1:ny - 3:-1]
    ghost_east = shifted(top_edges[1::-1], [(q, (n - 2 - q) % n) for q in range(n)])
    ghost_west = shifted(top_edges[3:1:-1], [(q, (n - q) % n) for q in range(n)])
    place = picker(spare, [0, 1, spare - 2, spare - 1]).T
    side = contract(jnp.concatenate([east, west]), place, ((0,), (0,))).reshape(count, ny, spare)
    ghost_halo = jnp.concatenate([ghost_east, ghost_west]).reshape(4, count * 2)
    ghost_side = contract(ghost_halo, place, ((0,), (0,))).reshape(count, 2, spare)
    top = jnp.concatenate([fields, side], axis=-1)
    folded = jnp.concatenate([ghost, ghost_side], axis=-1)
    pad = jnp.zeros((count, rows - ny - 2, lanes), fields.dtype)
    return jnp.concatenate([top, folded, pad], axis=1)


def roll(x, shift, axis):
    return pltpu.roll(x, shift % x.shape[axis], axis)


class Planes:
    def __init__(self, ref, start, levels):
        self.ref = ref
        self.start = start
        self.levels = levels

    def __getitem__(self, index):
        c, k = index
        return self.ref[self.start + c * self.levels + k]


def diffusion_kernel(
    x_ref,
    fin_ref, adj_ref, grad_ref,
    wet_ref, ce_ref, cn_ref, cz_ref, src_ref, gem_ref, gnm_ref, u1_ref, a_ref, b_ref,
):
    levels, rows, lanes = wet_ref.shape
    chans, _, ny, width = fin_ref.shape
    row = lax.broadcasted_iota(jnp.int32, (rows, lanes), 0)
    lane = lax.broadcasted_iota(jnp.int32, (rows, lanes), 1)
    owned = (row < ny) & (lane < width)
    planes = chans * levels
    ue_ref = Planes(x_ref, 0, levels)
    ve_ref = Planes(x_ref, planes, levels)
    ke_ref = Planes(x_ref, 2 * planes, levels)
    lev = x_ref[2 * planes + 2 * levels]
    shelf = x_ref[2 * planes + 2 * levels + 1]

    def wet_of(k):
        return (lev > k.astype(jnp.float32)).astype(jnp.float32)

    cz_ref[0] = jnp.zeros((rows, lanes), jnp.float32)

    def setup(k, carry):
        w = wet_of(k)
        w_next = jnp.where(k + 1 < levels, wet_of(k + 1), 0.0)
        w_east = roll(w, -1, 1)
        w_north = roll(w, -1, 0)
        ke = ke_ref[0, k]
        ke_sel = jnp.where(row >= ny, roll(ke, -1, 1), ke)
        east_mask = w * w_east
        ce_ref[k] = ke_sel * east_mask
        kn = ke_ref[1, k]
        kn_up = roll(kn, -1, 0)
        kn_sel = jnp.where(
            row < ny - 1, kn, jnp.where(row == ny - 1, 0.5 * (kn + kn_up), jnp.where(row == ny, kn_up, 0.0))
        )
        north_mask = w * w_north
        cn_ref[k] = kn_sel * north_mask
        cz_ref[k + 1] = vertical_rate * w * w_next
        src_ref[k] = thaw_rate * shelf * w * (1.0 - w_next)
        wet_ref[k] = w
        gem_ref[k] = jnp.where(owned, east_mask, 0.0)
        gnm_ref[k] = jnp.where(
            owned, jnp.where(row < ny - 1, north_mask, jnp.where(row == ny - 1, 0.5 * north_mask, 0.0)), 0.0
        )
        return carry

    lax.fori_loop(0, levels, setup, 0)

    def operate(x_ref, c, k):
        x = x_ref[c, k]
        above = x_ref[c, jnp.minimum(k + 1, levels - 1)]
        below = x_ref[c, jnp.maximum(k - 1, 0)]
        east = ce_ref[k] * (roll(x, -1, 1) - x)
        north = cn_ref[k] * (roll(x, -1, 0) - x)
        change = (east - roll(east, 1, 1)) + (north - roll(north, 1, 0))
        change = change + (cz_ref[k + 1] * (above - x) - cz_ref[k] * (x - below))
        return x, change

    def forward_first(ck, carry):
        c = ck // levels
        k = ck % levels
        x, change = operate(ue_ref, c, k)
        heat = jnp.where(c == 0, 1.0, 0.0)
        u1_ref[c, k] = wet_ref[k] * (x + change + heat * src_ref[k])
        return carry

    lax.fori_loop(0, planes, forward_first, 0)

    def forward_second(ck, carry):
        c = ck // levels
        k = ck % levels
        x, change = operate(u1_ref, c, k)
        heat = jnp.where(c == 0, 1.0, 0.0)
        out = wet_ref[k] * (x + change + heat * src_ref[k])
        fin_ref[c, k] = out[:ny, :width]
        return carry

    lax.fori_loop(0, planes, forward_second, 0)

    def weigh(ck, carry):
        c = ck // levels
        k = ck % levels
        a_ref[c, k] = wet_ref[k] * ve_ref[c, k]
        return carry

    lax.fori_loop(0, planes, weigh, 0)

    def backward_second(ck, carry):
        c = ck // levels
        k = ck % levels
        x, change = operate(a_ref, c, k)
        b_ref[c, k] = wet_ref[k] * (x + change)
        return carry

    lax.fori_loop(0, planes, backward_second, 0)

    def backward_first(ck, carry):
        c = ck // levels
        k = ck % levels
        x, change = operate(b_ref, c, k)
        adj_ref[c, k] = (x + change)[:ny, :width]
        return carry

    lax.fori_loop(0, planes, backward_first, 0)

    def gradient(k, carry):
        gem = gem_ref[k]
        gnm = gnm_ref[k]
        g_east = jnp.zeros((rows, lanes), jnp.float32)
        g_north = jnp.zeros((rows, lanes), jnp.float32)
        for c in range(2):
            for u_ref, v_ref in ((ue_ref, b_ref), (u1_ref, a_ref)):
                u = u_ref[c, k]
                v = v_ref[c, k]
                g_east = g_east + (roll(u, -1, 1) - u) * (v - roll(v, -1, 1))
                g_north = g_north + (roll(u, -1, 0) - u) * (v - roll(v, -1, 0))
        grad_ref[0, k] = (gem * g_east)[:ny, :width]
        grad_ref[1, k] = (gnm * g_north)[:ny, :width]
        return carry

    lax.fori_loop(0, levels, gradient, 0)


def on_device(tracers, diffusivity, level_count, shelf_mask, cotangent):
    _, chans, levels, ny, width = tracers.shape
    lanes = width + 128
    rows = -(-(ny + 2) // 8) * 8
    full_kappa = lax.all_gather(diffusivity, "scen", axis=2, tiled=True)
    fields = jnp.concatenate(
        [
            tracers[0].reshape(chans * levels, ny, width),
            cotangent[0].reshape(chans * levels, ny, width),
            full_kappa.reshape(2 * levels, ny, width),
            level_count.astype(jnp.float32)[None],
            shelf_mask.astype(jnp.float32)[None],
        ]
    )
    ext = extended(fields, lanes, rows)
    field = jax.ShapeDtypeStruct((chans, levels, ny, width), jnp.float32)
    plane = pltpu.VMEM((levels, rows, lanes), jnp.float32)
    planes_c = pltpu.VMEM((chans, levels, rows, lanes), jnp.float32)
    final, adjoint, grad = pl.pallas_call(
        diffusion_kernel,
        out_shape=(field, field, jax.ShapeDtypeStruct((2, levels, ny, width), jnp.float32)),
        scratch_shapes=[
            plane,
            plane,
            plane,
            pltpu.VMEM((levels + 1, rows, lanes), jnp.float32),
            plane,
            plane,
            plane,
            planes_c,
            planes_c,
            planes_c,
        ],
        compiler_params=pltpu.CompilerParams(vmem_limit_bytes=48 * 1024 * 1024),
        interpret=INTERPRET,
    )(ext)
    kappa_grad = summed_over_scen(grad)
    return (final[None], adjoint[None], kappa_grad)


def summed_over_scen(grad):
    parts = lax.axis_size("scen")
    kinds, levels, ny, width = grad.shape
    if parts % 2:
        split = grad.reshape(kinds, levels, parts, ny // parts, width)
        return lax.all_to_all(split, "scen", 2, 2, tiled=True).sum(axis=2)
    me = lax.axis_index("scen")
    core = me % 2
    chip = me // 2
    chips = parts // 2
    split = grad.reshape(kinds, levels, chips, 2, ny // parts, width)
    mine = lax.dynamic_index_in_dim(split, core, axis=3, keepdims=False)
    other = lax.dynamic_index_in_dim(split, 1 - core, axis=3, keepdims=False)
    pair = lax.ppermute(other, "scen", [(q, q ^ 1) for q in range(parts)])
    chip_sum = mine + pair
    total = lax.dynamic_index_in_dim(chip_sum, chip, axis=2, keepdims=False)
    for step in range(1, chips):
        send = lax.dynamic_index_in_dim(chip_sum, (chip + step) % chips, axis=2, keepdims=False)
        total = total + lax.ppermute(
            send, "scen", [(q, ((q // 2 + step) % chips) * 2 + q % 2) for q in range(parts)]
        )
    return total


def solution(mesh):
    placed = (
        P("scen", None, None, None, "space"),
        P(None, None, "scen", "space"),
        P(None, "space"),
        P(None, "space"),
        P("scen", None, None, None, "space"),
    )
    return jax.shard_map(
        on_device,
        mesh=mesh,
        in_specs=placed,
        out_specs=(
            P("scen", None, None, None, "space"),
            P("scen", None, None, None, "space"),
            P(None, None, "scen", "space"),
        ),
        check_vma=False,
    )
```

```python
import jax
import jax.numpy as jnp
from jax import lax
from jax.experimental import pallas as pl
from jax.experimental.pallas import tpu as pltpu
from jax.sharding import PartitionSpec as P

STEPS = 2
HALO = 2

vertical_rate = 0.1
thaw_rate = 0.3

INTERPRET = False


def shifted(x, perm):
    return lax.ppermute(x, "space", perm)


def picker(size, positions):
    where = lax.broadcasted_iota(jnp.int32, (size, len(positions)), 0)
    slot = lax.broadcasted_iota(jnp.int32, (size, len(positions)), 1)
    hit = jnp.zeros((size, len(positions)), jnp.bool_)
    for p, at in enumerate(positions):
        hit = hit | ((slot == p) & (where == at))
    return hit.astype(jnp.float32)


def contract(a, b, dims):
    return lax.dot_general(
        a, b, (dims, ((), ())), precision=lax.Precision.HIGHEST, preferred_element_type=jnp.float32
    )


def extended(fields, lanes, rows):
    n = lax.axis_size("space")
    count, ny, width = fields.shape
    spare = lanes - width
    flat = fields.reshape(count * ny, width)
    edges = contract(picker(width, [width - 2, width - 1, 0, 1]), flat, ((0,), (1,)))
    west = shifted(edges[0:2], [(q, (q + 1) % n) for q in range(n)])
    east = shifted(edges[2:4], [(q, (q - 1) % n) for q in range(n)])
    mirrored = fields[:, ny - 1:ny - 3:-1, ::-1]
    ghost = shifted(mirrored, [(q, n - 1 - q) for q in range(n)])
    top_edges = edges.reshape(4, count, ny)[:, :, ny - 1:ny - 3:-1]
    ghost_east = shifted(top_edges[1::-1], [(q, (n - 2 - q) % n) for q in range(n)])
    ghost_west = shifted(top_edges[3:1:-1], [(q, (n - q) % n) for q in range(n)])
    place = picker(spare, [0, 1, spare - 2, spare - 1]).T
    side = contract(jnp.concatenate([east, west]), place, ((0,), (0,))).reshape(count, ny, spare)
    ghost_halo = jnp.concatenate([ghost_east, ghost_west]).reshape(4, count * 2)
    ghost_side = contract(ghost_halo, place, ((0,), (0,))).reshape(count, 2, spare)
    top = jnp.concatenate([fields, side], axis=-1)
    folded = jnp.concatenate([ghost, ghost_side], axis=-1)
    pad = jnp.zeros((count, rows - ny - 2, lanes), fields.dtype)
    return jnp.concatenate([top, folded, pad], axis=1)


def roll(x, shift, axis):
    return pltpu.roll(x, shift % x.shape[axis], axis)


class Planes:
    def __init__(self, ref, start, levels):
        self.ref = ref
        self.start = start
        self.levels = levels

    def __getitem__(self, index):
        c, k = index
        return self.ref[self.start + c * self.levels + k]


def coefficients(x_ref, wet_ref, ce_ref, cn_ref, cz_ref, src_ref, ny, width, masks=None):
    levels, rows, lanes = wet_ref.shape
    row = lax.broadcasted_iota(jnp.int32, (rows, lanes), 0)
    lane = lax.broadcasted_iota(jnp.int32, (rows, lanes), 1)
    owned = (row < ny) & (lane < width)
    ke_ref = Planes(x_ref, 0, levels)
    lev = x_ref[2 * levels]
    shelf = x_ref[2 * levels + 1]

    def wet_of(k):
        return (lev > k.astype(jnp.float32)).astype(jnp.float32)

    cz_ref[0] = jnp.zeros((rows, lanes), jnp.float32)

    def setup(k, carry):
        w = wet_of(k)
        w_next = jnp.where(k + 1 < levels, wet_of(k + 1), 0.0)
        w_east = roll(w, -1, 1)
        w_north = roll(w, -1, 0)
        ke = ke_ref[0, k]
        ke_sel = jnp.where(row >= ny, roll(ke, -1, 1), ke)
        east_mask = w * w_east
        ce_ref[k] = ke_sel * east_mask
        kn = ke_ref[1, k]
        kn_up = roll(kn, -1, 0)
        kn_sel = jnp.where(
            row < ny - 1, kn, jnp.where(row == ny - 1, 0.5 * (kn + kn_up), jnp.where(row == ny, kn_up, 0.0))
        )
        north_mask = w * w_north
        cn_ref[k] = kn_sel * north_mask
        cz_ref[k + 1] = vertical_rate * w * w_next
        src_ref[k] = thaw_rate * shelf * w * (1.0 - w_next)
        wet_ref[k] = w
        if masks is not None:
            gem_ref, gnm_ref = masks
            gem_ref[k] = jnp.where(owned, east_mask, 0.0)
            gnm_ref[k] = jnp.where(
                owned, jnp.where(row < ny - 1, north_mask, jnp.where(row == ny - 1, 0.5 * north_mask, 0.0)), 0.0
            )
        return carry

    lax.fori_loop(0, levels, setup, 0)

    def operate(x_ref, c, k):
        x = x_ref[c, k]
        above = x_ref[c, jnp.minimum(k + 1, levels - 1)]
        below = x_ref[c, jnp.maximum(k - 1, 0)]
        east = ce_ref[k] * (roll(x, -1, 1) - x)
        north = cn_ref[k] * (roll(x, -1, 0) - x)
        change = (east - roll(east, 1, 1)) + (north - roll(north, 1, 0))
        change = change + (cz_ref[k + 1] * (above - x) - cz_ref[k] * (x - below))
        return x, change

    return operate


def gradient_kernel(
    x_ref, grad_ref, u1_ref, b_ref,
    wet_ref, ce_ref, cn_ref, cz_ref, src_ref, gem_ref, gnm_ref, a_ref,
):
    levels, rows, lanes = wet_ref.shape
    chans = u1_ref.shape[0]
    ny, width = grad_ref.shape[2:]
    operate = coefficients(x_ref, wet_ref, ce_ref, cn_ref, cz_ref, src_ref, ny, width, (gem_ref, gnm_ref))
    planes = chans * levels
    ue_ref = Planes(x_ref, 2 * levels + 2, levels)
    ve_ref = Planes(x_ref, 2 * levels + 2 + planes, levels)

    def forward_first(ck, carry):
        c = ck // levels
        k = ck % levels
        x, change = operate(ue_ref, c, k)
        heat = jnp.where(c == 0, 1.0, 0.0)
        u1_ref[c, k] = wet_ref[k] * (x + change + heat * src_ref[k])
        return carry

    lax.fori_loop(0, planes, forward_first, 0)

    def weigh(ck, carry):
        c = ck // levels
        k = ck % levels
        a_ref[c, k] = wet_ref[k] * ve_ref[c, k]
        return carry

    lax.fori_loop(0, planes, weigh, 0)

    def backward_second(ck, carry):
        c = ck // levels
        k = ck % levels
        x, change = operate(a_ref, c, k)
        b_ref[c, k] = wet_ref[k] * (x + change)
        return carry

    lax.fori_loop(0, planes, backward_second, 0)

    def gradient(k, carry):
        gem = gem_ref[k]
        gnm = gnm_ref[k]
        g_east = jnp.zeros((rows, lanes), jnp.float32)
        g_north = jnp.zeros((rows, lanes), jnp.float32)
        for c in range(chans):
            for u_ref, v_ref in ((ue_ref, b_ref), (u1_ref, a_ref)):
                u = u_ref[c, k]
                v = v_ref[c, k]
                g_east = g_east + (roll(u, -1, 1) - u) * (v - roll(v, -1, 1))
                g_north = g_north + (roll(u, -1, 0) - u) * (v - roll(v, -1, 0))
        grad_ref[0, k] = (gem * g_east)[:ny, :width]
        grad_ref[1, k] = (gnm * g_north)[:ny, :width]
        return carry

    lax.fori_loop(0, levels, gradient, 0)


def finishing_kernel(
    x_ref, u1_ref, b_ref, fin_ref, adj_ref,
    wet_ref, ce_ref, cn_ref, cz_ref, src_ref,
):
    levels = wet_ref.shape[0]
    chans, _, ny, width = fin_ref.shape
    operate = coefficients(x_ref, wet_ref, ce_ref, cn_ref, cz_ref, src_ref, ny, width)
    planes = chans * levels

    def forward_second(ck, carry):
        c = ck // levels
        k = ck % levels
        x, change = operate(u1_ref, c, k)
        heat = jnp.where(c == 0, 1.0, 0.0)
        out = wet_ref[k] * (x + change + heat * src_ref[k])
        fin_ref[c, k] = out[:ny, :width]
        return carry

    lax.fori_loop(0, planes, forward_second, 0)

    def backward_first(ck, carry):
        c = ck // levels
        k = ck % levels
        x, change = operate(b_ref, c, k)
        adj_ref[c, k] = (x + change)[:ny, :width]
        return carry

    lax.fori_loop(0, planes, backward_first, 0)


def on_device(tracers, diffusivity, level_count, shelf_mask, cotangent):
    _, chans, levels, ny, width = tracers.shape
    lanes = width + 128
    rows = -(-(ny + 2) // 8) * 8
    full_kappa = lax.all_gather(diffusivity, "scen", axis=2, tiled=True)
    fields = jnp.concatenate(
        [
            full_kappa.reshape(2 * levels, ny, width),
            level_count.astype(jnp.float32)[None],
            shelf_mask.astype(jnp.float32)[None],
            tracers[0].reshape(chans * levels, ny, width),
            cotangent[0].reshape(chans * levels, ny, width),
        ]
    )
    ext = extended(fields, lanes, rows)
    field = jax.ShapeDtypeStruct((chans, levels, ny, width), jnp.float32)
    state = jax.ShapeDtypeStruct((chans, levels, rows, lanes), jnp.float32)
    plane = pltpu.VMEM((levels, rows, lanes), jnp.float32)
    planes_c = pltpu.VMEM((chans, levels, rows, lanes), jnp.float32)
    heights = pltpu.VMEM((levels + 1, rows, lanes), jnp.float32)
    params = pltpu.CompilerParams(vmem_limit_bytes=48 * 1024 * 1024)
    grad, u1, b = pl.pallas_call(
        gradient_kernel,
        out_shape=(jax.ShapeDtypeStruct((2, levels, ny, width), jnp.float32), state, state),
        scratch_shapes=[plane, plane, plane, heights, plane, plane, plane, planes_c],
        compiler_params=params,
        interpret=INTERPRET,
    )(ext)
    coeff_planes = 2 * levels + 2
    final, adjoint = pl.pallas_call(
        finishing_kernel,
        out_shape=(field, field),
        grid=(1,),
        in_specs=[
            pl.BlockSpec((coeff_planes, rows, lanes), lambda i: (0, 0, 0)),
            pl.BlockSpec(state.shape, lambda i: (0, 0, 0, 0)),
            pl.BlockSpec(state.shape, lambda i: (0, 0, 0, 0)),
        ],
        out_specs=[pl.BlockSpec(field.shape, lambda i: (0, 0, 0, 0))] * 2,
        scratch_shapes=[plane, plane, plane, heights, plane],
        compiler_params=params,
        interpret=INTERPRET,
    )(ext, u1, b)
    kappa_grad = summed_over_scen(grad)
    return (final[None], adjoint[None], kappa_grad)


def summed_over_scen(grad):
    parts = lax.axis_size("scen")
    kinds, levels, ny, width = grad.shape
    if parts % 2:
        split = grad.reshape(kinds, levels, parts, ny // parts, width)
        return lax.all_to_all(split, "scen", 2, 2, tiled=True).sum(axis=2)
    me = lax.axis_index("scen")
    core = me % 2
    chip = me // 2
    chips = parts // 2
    split = grad.reshape(kinds, levels, chips, 2, ny // parts, width)
    mine = lax.dynamic_index_in_dim(split, core, axis=3, keepdims=False)
    other = lax.dynamic_index_in_dim(split, 1 - core, axis=3, keepdims=False)
    pair = lax.ppermute(other, "scen", [(q, q ^ 1) for q in range(parts)])
    chip_sum = mine + pair
    total = lax.dynamic_index_in_dim(chip_sum, chip, axis=2, keepdims=False)
    for step in range(1, chips):
        send = lax.dynamic_index_in_dim(chip_sum, (chip + step) % chips, axis=2, keepdims=False)
        total = total + lax.ppermute(
            send, "scen", [(q, ((q // 2 + step) % chips) * 2 + q % 2) for q in range(parts)]
        )
    return total


def solution(mesh):
    placed = (
        P("scen", None, None, None, "space"),
        P(None, None, "scen", "space"),
        P(None, "space"),
        P(None, "space"),
        P("scen", None, None, None, "space"),
    )
    return jax.shard_map(
        on_device,
        mesh=mesh,
        in_specs=placed,
        out_specs=(
            P("scen", None, None, None, "space"),
            P("scen", None, None, None, "space"),
            P(None, None, "scen", "space"),
        ),
        check_vma=False,
    )
```

```python
import jax
import jax.numpy as jnp
from jax import lax
from jax.experimental import pallas as pl
from jax.experimental.pallas import tpu as pltpu
from jax.sharding import PartitionSpec as P

STEPS = 2
HALO = 2

vertical_rate = 0.1
thaw_rate = 0.3

INTERPRET = False


def shifted(x, perm):
    return lax.ppermute(x, "space", perm)


def picker(size, positions):
    where = lax.broadcasted_iota(jnp.int32, (size, len(positions)), 0)
    slot = lax.broadcasted_iota(jnp.int32, (size, len(positions)), 1)
    hit = jnp.zeros((size, len(positions)), jnp.bool_)
    for p, at in enumerate(positions):
        hit = hit | ((slot == p) & (where == at))
    return hit.astype(jnp.float32)


def contract(a, b, dims):
    return lax.dot_general(
        a, b, (dims, ((), ())), precision=lax.Precision.HIGHEST, preferred_element_type=jnp.float32
    )


def extended(fields, lanes, rows):
    n = lax.axis_size("space")
    count, ny, width = fields.shape
    spare = lanes - width
    mirrored = fields[:, ny - 1:ny - 3:-1, ::-1]
    ghost = shifted(mirrored, [(q, n - 1 - q) for q in range(n)])
    pick = picker(width, [width - 2, width - 1, 0, 1])
    edges = jnp.concatenate(
        [
            contract(pick, fields.reshape(count * ny, width), ((0,), (1,))),
            contract(pick, ghost.reshape(count * 2, width), ((0,), (1,))),
        ],
        axis=1,
    )
    west = shifted(edges[0:2], [(q, (q + 1) % n) for q in range(n)])
    east = shifted(edges[2:4], [(q, (q - 1) % n) for q in range(n)])
    place = picker(spare, [0, 1, spare - 2, spare - 1]).T
    halo = jnp.concatenate([east, west])
    side = contract(halo[:, :count * ny], place, ((0,), (0,))).reshape(count, ny, spare)
    ghost_side = contract(halo[:, count * ny:], place, ((0,), (0,))).reshape(count, 2, spare)
    top = jnp.concatenate([fields, side], axis=-1)
    folded = jnp.concatenate([ghost, ghost_side], axis=-1)
    pad = jnp.zeros((count, rows - ny - 2, lanes), fields.dtype)
    return jnp.concatenate([top, folded, pad], axis=1)


def roll(x, shift, axis):
    return pltpu.roll(x, shift % x.shape[axis], axis)


class Planes:
    def __init__(self, ref, start, levels):
        self.ref = ref
        self.start = start
        self.levels = levels

    def __getitem__(self, index):
        c, k = index
        return self.ref[self.start + c * self.levels + k]


def diffusion_kernel(
    x_ref,
    fin_ref, adj_ref, grad_ref,
    wet_ref, ce_ref, cn_ref, cz_ref, src_ref, gem_ref, gnm_ref, u1_ref, a_ref, b_ref,
):
    levels, rows, lanes = wet_ref.shape
    chans, _, ny, width = fin_ref.shape
    row = lax.broadcasted_iota(jnp.int32, (rows, lanes), 0)
    lane = lax.broadcasted_iota(jnp.int32, (rows, lanes), 1)
    owned = (row < ny) & (lane < width)
    planes = chans * levels
    ue_ref = Planes(x_ref, 0, levels)
    ve_ref = Planes(x_ref, planes, levels)
    ke_ref = Planes(x_ref, 2 * planes, levels)
    lev = x_ref[2 * planes + 2 * levels]
    shelf = x_ref[2 * planes + 2 * levels + 1]

    def wet_of(k):
        return (lev > k.astype(jnp.float32)).astype(jnp.float32)

    cz_ref[0] = jnp.zeros((rows, lanes), jnp.float32)

    def setup(k, carry):
        w = wet_of(k)
        w_next = jnp.where(k + 1 < levels, wet_of(k + 1), 0.0)
        w_east = roll(w, -1, 1)
        w_north = roll(w, -1, 0)
        ke = ke_ref[0, k]
        ke_sel = jnp.where(row >= ny, roll(ke, -1, 1), ke)
        east_mask = w * w_east
        ce_ref[k] = ke_sel * east_mask
        kn = ke_ref[1, k]
        kn_up = roll(kn, -1, 0)
        kn_sel = jnp.where(
            row < ny - 1, kn, jnp.where(row == ny - 1, 0.5 * (kn + kn_up), jnp.where(row == ny, kn_up, 0.0))
        )
        north_mask = w * w_north
        cn_ref[k] = kn_sel * north_mask
        cz_ref[k + 1] = vertical_rate * w * w_next
        src_ref[k] = thaw_rate * shelf * w * (1.0 - w_next)
        wet_ref[k] = w
        gem_ref[k] = jnp.where(owned, east_mask, 0.0)
        gnm_ref[k] = jnp.where(
            owned, jnp.where(row < ny - 1, north_mask, jnp.where(row == ny - 1, 0.5 * north_mask, 0.0)), 0.0
        )
        return carry

    lax.fori_loop(0, levels, setup, 0)

    def operate(x_ref, c, k):
        x = x_ref[c, k]
        above = x_ref[c, jnp.minimum(k + 1, levels - 1)]
        below = x_ref[c, jnp.maximum(k - 1, 0)]
        east = ce_ref[k] * (roll(x, -1, 1) - x)
        north = cn_ref[k] * (roll(x, -1, 0) - x)
        change = (east - roll(east, 1, 1)) + (north - roll(north, 1, 0))
        change = change + (cz_ref[k + 1] * (above - x) - cz_ref[k] * (x - below))
        return x, change

    def forward_first(ck, carry):
        c = ck // levels
        k = ck % levels
        x, change = operate(ue_ref, c, k)
        heat = jnp.where(c == 0, 1.0, 0.0)
        u1_ref[c, k] = wet_ref[k] * (x + change + heat * src_ref[k])
        return carry

    lax.fori_loop(0, planes, forward_first, 0)

    def forward_second(ck, carry):
        c = ck // levels
        k = ck % levels
        x, change = operate(u1_ref, c, k)
        heat = jnp.where(c == 0, 1.0, 0.0)
        out = wet_ref[k] * (x + change + heat * src_ref[k])
        fin_ref[c, k] = out[:ny, :width]
        return carry

    lax.fori_loop(0, planes, forward_second, 0)

    def weigh(ck, carry):
        c = ck // levels
        k = ck % levels
        a_ref[c, k] = wet_ref[k] * ve_ref[c, k]
        return carry

    lax.fori_loop(0, planes, weigh, 0)

    def backward_second(ck, carry):
        c = ck // levels
        k = ck % levels
        x, change = operate(a_ref, c, k)
        b_ref[c, k] = wet_ref[k] * (x + change)
        return carry

    lax.fori_loop(0, planes, backward_second, 0)

    def backward_first(ck, carry):
        c = ck // levels
        k = ck % levels
        x, change = operate(b_ref, c, k)
        adj_ref[c, k] = (x + change)[:ny, :width]
        return carry

    lax.fori_loop(0, planes, backward_first, 0)

    def gradient(k, carry):
        gem = gem_ref[k]
        gnm = gnm_ref[k]
        g_east = jnp.zeros((rows, lanes), jnp.float32)
        g_north = jnp.zeros((rows, lanes), jnp.float32)
        for c in range(2):
            for u_ref, v_ref in ((ue_ref, b_ref), (u1_ref, a_ref)):
                u = u_ref[c, k]
                v = v_ref[c, k]
                g_east = g_east + (roll(u, -1, 1) - u) * (v - roll(v, -1, 1))
                g_north = g_north + (roll(u, -1, 0) - u) * (v - roll(v, -1, 0))
        grad_ref[0, k] = (gem * g_east)[:ny, :width]
        grad_ref[1, k] = (gnm * g_north)[:ny, :width]
        return carry

    lax.fori_loop(0, levels, gradient, 0)


def on_device(tracers, diffusivity, level_count, shelf_mask, cotangent):
    _, chans, levels, ny, width = tracers.shape
    lanes = width + 128
    rows = -(-(ny + 2) // 8) * 8
    full_kappa = lax.all_gather(diffusivity, "scen", axis=2, tiled=True)
    fields = jnp.concatenate(
        [
            tracers[0].reshape(chans * levels, ny, width),
            cotangent[0].reshape(chans * levels, ny, width),
            full_kappa.reshape(2 * levels, ny, width),
            level_count.astype(jnp.float32)[None],
            shelf_mask.astype(jnp.float32)[None],
        ]
    )
    ext = extended(fields, lanes, rows)
    field = jax.ShapeDtypeStruct((chans, levels, ny, width), jnp.float32)
    plane = pltpu.VMEM((levels, rows, lanes), jnp.float32)
    planes_c = pltpu.VMEM((chans, levels, rows, lanes), jnp.float32)
    final, adjoint, grad = pl.pallas_call(
        diffusion_kernel,
        out_shape=(field, field, jax.ShapeDtypeStruct((2, levels, ny, width), jnp.float32)),
        scratch_shapes=[
            plane,
            plane,
            plane,
            pltpu.VMEM((levels + 1, rows, lanes), jnp.float32),
            plane,
            plane,
            plane,
            planes_c,
            planes_c,
            planes_c,
        ],
        compiler_params=pltpu.CompilerParams(vmem_limit_bytes=48 * 1024 * 1024),
        interpret=INTERPRET,
    )(ext)
    kappa_grad = summed_over_scen(grad)
    return (final[None], adjoint[None], kappa_grad)


def summed_over_scen(grad):
    parts = lax.axis_size("scen")
    kinds, levels, ny, width = grad.shape
    if parts % 2:
        split = grad.reshape(kinds, levels, parts, ny // parts, width)
        return lax.all_to_all(split, "scen", 2, 2, tiled=True).sum(axis=2)
    me = lax.axis_index("scen")
    core = me % 2
    chip = me // 2
    chips = parts // 2
    split = grad.reshape(kinds, levels, chips, 2, ny // parts, width)
    mine = lax.dynamic_index_in_dim(split, core, axis=3, keepdims=False)
    other = lax.dynamic_index_in_dim(split, 1 - core, axis=3, keepdims=False)
    pair = lax.ppermute(other, "scen", [(q, q ^ 1) for q in range(parts)])
    chip_sum = mine + pair
    total = lax.dynamic_index_in_dim(chip_sum, chip, axis=2, keepdims=False)
    for step in range(1, chips):
        send = lax.dynamic_index_in_dim(chip_sum, (chip + step) % chips, axis=2, keepdims=False)
        total = total + lax.ppermute(
            send, "scen", [(q, ((q // 2 + step) % chips) * 2 + q % 2) for q in range(parts)]
        )
    return total


def solution(mesh):
    placed = (
        P("scen", None, None, None, "space"),
        P(None, None, "scen", "space"),
        P(None, "space"),
        P(None, "space"),
        P("scen", None, None, None, "space"),
    )
    return jax.shard_map(
        on_device,
        mesh=mesh,
        in_specs=placed,
        out_specs=(
            P("scen", None, None, None, "space"),
            P("scen", None, None, None, "space"),
            P(None, None, "scen", "space"),
        ),
        check_vma=False,
    )
```

```python
import jax
import jax.numpy as jnp
from jax import lax
from jax.experimental import pallas as pl
from jax.experimental.pallas import tpu as pltpu
from jax.sharding import PartitionSpec as P

STEPS = 2
HALO = 2

vertical_rate = 0.1
thaw_rate = 0.3

INTERPRET = False


def shifted(x, perm):
    return lax.ppermute(x, "space", perm)


def picker(size, positions):
    where = lax.broadcasted_iota(jnp.int32, (size, len(positions)), 0)
    slot = lax.broadcasted_iota(jnp.int32, (size, len(positions)), 1)
    hit = jnp.zeros((size, len(positions)), jnp.bool_)
    for p, at in enumerate(positions):
        hit = hit | ((slot == p) & (where == at))
    return hit.astype(jnp.float32)


def contract(a, b, dims):
    return lax.dot_general(
        a, b, (dims, ((), ())), precision=lax.Precision.HIGHEST, preferred_element_type=jnp.float32
    )


def extended(fields, lanes, rows):
    n = lax.axis_size("space")
    count, ny, width = fields.shape
    spare = lanes - width
    mirrored = fields[:, ny - 1:ny - 3:-1, ::-1]
    ghost = shifted(mirrored, [(q, n - 1 - q) for q in range(n)])
    pick = picker(width, [width - 2, width - 1, 0, 1])
    edges = jnp.concatenate(
        [
            contract(pick, fields.reshape(count * ny, width), ((0,), (1,))),
            contract(pick, ghost.reshape(count * 2, width), ((0,), (1,))),
        ],
        axis=1,
    )
    west = shifted(edges[0:2], [(q, (q + 1) % n) for q in range(n)])
    east = shifted(edges[2:4], [(q, (q - 1) % n) for q in range(n)])
    place = picker(spare, [0, 1, spare - 2, spare - 1]).T
    halo = jnp.concatenate([east, west])
    side = contract(halo[:, :count * ny], place, ((0,), (0,))).reshape(count, ny, spare)
    ghost_side = contract(halo[:, count * ny:], place, ((0,), (0,))).reshape(count, 2, spare)
    top = jnp.concatenate([fields, side], axis=-1)
    folded = jnp.concatenate([ghost, ghost_side], axis=-1)
    pad = jnp.zeros((count, rows - ny - 2, lanes), fields.dtype)
    return jnp.concatenate([top, folded, pad], axis=1)


def roll(x, shift, axis):
    return pltpu.roll(x, shift % x.shape[axis], axis)


class Planes:
    def __init__(self, ref, start, levels):
        self.ref = ref
        self.start = start
        self.levels = levels

    def __getitem__(self, index):
        c, k = index
        return self.ref[self.start + c * self.levels + k]


def diffusion_kernel(
    x_ref,
    fin_ref, adj_ref, grad_ref,
    wet_ref, ce_ref, cn_ref, cz_ref, src_ref, gem_ref, gnm_ref, u1_ref, a_ref, b_ref,
    du0e_ref, du0n_ref, du1e_ref, du1n_ref, dv1e_ref, dv1n_ref, dv2e_ref, dv2n_ref,
):
    levels, rows, lanes = wet_ref.shape
    chans, _, ny, width = fin_ref.shape
    row = lax.broadcasted_iota(jnp.int32, (rows, lanes), 0)
    lane = lax.broadcasted_iota(jnp.int32, (rows, lanes), 1)
    planes = chans * levels
    ue_ref = Planes(x_ref, 0, levels)
    ve_ref = Planes(x_ref, planes, levels)
    ke_ref = Planes(x_ref, 2 * planes, levels)
    lev = x_ref[2 * planes + 2 * levels]
    shelf = x_ref[2 * planes + 2 * levels + 1]

    def wet_of(k):
        return (lev > k.astype(jnp.float32)).astype(jnp.float32)

    cz_ref[0] = jnp.zeros((rows, lanes), jnp.float32)

    def setup(k, carry):
        w = wet_of(k)
        w_next = jnp.where(k + 1 < levels, wet_of(k + 1), 0.0)
        w_east = roll(w, -1, 1)
        w_north = roll(w, -1, 0)
        ke = ke_ref[0, k]
        ke_sel = jnp.where(row >= ny, roll(ke, -1, 1), ke)
        east_mask = w * w_east
        ce_ref[k] = ke_sel * east_mask
        kn = ke_ref[1, k]
        kn_up = roll(kn, -1, 0)
        kn_sel = jnp.where(
            row < ny - 1, kn, jnp.where(row == ny - 1, 0.5 * (kn + kn_up), jnp.where(row == ny, kn_up, 0.0))
        )
        north_mask = w * w_north
        cn_ref[k] = kn_sel * north_mask
        cz_ref[k + 1] = vertical_rate * w * w_next
        src_ref[k] = thaw_rate * shelf * w * (1.0 - w_next)
        wet_ref[k] = w
        gem_ref[k] = east_mask[:ny, :width]
        gnm_ref[k] = jnp.where(row < ny - 1, north_mask, 0.5 * north_mask)[:ny, :width]
        for c in range(chans):
            a_ref[c, k] = w * ve_ref[c, k]
        return carry

    lax.fori_loop(0, levels, setup, 0)

    def operate(x_ref, c, k, diffs=None):
        x = x_ref[c, k]
        above = x_ref[c, jnp.minimum(k + 1, levels - 1)]
        below = x_ref[c, jnp.maximum(k - 1, 0)]
        d_east = roll(x, -1, 1) - x
        d_north = roll(x, -1, 0) - x
        if diffs is not None:
            diffs[0][c, k] = d_east[:ny, :width]
            diffs[1][c, k] = d_north[:ny, :width]
        east = ce_ref[k] * d_east
        north = cn_ref[k] * d_north
        change = (east - roll(east, 1, 1)) + (north - roll(north, 1, 0))
        change = change + (cz_ref[k + 1] * (above - x) - cz_ref[k] * (x - below))
        return x, change

    def forward_first(ck, carry):
        c = ck // levels
        k = ck % levels
        x, change = operate(ue_ref, c, k, (du0e_ref, du0n_ref))
        heat = jnp.where(c == 0, 1.0, 0.0)
        u1_ref[c, k] = wet_ref[k] * (x + change + heat * src_ref[k])
        return carry

    lax.fori_loop(0, planes, forward_first, 0)

    def forward_second(ck, carry):
        c = ck // levels
        k = ck % levels
        x, change = operate(u1_ref, c, k, (du1e_ref, du1n_ref))
        heat = jnp.where(c == 0, 1.0, 0.0)
        out = wet_ref[k] * (x + change + heat * src_ref[k])
        fin_ref[c, k] = out[:ny, :width]
        return carry

    lax.fori_loop(0, planes, forward_second, 0)

    def backward_second(ck, carry):
        c = ck // levels
        k = ck % levels
        x, change = operate(a_ref, c, k, (dv2e_ref, dv2n_ref))
        b_ref[c, k] = wet_ref[k] * (x + change)
        return carry

    lax.fori_loop(0, planes, backward_second, 0)

    def backward_first(ck, carry):
        c = ck // levels
        k = ck % levels
        x, change = operate(b_ref, c, k, (dv1e_ref, dv1n_ref))
        adj_ref[c, k] = (x + change)[:ny, :width]
        return carry

    lax.fori_loop(0, planes, backward_first, 0)

    def gradient(k, carry):
        g_east = jnp.zeros((ny, width), jnp.float32)
        g_north = jnp.zeros((ny, width), jnp.float32)
        for c in range(chans):
            g_east = g_east - du0e_ref[c, k] * dv1e_ref[c, k] - du1e_ref[c, k] * dv2e_ref[c, k]
            g_north = g_north - du0n_ref[c, k] * dv1n_ref[c, k] - du1n_ref[c, k] * dv2n_ref[c, k]
        grad_ref[0, k] = gem_ref[k] * g_east
        grad_ref[1, k] = gnm_ref[k] * g_north
        return carry

    lax.fori_loop(0, levels, gradient, 0)


def on_device(tracers, diffusivity, level_count, shelf_mask, cotangent):
    _, chans, levels, ny, width = tracers.shape
    lanes = width + 128
    rows = -(-(ny + 2) // 8) * 8
    full_kappa = lax.all_gather(diffusivity, "scen", axis=2, tiled=True)
    fields = jnp.concatenate(
        [
            tracers[0].reshape(chans * levels, ny, width),
            cotangent[0].reshape(chans * levels, ny, width),
            full_kappa.reshape(2 * levels, ny, width),
            level_count.astype(jnp.float32)[None],
            shelf_mask.astype(jnp.float32)[None],
        ]
    )
    ext = extended(fields, lanes, rows)
    field = jax.ShapeDtypeStruct((chans, levels, ny, width), jnp.float32)
    plane = pltpu.VMEM((levels, rows, lanes), jnp.float32)
    planes_c = pltpu.VMEM((chans, levels, rows, lanes), jnp.float32)
    diff = pltpu.VMEM((chans, levels, ny, width), jnp.float32)
    mask = pltpu.VMEM((levels, ny, width), jnp.float32)
    final, adjoint, grad = pl.pallas_call(
        diffusion_kernel,
        out_shape=(field, field, jax.ShapeDtypeStruct((2, levels, ny, width), jnp.float32)),
        scratch_shapes=[
            plane,
            plane,
            plane,
            pltpu.VMEM((levels + 1, rows, lanes), jnp.float32),
            plane,
            mask,
            mask,
            planes_c,
            planes_c,
            planes_c,
        ]
        + [diff] * 8,
        compiler_params=pltpu.CompilerParams(vmem_limit_bytes=48 * 1024 * 1024),
        interpret=INTERPRET,
    )(ext)
    kappa_grad = summed_over_scen(grad)
    return (final[None], adjoint[None], kappa_grad)


def summed_over_scen(grad):
    parts = lax.axis_size("scen")
    kinds, levels, ny, width = grad.shape
    if parts % 2:
        split = grad.reshape(kinds, levels, parts, ny // parts, width)
        return lax.all_to_all(split, "scen", 2, 2, tiled=True).sum(axis=2)
    me = lax.axis_index("scen")
    core = me % 2
    chip = me // 2
    chips = parts // 2
    split = grad.reshape(kinds, levels, chips, 2, ny // parts, width)
    mine = lax.dynamic_index_in_dim(split, core, axis=3, keepdims=False)
    other = lax.dynamic_index_in_dim(split, 1 - core, axis=3, keepdims=False)
    pair = lax.ppermute(other, "scen", [(q, q ^ 1) for q in range(parts)])
    chip_sum = mine + pair
    total = lax.dynamic_index_in_dim(chip_sum, chip, axis=2, keepdims=False)
    for step in range(1, chips):
        send = lax.dynamic_index_in_dim(chip_sum, (chip + step) % chips, axis=2, keepdims=False)
        total = total + lax.ppermute(
            send, "scen", [(q, ((q // 2 + step) % chips) * 2 + q % 2) for q in range(parts)]
        )
    return total


def solution(mesh):
    placed = (
        P("scen", None, None, None, "space"),
        P(None, None, "scen", "space"),
        P(None, "space"),
        P(None, "space"),
        P("scen", None, None, None, "space"),
    )
    return jax.shard_map(
        on_device,
        mesh=mesh,
        in_specs=placed,
        out_specs=(
            P("scen", None, None, None, "space"),
            P("scen", None, None, None, "space"),
            P(None, None, "scen", "space"),
        ),
        check_vma=False,
    )
```

```python
import jax
import jax.numpy as jnp
from jax import lax
from jax.experimental import pallas as pl
from jax.experimental.pallas import tpu as pltpu
from jax.sharding import PartitionSpec as P

STEPS = 2
HALO = 2

vertical_rate = 0.1
thaw_rate = 0.3

INTERPRET = False


def shifted(x, perm):
    return lax.ppermute(x, "space", perm)


def picker(size, positions):
    where = lax.broadcasted_iota(jnp.int32, (size, len(positions)), 0)
    slot = lax.broadcasted_iota(jnp.int32, (size, len(positions)), 1)
    hit = jnp.zeros((size, len(positions)), jnp.bool_)
    for p, at in enumerate(positions):
        hit = hit | ((slot == p) & (where == at))
    return hit.astype(jnp.float32)


def contract(a, b, dims):
    return lax.dot_general(
        a, b, (dims, ((), ())), precision=lax.Precision.HIGHEST, preferred_element_type=jnp.float32
    )


def extended(fields, lanes, rows):
    n = lax.axis_size("space")
    count, ny, width = fields.shape
    spare = lanes - width
    mirrored = fields[:, ny - 1:ny - 3:-1, ::-1]
    ghost = shifted(mirrored, [(q, n - 1 - q) for q in range(n)])
    pick = picker(width, [width - 2, width - 1, 0, 1])
    edges = jnp.concatenate(
        [
            contract(pick, fields.reshape(count * ny, width), ((0,), (1,))),
            contract(pick, ghost.reshape(count * 2, width), ((0,), (1,))),
        ],
        axis=1,
    )
    west = shifted(edges[0:2], [(q, (q + 1) % n) for q in range(n)])
    east = shifted(edges[2:4], [(q, (q - 1) % n) for q in range(n)])
    place = picker(spare, [0, 1, spare - 2, spare - 1]).T
    halo = jnp.concatenate([east, west])
    side = contract(halo[:, :count * ny], place, ((0,), (0,))).reshape(count, ny, spare)
    ghost_side = contract(halo[:, count * ny:], place, ((0,), (0,))).reshape(count, 2, spare)
    top = jnp.concatenate([fields, side], axis=-1)
    folded = jnp.concatenate([ghost, ghost_side], axis=-1)
    pad = jnp.zeros((count, rows - ny - 2, lanes), fields.dtype)
    return jnp.concatenate([top, folded, pad], axis=1)


def roll(x, shift, axis):
    return pltpu.roll(x, shift % x.shape[axis], axis)


class Planes:
    def __init__(self, ref, start, levels):
        self.ref = ref
        self.start = start
        self.levels = levels

    def __getitem__(self, index):
        c, k = index
        return self.ref[self.start + c * self.levels + k]


def diffusion_kernel(
    x_ref,
    fin_ref, adj_ref, grad_ref,
    wet_ref, ce_ref, cn_ref, cz_ref, src_ref, gem_ref, gnm_ref, u1_ref, a_ref, b_ref,
    du0e_ref, du0n_ref, du1e_ref, du1n_ref, dv1e_ref, dv1n_ref, dv2e_ref, dv2n_ref,
):
    levels, rows, lanes = wet_ref.shape
    chans, _, ny, width = fin_ref.shape
    row = lax.broadcasted_iota(jnp.int32, (rows, lanes), 0)
    lane = lax.broadcasted_iota(jnp.int32, (rows, lanes), 1)
    planes = chans * levels
    ue_ref = Planes(x_ref, 0, levels)
    ve_ref = Planes(x_ref, planes, levels)
    ke_ref = Planes(x_ref, 2 * planes, levels)
    lev = x_ref[2 * planes + 2 * levels]
    shelf = x_ref[2 * planes + 2 * levels + 1]

    def wet_of(k):
        return (lev > k.astype(jnp.float32)).astype(jnp.float32)

    cz_ref[0] = jnp.zeros((rows, lanes), jnp.float32)

    def setup(k, carry):
        w = wet_of(k)
        w_next = jnp.where(k + 1 < levels, wet_of(k + 1), 0.0)
        w_east = roll(w, -1, 1)
        w_north = roll(w, -1, 0)
        ke = ke_ref[0, k]
        ke_sel = jnp.where(row >= ny, roll(ke, -1, 1), ke)
        east_mask = w * w_east
        ce_ref[k] = ke_sel * east_mask
        kn = ke_ref[1, k]
        kn_up = roll(kn, -1, 0)
        kn_sel = jnp.where(
            row < ny - 1, kn, jnp.where(row == ny - 1, 0.5 * (kn + kn_up), jnp.where(row == ny, kn_up, 0.0))
        )
        north_mask = w * w_north
        cn_ref[k] = kn_sel * north_mask
        cz_ref[k + 1] = vertical_rate * w * w_next
        src_ref[k] = thaw_rate * shelf * w * (1.0 - w_next)
        wet_ref[k] = w
        gem_ref[k] = east_mask[:ny, :width]
        gnm_ref[k] = jnp.where(row < ny - 1, north_mask, 0.5 * north_mask)[:ny, :width]
        for c in range(chans):
            a_ref[c, k] = w * ve_ref[c, k]
        return carry

    lax.fori_loop(0, levels, setup, 0)

    def operate(x_ref, c, k, diffs=None):
        x = x_ref[c, k]
        above = x_ref[c, jnp.minimum(k + 1, levels - 1)]
        below = x_ref[c, jnp.maximum(k - 1, 0)]
        d_east = roll(x, -1, 1) - x
        d_north = roll(x, -1, 0) - x
        if diffs is not None:
            diffs[0][c, k] = d_east[:ny, :width]
            diffs[1][c, k] = d_north[:ny, :width]
        east = ce_ref[k] * d_east
        north = cn_ref[k] * d_north
        change = (east - roll(east, 1, 1)) + (north - roll(north, 1, 0))
        change = change + (cz_ref[k + 1] * (above - x) - cz_ref[k] * (x - below))
        return x, change

    def forward_first(ck, carry):
        c = ck // levels
        k = ck % levels
        x, change = operate(ue_ref, c, k, (du0e_ref, du0n_ref))
        heat = jnp.where(c == 0, 1.0, 0.0)
        u1_ref[c, k] = wet_ref[k] * (x + change + heat * src_ref[k])
        return carry

    lax.fori_loop(0, planes, forward_first, 0, unroll=2)

    def forward_second(ck, carry):
        c = ck // levels
        k = ck % levels
        x, change = operate(u1_ref, c, k, (du1e_ref, du1n_ref))
        heat = jnp.where(c == 0, 1.0, 0.0)
        out = wet_ref[k] * (x + change + heat * src_ref[k])
        fin_ref[c, k] = out[:ny, :width]
        return carry

    lax.fori_loop(0, planes, forward_second, 0, unroll=2)

    def backward_second(ck, carry):
        c = ck // levels
        k = ck % levels
        x, change = operate(a_ref, c, k, (dv2e_ref, dv2n_ref))
        b_ref[c, k] = wet_ref[k] * (x + change)
        return carry

    lax.fori_loop(0, planes, backward_second, 0, unroll=2)

    def backward_first(ck, carry):
        c = ck // levels
        k = ck % levels
        x, change = operate(b_ref, c, k, (dv1e_ref, dv1n_ref))
        adj_ref[c, k] = (x + change)[:ny, :width]
        return carry

    lax.fori_loop(0, planes, backward_first, 0, unroll=2)

    def gradient(k, carry):
        g_east = jnp.zeros((ny, width), jnp.float32)
        g_north = jnp.zeros((ny, width), jnp.float32)
        for c in range(chans):
            g_east = g_east - du0e_ref[c, k] * dv1e_ref[c, k] - du1e_ref[c, k] * dv2e_ref[c, k]
            g_north = g_north - du0n_ref[c, k] * dv1n_ref[c, k] - du1n_ref[c, k] * dv2n_ref[c, k]
        grad_ref[0, k] = gem_ref[k] * g_east
        grad_ref[1, k] = gnm_ref[k] * g_north
        return carry

    lax.fori_loop(0, levels, gradient, 0)


def on_device(tracers, diffusivity, level_count, shelf_mask, cotangent):
    _, chans, levels, ny, width = tracers.shape
    lanes = width + 128
    rows = -(-(ny + 2) // 8) * 8
    full_kappa = lax.all_gather(diffusivity, "scen", axis=2, tiled=True)
    fields = jnp.concatenate(
        [
            tracers[0].reshape(chans * levels, ny, width),
            cotangent[0].reshape(chans * levels, ny, width),
            full_kappa.reshape(2 * levels, ny, width),
            level_count.astype(jnp.float32)[None],
            shelf_mask.astype(jnp.float32)[None],
        ]
    )
    ext = extended(fields, lanes, rows)
    field = jax.ShapeDtypeStruct((chans, levels, ny, width), jnp.float32)
    plane = pltpu.VMEM((levels, rows, lanes), jnp.float32)
    planes_c = pltpu.VMEM((chans, levels, rows, lanes), jnp.float32)
    diff = pltpu.VMEM((chans, levels, ny, width), jnp.float32)
    mask = pltpu.VMEM((levels, ny, width), jnp.float32)
    final, adjoint, grad = pl.pallas_call(
        diffusion_kernel,
        out_shape=(field, field, jax.ShapeDtypeStruct((2, levels, ny, width), jnp.float32)),
        scratch_shapes=[
            plane,
            plane,
            plane,
            pltpu.VMEM((levels + 1, rows, lanes), jnp.float32),
            plane,
            mask,
            mask,
            planes_c,
            planes_c,
            planes_c,
        ]
        + [diff] * 8,
        compiler_params=pltpu.CompilerParams(vmem_limit_bytes=48 * 1024 * 1024),
        interpret=INTERPRET,
    )(ext)
    kappa_grad = summed_over_scen(grad)
    return (final[None], adjoint[None], kappa_grad)


def summed_over_scen(grad):
    parts = lax.axis_size("scen")
    kinds, levels, ny, width = grad.shape
    if parts % 2:
        split = grad.reshape(kinds, levels, parts, ny // parts, width)
        return lax.all_to_all(split, "scen", 2, 2, tiled=True).sum(axis=2)
    me = lax.axis_index("scen")
    core = me % 2
    chip = me // 2
    chips = parts // 2
    split = grad.reshape(kinds, levels, chips, 2, ny // parts, width)
    mine = lax.dynamic_index_in_dim(split, core, axis=3, keepdims=False)
    other = lax.dynamic_index_in_dim(split, 1 - core, axis=3, keepdims=False)
    pair = lax.ppermute(other, "scen", [(q, q ^ 1) for q in range(parts)])
    chip_sum = mine + pair
    total = lax.dynamic_index_in_dim(chip_sum, chip, axis=2, keepdims=False)
    for step in range(1, chips):
        send = lax.dynamic_index_in_dim(chip_sum, (chip + step) % chips, axis=2, keepdims=False)
        total = total + lax.ppermute(
            send, "scen", [(q, ((q // 2 + step) % chips) * 2 + q % 2) for q in range(parts)]
        )
    return total


def solution(mesh):
    placed = (
        P("scen", None, None, None, "space"),
        P(None, None, "scen", "space"),
        P(None, "space"),
        P(None, "space"),
        P("scen", None, None, None, "space"),
    )
    return jax.shard_map(
        on_device,
        mesh=mesh,
        in_specs=placed,
        out_specs=(
            P("scen", None, None, None, "space"),
            P("scen", None, None, None, "space"),
            P(None, None, "scen", "space"),
        ),
        check_vma=False,
    )
```

```python
import jax
import jax.numpy as jnp
from jax import lax
from jax.experimental import pallas as pl
from jax.experimental.pallas import tpu as pltpu
from jax.sharding import PartitionSpec as P

STEPS = 2
HALO = 2

vertical_rate = 0.1
thaw_rate = 0.3

INTERPRET = False


def shifted(x, perm):
    return lax.ppermute(x, "space", perm)


def picker(size, positions):
    where = lax.broadcasted_iota(jnp.int32, (size, len(positions)), 0)
    slot = lax.broadcasted_iota(jnp.int32, (size, len(positions)), 1)
    hit = jnp.zeros((size, len(positions)), jnp.bool_)
    for p, at in enumerate(positions):
        hit = hit | ((slot == p) & (where == at))
    return hit.astype(jnp.float32)


def contract(a, b, dims):
    return lax.dot_general(
        a, b, (dims, ((), ())), precision=lax.Precision.HIGHEST, preferred_element_type=jnp.float32
    )


def extended(fields, lanes, rows):
    n = lax.axis_size("space")
    count, ny, width = fields.shape
    spare = lanes - width
    mirrored = fields[:, ny - 1:ny - 3:-1, ::-1]
    ghost = shifted(mirrored, [(q, n - 1 - q) for q in range(n)])
    pick = picker(width, [width - 2, width - 1, 0, 1])
    edges = jnp.concatenate(
        [
            contract(pick, fields.reshape(count * ny, width), ((0,), (1,))),
            contract(pick, ghost.reshape(count * 2, width), ((0,), (1,))),
        ],
        axis=1,
    )
    west = shifted(edges[0:2], [(q, (q + 1) % n) for q in range(n)])
    east = shifted(edges[2:4], [(q, (q - 1) % n) for q in range(n)])
    place = picker(spare, [0, 1, spare - 2, spare - 1]).T
    halo = jnp.concatenate([east, west])
    side = contract(halo[:, :count * ny], place, ((0,), (0,))).reshape(count, ny, spare)
    ghost_side = contract(halo[:, count * ny:], place, ((0,), (0,))).reshape(count, 2, spare)
    top = jnp.concatenate([fields, side], axis=-1)
    folded = jnp.concatenate([ghost, ghost_side], axis=-1)
    pad = jnp.zeros((count, rows - ny - 2, lanes), fields.dtype)
    return jnp.concatenate([top, folded, pad], axis=1)


def roll(x, shift, axis):
    return pltpu.roll(x, shift % x.shape[axis], axis)


class Planes:
    def __init__(self, ref, start, levels):
        self.ref = ref
        self.start = start
        self.levels = levels

    def __getitem__(self, index):
        c, k = index
        return self.ref[self.start + c * self.levels + k]


def diffusion_kernel(
    x_ref,
    fin_ref, adj_ref, grad_ref,
    wet_ref, ce_ref, cn_ref, cz_ref, src_ref, gem_ref, gnm_ref, u1_ref, a_ref, b_ref,
    du0e_ref, du0n_ref, du1e_ref, du1n_ref, dv1e_ref, dv1n_ref, dv2e_ref, dv2n_ref,
):
    levels, rows, lanes = wet_ref.shape
    chans, _, ny, width = fin_ref.shape
    row = lax.broadcasted_iota(jnp.int32, (rows, lanes), 0)
    lane = lax.broadcasted_iota(jnp.int32, (rows, lanes), 1)
    planes = chans * levels
    ue_ref = Planes(x_ref, 0, levels)
    ve_ref = Planes(x_ref, planes, levels)
    ke_ref = Planes(x_ref, 2 * planes, levels)
    lev = x_ref[2 * planes + 2 * levels]
    shelf = x_ref[2 * planes + 2 * levels + 1]

    def wet_of(k):
        return (lev > k.astype(jnp.float32)).astype(jnp.float32)

    cz_ref[0] = jnp.zeros((rows, lanes), jnp.float32)

    def setup(k, carry):
        w = wet_of(k)
        w_next = jnp.where(k + 1 < levels, wet_of(k + 1), 0.0)
        w_east = roll(w, -1, 1)
        w_north = roll(w, -1, 0)
        ke = ke_ref[0, k]
        ke_sel = jnp.where(row >= ny, roll(ke, -1, 1), ke)
        east_mask = w * w_east
        ce_ref[k] = ke_sel * east_mask
        kn = ke_ref[1, k]
        kn_up = roll(kn, -1, 0)
        kn_sel = jnp.where(
            row < ny - 1, kn, jnp.where(row == ny - 1, 0.5 * (kn + kn_up), jnp.where(row == ny, kn_up, 0.0))
        )
        north_mask = w * w_north
        cn_ref[k] = kn_sel * north_mask
        cz_ref[k + 1] = vertical_rate * w * w_next
        src_ref[k] = thaw_rate * shelf * w * (1.0 - w_next)
        wet_ref[k] = w
        gem_ref[k] = east_mask[:ny, :width]
        gnm_ref[k] = jnp.where(row < ny - 1, north_mask, 0.5 * north_mask)[:ny, :width]
        for c in range(chans):
            a_ref[c, k] = w * ve_ref[c, k]
        return carry

    lax.fori_loop(0, levels, setup, 0, unroll=2)

    def operate(x_ref, c, k, diffs=None):
        x = x_ref[c, k]
        above = x_ref[c, jnp.minimum(k + 1, levels - 1)]
        below = x_ref[c, jnp.maximum(k - 1, 0)]
        d_east = roll(x, -1, 1) - x
        d_north = roll(x, -1, 0) - x
        if diffs is not None:
            diffs[0][c, k] = d_east[:ny, :width]
            diffs[1][c, k] = d_north[:ny, :width]
        east = ce_ref[k] * d_east
        north = cn_ref[k] * d_north
        change = (east - roll(east, 1, 1)) + (north - roll(north, 1, 0))
        change = change + (cz_ref[k + 1] * (above - x) - cz_ref[k] * (x - below))
        return x, change

    def forward_first(ck, carry):
        c = ck // levels
        k = ck % levels
        x, change = operate(ue_ref, c, k, (du0e_ref, du0n_ref))
        heat = jnp.where(c == 0, 1.0, 0.0)
        u1_ref[c, k] = wet_ref[k] * (x + change + heat * src_ref[k])
        return carry

    lax.fori_loop(0, planes, forward_first, 0, unroll=4)

    def forward_second(ck, carry):
        c = ck // levels
        k = ck % levels
        x, change = operate(u1_ref, c, k, (du1e_ref, du1n_ref))
        heat = jnp.where(c == 0, 1.0, 0.0)
        out = wet_ref[k] * (x + change + heat * src_ref[k])
        fin_ref[c, k] = out[:ny, :width]
        return carry

    lax.fori_loop(0, planes, forward_second, 0, unroll=4)

    def backward_second(ck, carry):
        c = ck // levels
        k = ck % levels
        x, change = operate(a_ref, c, k, (dv2e_ref, dv2n_ref))
        b_ref[c, k] = wet_ref[k] * (x + change)
        return carry

    lax.fori_loop(0, planes, backward_second, 0, unroll=4)

    def backward_first(ck, carry):
        c = ck // levels
        k = ck % levels
        x, change = operate(b_ref, c, k, (dv1e_ref, dv1n_ref))
        adj_ref[c, k] = (x + change)[:ny, :width]
        return carry

    lax.fori_loop(0, planes, backward_first, 0, unroll=4)

    def gradient(k, carry):
        g_east = jnp.zeros((ny, width), jnp.float32)
        g_north = jnp.zeros((ny, width), jnp.float32)
        for c in range(chans):
            g_east = g_east - du0e_ref[c, k] * dv1e_ref[c, k] - du1e_ref[c, k] * dv2e_ref[c, k]
            g_north = g_north - du0n_ref[c, k] * dv1n_ref[c, k] - du1n_ref[c, k] * dv2n_ref[c, k]
        grad_ref[0, k] = gem_ref[k] * g_east
        grad_ref[1, k] = gnm_ref[k] * g_north
        return carry

    lax.fori_loop(0, levels, gradient, 0, unroll=2)


def on_device(tracers, diffusivity, level_count, shelf_mask, cotangent):
    _, chans, levels, ny, width = tracers.shape
    lanes = width + 128
    rows = -(-(ny + 2) // 8) * 8
    full_kappa = lax.all_gather(diffusivity, "scen", axis=2, tiled=True)
    fields = jnp.concatenate(
        [
            tracers[0].reshape(chans * levels, ny, width),
            cotangent[0].reshape(chans * levels, ny, width),
            full_kappa.reshape(2 * levels, ny, width),
            level_count.astype(jnp.float32)[None],
            shelf_mask.astype(jnp.float32)[None],
        ]
    )
    ext = extended(fields, lanes, rows)
    field = jax.ShapeDtypeStruct((chans, levels, ny, width), jnp.float32)
    plane = pltpu.VMEM((levels, rows, lanes), jnp.float32)
    planes_c = pltpu.VMEM((chans, levels, rows, lanes), jnp.float32)
    diff = pltpu.VMEM((chans, levels, ny, width), jnp.float32)
    mask = pltpu.VMEM((levels, ny, width), jnp.float32)
    final, adjoint, grad = pl.pallas_call(
        diffusion_kernel,
        out_shape=(field, field, jax.ShapeDtypeStruct((2, levels, ny, width), jnp.float32)),
        scratch_shapes=[
            plane,
            plane,
            plane,
            pltpu.VMEM((levels + 1, rows, lanes), jnp.float32),
            plane,
            mask,
            mask,
            planes_c,
            planes_c,
            planes_c,
        ]
        + [diff] * 8,
        compiler_params=pltpu.CompilerParams(vmem_limit_bytes=48 * 1024 * 1024),
        interpret=INTERPRET,
    )(ext)
    kappa_grad = summed_over_scen(grad)
    return (final[None], adjoint[None], kappa_grad)


def summed_over_scen(grad):
    parts = lax.axis_size("scen")
    kinds, levels, ny, width = grad.shape
    if parts % 2:
        split = grad.reshape(kinds, levels, parts, ny // parts, width)
        return lax.all_to_all(split, "scen", 2, 2, tiled=True).sum(axis=2)
    me = lax.axis_index("scen")
    core = me % 2
    chip = me // 2
    chips = parts // 2
    split = grad.reshape(kinds, levels, chips, 2, ny // parts, width)
    mine = lax.dynamic_index_in_dim(split, core, axis=3, keepdims=False)
    other = lax.dynamic_index_in_dim(split, 1 - core, axis=3, keepdims=False)
    pair = lax.ppermute(other, "scen", [(q, q ^ 1) for q in range(parts)])
    chip_sum = mine + pair
    total = lax.dynamic_index_in_dim(chip_sum, chip, axis=2, keepdims=False)
    for step in range(1, chips):
        send = lax.dynamic_index_in_dim(chip_sum, (chip + step) % chips, axis=2, keepdims=False)
        total = total + lax.ppermute(
            send, "scen", [(q, ((q // 2 + step) % chips) * 2 + q % 2) for q in range(parts)]
        )
    return total


def solution(mesh):
    placed = (
        P("scen", None, None, None, "space"),
        P(None, None, "scen", "space"),
        P(None, "space"),
        P(None, "space"),
        P("scen", None, None, None, "space"),
    )
    return jax.shard_map(
        on_device,
        mesh=mesh,
        in_specs=placed,
        out_specs=(
            P("scen", None, None, None, "space"),
            P("scen", None, None, None, "space"),
            P(None, None, "scen", "space"),
        ),
        check_vma=False,
    )
```

```python
import jax
import jax.numpy as jnp
from jax import lax
from jax.experimental import pallas as pl
from jax.experimental.pallas import tpu as pltpu
from jax.sharding import PartitionSpec as P

STEPS = 2
HALO = 2

vertical_rate = 0.1
thaw_rate = 0.3

INTERPRET = False


def shifted(x, perm):
    return lax.ppermute(x, "space", perm)


def picker(size, positions):
    where = lax.broadcasted_iota(jnp.int32, (size, len(positions)), 0)
    slot = lax.broadcasted_iota(jnp.int32, (size, len(positions)), 1)
    hit = jnp.zeros((size, len(positions)), jnp.bool_)
    for p, at in enumerate(positions):
        hit = hit | ((slot == p) & (where == at))
    return hit.astype(jnp.float32)


def contract(a, b, dims):
    return lax.dot_general(
        a, b, (dims, ((), ())), precision=lax.Precision.HIGHEST, preferred_element_type=jnp.float32
    )


def extended(fields, lanes, rows):
    n = lax.axis_size("space")
    count, ny, width = fields.shape
    spare = lanes - width
    mirrored = fields[:, ny - 1:ny - 3:-1, ::-1]
    ghost = shifted(mirrored, [(q, n - 1 - q) for q in range(n)])
    pick = picker(width, [width - 2, width - 1, 0, 1])
    edges = jnp.concatenate(
        [
            contract(pick, fields.reshape(count * ny, width), ((0,), (1,))),
            contract(pick, ghost.reshape(count * 2, width), ((0,), (1,))),
        ],
        axis=1,
    )
    west = shifted(edges[0:2], [(q, (q + 1) % n) for q in range(n)])
    east = shifted(edges[2:4], [(q, (q - 1) % n) for q in range(n)])
    place = picker(spare, [0, 1, spare - 2, spare - 1]).T
    halo = jnp.concatenate([east, west])
    side = contract(halo[:, :count * ny], place, ((0,), (0,))).reshape(count, ny, spare)
    ghost_side = contract(halo[:, count * ny:], place, ((0,), (0,))).reshape(count, 2, spare)
    top = jnp.concatenate([fields, side], axis=-1)
    folded = jnp.concatenate([ghost, ghost_side], axis=-1)
    pad = jnp.zeros((count, rows - ny - 2, lanes), fields.dtype)
    return jnp.concatenate([top, folded, pad], axis=1)


def roll(x, shift, axis):
    return pltpu.roll(x, shift % x.shape[axis], axis)


class Planes:
    def __init__(self, ref, start, levels):
        self.ref = ref
        self.start = start
        self.levels = levels

    def __getitem__(self, index):
        c, k = index
        return self.ref[self.start + c * self.levels + k]


def diffusion_kernel(
    x_ref,
    fin_ref, adj_ref, grad_ref,
    wet_ref, ce_ref, cn_ref, cz_ref, src_ref, gem_ref, gnm_ref, u1_ref, a_ref, b_ref,
    du0e_ref, du0n_ref, du1e_ref, du1n_ref, dv1e_ref, dv1n_ref, dv2e_ref, dv2n_ref,
):
    levels, rows, lanes = wet_ref.shape
    chans, _, ny, width = fin_ref.shape
    row = lax.broadcasted_iota(jnp.int32, (rows, lanes), 0)
    lane = lax.broadcasted_iota(jnp.int32, (rows, lanes), 1)
    planes = chans * levels
    ue_ref = Planes(x_ref, 0, levels)
    ve_ref = Planes(x_ref, planes, levels)
    ke_ref = Planes(x_ref, 2 * planes, levels)
    lev = x_ref[2 * planes + 2 * levels]
    shelf = x_ref[2 * planes + 2 * levels + 1]

    def wet_of(k):
        return (lev > k.astype(jnp.float32)).astype(jnp.float32)

    cz_ref[0] = jnp.zeros((rows, lanes), jnp.float32)

    def setup(k, carry):
        w = wet_of(k)
        w_next = jnp.where(k + 1 < levels, wet_of(k + 1), 0.0)
        w_east = roll(w, -1, 1)
        w_north = roll(w, -1, 0)
        ke = ke_ref[0, k]
        ke_sel = jnp.where(row >= ny, roll(ke, -1, 1), ke)
        east_mask = w * w_east
        ce_ref[k] = ke_sel * east_mask
        kn = ke_ref[1, k]
        kn_up = roll(kn, -1, 0)
        kn_sel = jnp.where(
            row < ny - 1, kn, jnp.where(row == ny - 1, 0.5 * (kn + kn_up), jnp.where(row == ny, kn_up, 0.0))
        )
        north_mask = w * w_north
        cn_ref[k] = kn_sel * north_mask
        cz_ref[k + 1] = vertical_rate * w * w_next
        src_ref[k] = thaw_rate * shelf * w * (1.0 - w_next)
        wet_ref[k] = w
        gem_ref[k] = east_mask[:ny, :width]
        gnm_ref[k] = jnp.where(row < ny - 1, north_mask, 0.5 * north_mask)[:ny, :width]
        for c in range(chans):
            a_ref[c, k] = w * ve_ref[c, k]
        return carry

    lax.fori_loop(0, levels, setup, 0, unroll=4)

    def operate(x_ref, c, k, diffs=None):
        x = x_ref[c, k]
        above = x_ref[c, jnp.minimum(k + 1, levels - 1)]
        below = x_ref[c, jnp.maximum(k - 1, 0)]
        d_east = roll(x, -1, 1) - x
        d_north = roll(x, -1, 0) - x
        if diffs is not None:
            diffs[0][c, k] = d_east[:ny, :width]
            diffs[1][c, k] = d_north[:ny, :width]
        east = ce_ref[k] * d_east
        north = cn_ref[k] * d_north
        change = (east - roll(east, 1, 1)) + (north - roll(north, 1, 0))
        change = change + (cz_ref[k + 1] * (above - x) - cz_ref[k] * (x - below))
        return x, change

    def forward_first(ck, carry):
        c = ck // levels
        k = ck % levels
        x, change = operate(ue_ref, c, k, (du0e_ref, du0n_ref))
        heat = jnp.where(c == 0, 1.0, 0.0)
        u1_ref[c, k] = wet_ref[k] * (x + change + heat * src_ref[k])
        return carry

    lax.fori_loop(0, planes, forward_first, 0, unroll=8)

    def forward_second(ck, carry):
        c = ck // levels
        k = ck % levels
        x, change = operate(u1_ref, c, k, (du1e_ref, du1n_ref))
        heat = jnp.where(c == 0, 1.0, 0.0)
        out = wet_ref[k] * (x + change + heat * src_ref[k])
        fin_ref[c, k] = out[:ny, :width]
        return carry

    lax.fori_loop(0, planes, forward_second, 0, unroll=8)

    def backward_second(ck, carry):
        c = ck // levels
        k = ck % levels
        x, change = operate(a_ref, c, k, (dv2e_ref, dv2n_ref))
        b_ref[c, k] = wet_ref[k] * (x + change)
        return carry

    lax.fori_loop(0, planes, backward_second, 0, unroll=8)

    def backward_first(ck, carry):
        c = ck // levels
        k = ck % levels
        x, change = operate(b_ref, c, k, (dv1e_ref, dv1n_ref))
        adj_ref[c, k] = (x + change)[:ny, :width]
        return carry

    lax.fori_loop(0, planes, backward_first, 0, unroll=8)

    def gradient(k, carry):
        g_east = jnp.zeros((ny, width), jnp.float32)
        g_north = jnp.zeros((ny, width), jnp.float32)
        for c in range(chans):
            g_east = g_east - du0e_ref[c, k] * dv1e_ref[c, k] - du1e_ref[c, k] * dv2e_ref[c, k]
            g_north = g_north - du0n_ref[c, k] * dv1n_ref[c, k] - du1n_ref[c, k] * dv2n_ref[c, k]
        grad_ref[0, k] = gem_ref[k] * g_east
        grad_ref[1, k] = gnm_ref[k] * g_north
        return carry

    lax.fori_loop(0, levels, gradient, 0, unroll=4)


def on_device(tracers, diffusivity, level_count, shelf_mask, cotangent):
    _, chans, levels, ny, width = tracers.shape
    lanes = width + 128
    rows = -(-(ny + 2) // 8) * 8
    full_kappa = lax.all_gather(diffusivity, "scen", axis=2, tiled=True)
    fields = jnp.concatenate(
        [
            tracers[0].reshape(chans * levels, ny, width),
            cotangent[0].reshape(chans * levels, ny, width),
            full_kappa.reshape(2 * levels, ny, width),
            level_count.astype(jnp.float32)[None],
            shelf_mask.astype(jnp.float32)[None],
        ]
    )
    ext = extended(fields, lanes, rows)
    field = jax.ShapeDtypeStruct((chans, levels, ny, width), jnp.float32)
    plane = pltpu.VMEM((levels, rows, lanes), jnp.float32)
    planes_c = pltpu.VMEM((chans, levels, rows, lanes), jnp.float32)
    diff = pltpu.VMEM((chans, levels, ny, width), jnp.float32)
    mask = pltpu.VMEM((levels, ny, width), jnp.float32)
    final, adjoint, grad = pl.pallas_call(
        diffusion_kernel,
        out_shape=(field, field, jax.ShapeDtypeStruct((2, levels, ny, width), jnp.float32)),
        scratch_shapes=[
            plane,
            plane,
            plane,
            pltpu.VMEM((levels + 1, rows, lanes), jnp.float32),
            plane,
            mask,
            mask,
            planes_c,
            planes_c,
            planes_c,
        ]
        + [diff] * 8,
        compiler_params=pltpu.CompilerParams(vmem_limit_bytes=48 * 1024 * 1024),
        interpret=INTERPRET,
    )(ext)
    kappa_grad = summed_over_scen(grad)
    return (final[None], adjoint[None], kappa_grad)


def summed_over_scen(grad):
    parts = lax.axis_size("scen")
    kinds, levels, ny, width = grad.shape
    if parts % 2:
        split = grad.reshape(kinds, levels, parts, ny // parts, width)
        return lax.all_to_all(split, "scen", 2, 2, tiled=True).sum(axis=2)
    me = lax.axis_index("scen")
    core = me % 2
    chip = me // 2
    chips = parts // 2
    split = grad.reshape(kinds, levels, chips, 2, ny // parts, width)
    mine = lax.dynamic_index_in_dim(split, core, axis=3, keepdims=False)
    other = lax.dynamic_index_in_dim(split, 1 - core, axis=3, keepdims=False)
    pair = lax.ppermute(other, "scen", [(q, q ^ 1) for q in range(parts)])
    chip_sum = mine + pair
    total = lax.dynamic_index_in_dim(chip_sum, chip, axis=2, keepdims=False)
    for step in range(1, chips):
        send = lax.dynamic_index_in_dim(chip_sum, (chip + step) % chips, axis=2, keepdims=False)
        total = total + lax.ppermute(
            send, "scen", [(q, ((q // 2 + step) % chips) * 2 + q % 2) for q in range(parts)]
        )
    return total


def solution(mesh):
    placed = (
        P("scen", None, None, None, "space"),
        P(None, None, "scen", "space"),
        P(None, "space"),
        P(None, "space"),
        P("scen", None, None, None, "space"),
    )
    return jax.shard_map(
        on_device,
        mesh=mesh,
        in_specs=placed,
        out_specs=(
            P("scen", None, None, None, "space"),
            P("scen", None, None, None, "space"),
            P(None, None, "scen", "space"),
        ),
        check_vma=False,
    )
```

```python
import jax
import jax.numpy as jnp
from jax import lax
from jax.experimental import pallas as pl
from jax.experimental.pallas import tpu as pltpu
from jax.sharding import PartitionSpec as P

STEPS = 2
HALO = 2

vertical_rate = 0.1
thaw_rate = 0.3

INTERPRET = False


def shifted(x, perm):
    return lax.ppermute(x, "space", perm)


def picker(size, positions):
    where = lax.broadcasted_iota(jnp.int32, (size, len(positions)), 0)
    slot = lax.broadcasted_iota(jnp.int32, (size, len(positions)), 1)
    hit = jnp.zeros((size, len(positions)), jnp.bool_)
    for p, at in enumerate(positions):
        hit = hit | ((slot == p) & (where == at))
    return hit.astype(jnp.float32)


def contract(a, b, dims):
    return lax.dot_general(
        a, b, (dims, ((), ())), precision=lax.Precision.HIGHEST, preferred_element_type=jnp.float32
    )


def extended(fields, lanes, rows):
    n = lax.axis_size("space")
    count, ny, width = fields.shape
    spare = lanes - width
    mirrored = fields[:, ny - 1:ny - 3:-1, ::-1]
    ghost = shifted(mirrored, [(q, n - 1 - q) for q in range(n)])
    pick = picker(width, [width - 2, width - 1, 0, 1])
    edges = jnp.concatenate(
        [
            contract(pick, fields.reshape(count * ny, width), ((0,), (1,))),
            contract(pick, ghost.reshape(count * 2, width), ((0,), (1,))),
        ],
        axis=1,
    )
    west = shifted(edges[0:2], [(q, (q + 1) % n) for q in range(n)])
    east = shifted(edges[2:4], [(q, (q - 1) % n) for q in range(n)])
    place = picker(spare, [0, 1, spare - 2, spare - 1]).T
    halo = jnp.concatenate([east, west])
    side = contract(halo[:, :count * ny], place, ((0,), (0,))).reshape(count, ny, spare)
    ghost_side = contract(halo[:, count * ny:], place, ((0,), (0,))).reshape(count, 2, spare)
    top = jnp.concatenate([fields, side], axis=-1)
    folded = jnp.concatenate([ghost, ghost_side], axis=-1)
    pad = jnp.zeros((count, rows - ny - 2, lanes), fields.dtype)
    return jnp.concatenate([top, folded, pad], axis=1)


def roll(x, shift, axis):
    return pltpu.roll(x, shift % x.shape[axis], axis)


class Planes:
    def __init__(self, ref, start, levels):
        self.ref = ref
        self.start = start
        self.levels = levels

    def __getitem__(self, index):
        c, k = index
        return self.ref[self.start + c * self.levels + k]


def diffusion_kernel(
    x_ref,
    fin_ref, adj_ref, grad_ref,
    wet_ref, ce_ref, cn_ref, cz_ref, src_ref, gem_ref, gnm_ref, u1_ref, a_ref, b_ref,
    du0e_ref, du0n_ref, du1e_ref, du1n_ref, dv1e_ref, dv1n_ref, dv2e_ref, dv2n_ref,
):
    levels, rows, lanes = wet_ref.shape
    chans, _, ny, width = fin_ref.shape
    row = lax.broadcasted_iota(jnp.int32, (rows, lanes), 0)
    lane = lax.broadcasted_iota(jnp.int32, (rows, lanes), 1)
    planes = chans * levels
    ue_ref = Planes(x_ref, 0, levels)
    ve_ref = Planes(x_ref, planes, levels)
    ke_ref = Planes(x_ref, 2 * planes, levels)
    lev = x_ref[2 * planes + 2 * levels]
    shelf = x_ref[2 * planes + 2 * levels + 1]

    def wet_of(k):
        return (lev > k.astype(jnp.float32)).astype(jnp.float32)

    cz_ref[0] = jnp.zeros((rows, lanes), jnp.float32)

    def setup(k, carry):
        w = wet_of(k)
        w_next = jnp.where(k + 1 < levels, wet_of(k + 1), 0.0)
        w_east = roll(w, -1, 1)
        w_north = roll(w, -1, 0)
        ke = ke_ref[0, k]
        ke_sel = jnp.where(row >= ny, roll(ke, -1, 1), ke)
        east_mask = w * w_east
        ce_ref[k] = ke_sel * east_mask
        kn = ke_ref[1, k]
        kn_up = roll(kn, -1, 0)
        kn_sel = jnp.where(
            row < ny - 1, kn, jnp.where(row == ny - 1, 0.5 * (kn + kn_up), jnp.where(row == ny, kn_up, 0.0))
        )
        north_mask = w * w_north
        cn_ref[k] = kn_sel * north_mask
        cz_ref[k + 1] = vertical_rate * w * w_next
        src_ref[k] = thaw_rate * shelf * w * (1.0 - w_next)
        wet_ref[k] = w
        gem_ref[k] = east_mask[:ny, :width]
        gnm_ref[k] = jnp.where(row < ny - 1, north_mask, 0.5 * north_mask)[:ny, :width]
        for c in range(chans):
            a_ref[c, k] = w * ve_ref[c, k]
        return carry

    lax.fori_loop(0, levels, setup, 0, unroll=True)

    def operate(x_ref, c, k, diffs=None):
        x = x_ref[c, k]
        above = x_ref[c, jnp.minimum(k + 1, levels - 1)]
        below = x_ref[c, jnp.maximum(k - 1, 0)]
        d_east = roll(x, -1, 1) - x
        d_north = roll(x, -1, 0) - x
        if diffs is not None:
            diffs[0][c, k] = d_east[:ny, :width]
            diffs[1][c, k] = d_north[:ny, :width]
        east = ce_ref[k] * d_east
        north = cn_ref[k] * d_north
        change = (east - roll(east, 1, 1)) + (north - roll(north, 1, 0))
        change = change + (cz_ref[k + 1] * (above - x) - cz_ref[k] * (x - below))
        return x, change

    def forward_first(ck, carry):
        c = ck // levels
        k = ck % levels
        x, change = operate(ue_ref, c, k, (du0e_ref, du0n_ref))
        heat = jnp.where(c == 0, 1.0, 0.0)
        u1_ref[c, k] = wet_ref[k] * (x + change + heat * src_ref[k])
        return carry

    lax.fori_loop(0, planes, forward_first, 0, unroll=True)

    def forward_second(ck, carry):
        c = ck // levels
        k = ck % levels
        x, change = operate(u1_ref, c, k, (du1e_ref, du1n_ref))
        heat = jnp.where(c == 0, 1.0, 0.0)
        out = wet_ref[k] * (x + change + heat * src_ref[k])
        fin_ref[c, k] = out[:ny, :width]
        return carry

    lax.fori_loop(0, planes, forward_second, 0, unroll=True)

    def backward_second(ck, carry):
        c = ck // levels
        k = ck % levels
        x, change = operate(a_ref, c, k, (dv2e_ref, dv2n_ref))
        b_ref[c, k] = wet_ref[k] * (x + change)
        return carry

    lax.fori_loop(0, planes, backward_second, 0, unroll=True)

    def backward_first(ck, carry):
        c = ck // levels
        k = ck % levels
        x, change = operate(b_ref, c, k, (dv1e_ref, dv1n_ref))
        adj_ref[c, k] = (x + change)[:ny, :width]
        return carry

    lax.fori_loop(0, planes, backward_first, 0, unroll=True)

    def gradient(k, carry):
        g_east = jnp.zeros((ny, width), jnp.float32)
        g_north = jnp.zeros((ny, width), jnp.float32)
        for c in range(chans):
            g_east = g_east - du0e_ref[c, k] * dv1e_ref[c, k] - du1e_ref[c, k] * dv2e_ref[c, k]
            g_north = g_north - du0n_ref[c, k] * dv1n_ref[c, k] - du1n_ref[c, k] * dv2n_ref[c, k]
        grad_ref[0, k] = gem_ref[k] * g_east
        grad_ref[1, k] = gnm_ref[k] * g_north
        return carry

    lax.fori_loop(0, levels, gradient, 0, unroll=True)


def on_device(tracers, diffusivity, level_count, shelf_mask, cotangent):
    _, chans, levels, ny, width = tracers.shape
    lanes = width + 128
    rows = -(-(ny + 2) // 8) * 8
    full_kappa = lax.all_gather(diffusivity, "scen", axis=2, tiled=True)
    fields = jnp.concatenate(
        [
            tracers[0].reshape(chans * levels, ny, width),
            cotangent[0].reshape(chans * levels, ny, width),
            full_kappa.reshape(2 * levels, ny, width),
            level_count.astype(jnp.float32)[None],
            shelf_mask.astype(jnp.float32)[None],
        ]
    )
    ext = extended(fields, lanes, rows)
    field = jax.ShapeDtypeStruct((chans, levels, ny, width), jnp.float32)
    plane = pltpu.VMEM((levels, rows, lanes), jnp.float32)
    planes_c = pltpu.VMEM((chans, levels, rows, lanes), jnp.float32)
    diff = pltpu.VMEM((chans, levels, ny, width), jnp.float32)
    mask = pltpu.VMEM((levels, ny, width), jnp.float32)
    final, adjoint, grad = pl.pallas_call(
        diffusion_kernel,
        out_shape=(field, field, jax.ShapeDtypeStruct((2, levels, ny, width), jnp.float32)),
        scratch_shapes=[
            plane,
            plane,
            plane,
            pltpu.VMEM((levels + 1, rows, lanes), jnp.float32),
            plane,
            mask,
            mask,
            planes_c,
            planes_c,
            planes_c,
        ]
        + [diff] * 8,
        compiler_params=pltpu.CompilerParams(vmem_limit_bytes=48 * 1024 * 1024),
        interpret=INTERPRET,
    )(ext)
    kappa_grad = summed_over_scen(grad)
    return (final[None], adjoint[None], kappa_grad)


def summed_over_scen(grad):
    parts = lax.axis_size("scen")
    kinds, levels, ny, width = grad.shape
    if parts % 2:
        split = grad.reshape(kinds, levels, parts, ny // parts, width)
        return lax.all_to_all(split, "scen", 2, 2, tiled=True).sum(axis=2)
    me = lax.axis_index("scen")
    core = me % 2
    chip = me // 2
    chips = parts // 2
    split = grad.reshape(kinds, levels, chips, 2, ny // parts, width)
    mine = lax.dynamic_index_in_dim(split, core, axis=3, keepdims=False)
    other = lax.dynamic_index_in_dim(split, 1 - core, axis=3, keepdims=False)
    pair = lax.ppermute(other, "scen", [(q, q ^ 1) for q in range(parts)])
    chip_sum = mine + pair
    total = lax.dynamic_index_in_dim(chip_sum, chip, axis=2, keepdims=False)
    for step in range(1, chips):
        send = lax.dynamic_index_in_dim(chip_sum, (chip + step) % chips, axis=2, keepdims=False)
        total = total + lax.ppermute(
            send, "scen", [(q, ((q // 2 + step) % chips) * 2 + q % 2) for q in range(parts)]
        )
    return total


def solution(mesh):
    placed = (
        P("scen", None, None, None, "space"),
        P(None, None, "scen", "space"),
        P(None, "space"),
        P(None, "space"),
        P("scen", None, None, None, "space"),
    )
    return jax.shard_map(
        on_device,
        mesh=mesh,
        in_specs=placed,
        out_specs=(
            P("scen", None, None, None, "space"),
            P("scen", None, None, None, "space"),
            P(None, None, "scen", "space"),
        ),
        check_vma=False,
    )
```

```python
import jax
import jax.numpy as jnp
from jax import lax
from jax.experimental import pallas as pl
from jax.experimental.pallas import tpu as pltpu
from jax.sharding import PartitionSpec as P

STEPS = 2
HALO = 2

vertical_rate = 0.1
thaw_rate = 0.3

INTERPRET = False


def shifted(x, perm):
    return lax.ppermute(x, "space", perm)


def picker(size, positions):
    where = lax.broadcasted_iota(jnp.int32, (size, len(positions)), 0)
    slot = lax.broadcasted_iota(jnp.int32, (size, len(positions)), 1)
    hit = jnp.zeros((size, len(positions)), jnp.bool_)
    for p, at in enumerate(positions):
        hit = hit | ((slot == p) & (where == at))
    return hit.astype(jnp.float32)


def contract(a, b, dims):
    return lax.dot_general(
        a, b, (dims, ((), ())), precision=lax.Precision.HIGHEST, preferred_element_type=jnp.float32
    )


def extended(fields, lanes, rows):
    n = lax.axis_size("space")
    count, ny, width = fields.shape
    spare = lanes - width
    mirrored = fields[:, ny - 1:ny - 3:-1, ::-1]
    ghost = shifted(mirrored, [(q, n - 1 - q) for q in range(n)])
    pick = picker(width, [width - 2, width - 1, 0, 1])
    edges = jnp.concatenate(
        [
            contract(pick, fields.reshape(count * ny, width), ((0,), (1,))),
            contract(pick, ghost.reshape(count * 2, width), ((0,), (1,))),
        ],
        axis=1,
    )
    west = shifted(edges[0:2], [(q, (q + 1) % n) for q in range(n)])
    east = shifted(edges[2:4], [(q, (q - 1) % n) for q in range(n)])
    place = picker(spare, [0, 1, spare - 2, spare - 1]).T
    halo = jnp.concatenate([east, west])
    side = contract(halo[:, :count * ny], place, ((0,), (0,))).reshape(count, ny, spare)
    ghost_side = contract(halo[:, count * ny:], place, ((0,), (0,))).reshape(count, 2, spare)
    top = jnp.concatenate([fields, side], axis=-1)
    folded = jnp.concatenate([ghost, ghost_side], axis=-1)
    pad = jnp.zeros((count, rows - ny - 2, lanes), fields.dtype)
    return jnp.concatenate([top, folded, pad], axis=1)


def roll(x, shift, axis):
    return pltpu.roll(x, shift % x.shape[axis], axis)


class Planes:
    def __init__(self, ref, start, levels):
        self.ref = ref
        self.start = start
        self.levels = levels

    def __getitem__(self, index):
        c, k = index
        return self.ref[self.start + c * self.levels + k]


def diffusion_kernel(
    x_ref,
    fin_ref, adj_ref, grad_ref,
    wet_ref, ce_ref, cn_ref, cz_ref, src_ref, gem_ref, gnm_ref, u1_ref, a_ref, b_ref,
    du0e_ref, du0n_ref, du1e_ref, du1n_ref, dv1e_ref, dv1n_ref, dv2e_ref, dv2n_ref,
):
    levels, rows, lanes = wet_ref.shape
    chans, _, ny, width = fin_ref.shape
    row = lax.broadcasted_iota(jnp.int32, (rows, lanes), 0)
    lane = lax.broadcasted_iota(jnp.int32, (rows, lanes), 1)
    planes = chans * levels
    ue_ref = Planes(x_ref, 0, levels)
    ve_ref = Planes(x_ref, planes, levels)
    ke_ref = Planes(x_ref, 2 * planes, levels)
    lev = x_ref[2 * planes + 2 * levels]
    shelf = x_ref[2 * planes + 2 * levels + 1]

    def wet_of(k):
        return (lev > k.astype(jnp.float32)).astype(jnp.float32)

    cz_ref[0] = jnp.zeros((rows, lanes), jnp.float32)

    def setup(k, carry):
        w = wet_of(k)
        w_next = jnp.where(k + 1 < levels, wet_of(k + 1), 0.0)
        w_east = roll(w, -1, 1)
        w_north = roll(w, -1, 0)
        ke = ke_ref[0, k]
        ke_sel = jnp.where(row >= ny, roll(ke, -1, 1), ke)
        east_mask = w * w_east
        ce_ref[k] = ke_sel * east_mask
        kn = ke_ref[1, k]
        kn_up = roll(kn, -1, 0)
        kn_sel = jnp.where(
            row < ny - 1, kn, jnp.where(row == ny - 1, 0.5 * (kn + kn_up), jnp.where(row == ny, kn_up, 0.0))
        )
        north_mask = w * w_north
        cn_ref[k] = kn_sel * north_mask
        cz_ref[k + 1] = vertical_rate * w * w_next
        src_ref[k] = thaw_rate * shelf * w * (1.0 - w_next)
        wet_ref[k] = w
        gem_ref[k] = east_mask[:ny, :width]
        gnm_ref[k] = jnp.where(row < ny - 1, north_mask, 0.5 * north_mask)[:ny, :width]
        for c in range(chans):
            a_ref[c, k] = w * ve_ref[c, k]
        return carry

    lax.fori_loop(0, levels, setup, 0, unroll=4)

    def operate(x_ref, c, k, diffs=None):
        x = x_ref[c, k]
        above = x_ref[c, jnp.minimum(k + 1, levels - 1)]
        below = x_ref[c, jnp.maximum(k - 1, 0)]
        d_east = roll(x, -1, 1) - x
        d_north = roll(x, -1, 0) - x
        if diffs is not None:
            diffs[0][c, k] = d_east[:ny, :width]
            diffs[1][c, k] = d_north[:ny, :width]
        east = ce_ref[k] * d_east
        north = cn_ref[k] * d_north
        change = (east - roll(east, 1, 1)) + (north - roll(north, 1, 0))
        change = change + (cz_ref[k + 1] * (above - x) - cz_ref[k] * (x - below))
        return x, change

    def forward_first(ck, carry):
        c = ck // levels
        k = ck % levels
        x, change = operate(ue_ref, c, k, (du0e_ref, du0n_ref))
        heat = jnp.where(c == 0, 1.0, 0.0)
        u1_ref[c, k] = wet_ref[k] * (x + change + heat * src_ref[k])
        return carry

    lax.fori_loop(0, planes, forward_first, 0, unroll=8)

    def forward_second(ck, carry):
        c = ck // levels
        k = ck % levels
        x, change = operate(u1_ref, c, k, (du1e_ref, du1n_ref))
        heat = jnp.where(c == 0, 1.0, 0.0)
        out = wet_ref[k] * (x + change + heat * src_ref[k])
        fin_ref[c, k] = out[:ny, :width]
        return carry

    lax.fori_loop(0, planes, forward_second, 0, unroll=8)

    def backward_second(ck, carry):
        c = ck // levels
        k = ck % levels
        x, change = operate(a_ref, c, k, (dv2e_ref, dv2n_ref))
        b_ref[c, k] = wet_ref[k] * (x + change)
        return carry

    lax.fori_loop(0, planes, backward_second, 0, unroll=8)

    def backward_first(ck, carry):
        c = ck // levels
        k = ck % levels
        x, change = operate(b_ref, c, k, (dv1e_ref, dv1n_ref))
        adj_ref[c, k] = (x + change)[:ny, :width]
        return carry

    lax.fori_loop(0, planes, backward_first, 0, unroll=8)

    def gradient(k, carry):
        g_east = jnp.zeros((ny, width), jnp.float32)
        g_north = jnp.zeros((ny, width), jnp.float32)
        for c in range(chans):
            g_east = g_east - du0e_ref[c, k] * dv1e_ref[c, k] - du1e_ref[c, k] * dv2e_ref[c, k]
            g_north = g_north - du0n_ref[c, k] * dv1n_ref[c, k] - du1n_ref[c, k] * dv2n_ref[c, k]
        grad_ref[0, k] = gem_ref[k] * g_east
        grad_ref[1, k] = gnm_ref[k] * g_north
        return carry

    lax.fori_loop(0, levels, gradient, 0, unroll=4)


def on_device(tracers, diffusivity, level_count, shelf_mask, cotangent):
    _, chans, levels, ny, width = tracers.shape
    lanes = width + 128
    rows = -(-(ny + 2) // 8) * 8
    full_kappa = gathered_over_scen(diffusivity)
    fields = jnp.concatenate(
        [
            tracers[0].reshape(chans * levels, ny, width),
            cotangent[0].reshape(chans * levels, ny, width),
            full_kappa.reshape(2 * levels, ny, width),
            level_count.astype(jnp.float32)[None],
            shelf_mask.astype(jnp.float32)[None],
        ]
    )
    ext = extended(fields, lanes, rows)
    field = jax.ShapeDtypeStruct((chans, levels, ny, width), jnp.float32)
    plane = pltpu.VMEM((levels, rows, lanes), jnp.float32)
    planes_c = pltpu.VMEM((chans, levels, rows, lanes), jnp.float32)
    diff = pltpu.VMEM((chans, levels, ny, width), jnp.float32)
    mask = pltpu.VMEM((levels, ny, width), jnp.float32)
    final, adjoint, grad = pl.pallas_call(
        diffusion_kernel,
        out_shape=(field, field, jax.ShapeDtypeStruct((2, levels, ny, width), jnp.float32)),
        scratch_shapes=[
            plane,
            plane,
            plane,
            pltpu.VMEM((levels + 1, rows, lanes), jnp.float32),
            plane,
            mask,
            mask,
            planes_c,
            planes_c,
            planes_c,
        ]
        + [diff] * 8,
        compiler_params=pltpu.CompilerParams(vmem_limit_bytes=48 * 1024 * 1024),
        interpret=INTERPRET,
    )(ext)
    kappa_grad = summed_over_scen(grad)
    return (final[None], adjoint[None], kappa_grad)


def gathered_over_scen(block):
    parts = lax.axis_size("scen")
    if parts % 2:
        return lax.all_gather(block, "scen", axis=2, tiled=True)
    kinds, levels, rows, width = block.shape
    me = lax.axis_index("scen")
    core = me % 2
    chip = me // 2
    chips = parts // 2
    got = [block]
    for step in range(1, chips):
        got.append(
            lax.ppermute(block, "scen", [(q, ((q // 2 + step) % chips) * 2 + q % 2) for q in range(parts)])
        )
    same = jnp.stack(got)
    other = lax.ppermute(same, "scen", [(q, q ^ 1) for q in range(parts)])
    by_core = jnp.where(core == 0, jnp.stack([same, other], axis=1), jnp.stack([other, same], axis=1))
    order = (chip - jnp.arange(chips)) % chips
    by_chip = jnp.take(by_core, order, axis=0)
    return by_chip.transpose(2, 3, 0, 1, 4, 5).reshape(kinds, levels, parts * rows, width)


def summed_over_scen(grad):
    parts = lax.axis_size("scen")
    kinds, levels, ny, width = grad.shape
    if parts % 2:
        split = grad.reshape(kinds, levels, parts, ny // parts, width)
        return lax.all_to_all(split, "scen", 2, 2, tiled=True).sum(axis=2)
    me = lax.axis_index("scen")
    core = me % 2
    chip = me // 2
    chips = parts // 2
    split = grad.reshape(kinds, levels, chips, 2, ny // parts, width)
    mine = lax.dynamic_index_in_dim(split, core, axis=3, keepdims=False)
    other = lax.dynamic_index_in_dim(split, 1 - core, axis=3, keepdims=False)
    pair = lax.ppermute(other, "scen", [(q, q ^ 1) for q in range(parts)])
    chip_sum = mine + pair
    total = lax.dynamic_index_in_dim(chip_sum, chip, axis=2, keepdims=False)
    for step in range(1, chips):
        send = lax.dynamic_index_in_dim(chip_sum, (chip + step) % chips, axis=2, keepdims=False)
        total = total + lax.ppermute(
            send, "scen", [(q, ((q // 2 + step) % chips) * 2 + q % 2) for q in range(parts)]
        )
    return total


def solution(mesh):
    placed = (
        P("scen", None, None, None, "space"),
        P(None, None, "scen", "space"),
        P(None, "space"),
        P(None, "space"),
        P("scen", None, None, None, "space"),
    )
    return jax.shard_map(
        on_device,
        mesh=mesh,
        in_specs=placed,
        out_specs=(
            P("scen", None, None, None, "space"),
            P("scen", None, None, None, "space"),
            P(None, None, "scen", "space"),
        ),
        check_vma=False,
    )
```

```python
import jax
import jax.numpy as jnp
from jax import lax
from jax.experimental import pallas as pl
from jax.experimental.pallas import tpu as pltpu
from jax.sharding import PartitionSpec as P

STEPS = 2
HALO = 2

vertical_rate = 0.1
thaw_rate = 0.3

INTERPRET = False


def shifted(x, perm):
    return lax.ppermute(x, "space", perm)


def picker(size, positions):
    where = lax.broadcasted_iota(jnp.int32, (size, len(positions)), 0)
    slot = lax.broadcasted_iota(jnp.int32, (size, len(positions)), 1)
    hit = jnp.zeros((size, len(positions)), jnp.bool_)
    for p, at in enumerate(positions):
        hit = hit | ((slot == p) & (where == at))
    return hit.astype(jnp.float32)


def contract(a, b, dims):
    return lax.dot_general(
        a, b, (dims, ((), ())), precision=lax.Precision.HIGHEST, preferred_element_type=jnp.float32
    )


def extended(fields, lanes, rows):
    n = lax.axis_size("space")
    count, ny, width = fields.shape
    spare = lanes - width
    flat = fields.reshape(count * ny, width)
    edges = contract(picker(width, [width - 2, width - 1, 0, 1]), flat, ((0,), (1,)))
    west = shifted(edges[0:2], [(q, (q + 1) % n) for q in range(n)])
    east = shifted(edges[2:4], [(q, (q - 1) % n) for q in range(n)])
    mirrored = fields[:, ny - 1:ny - 3:-1, ::-1]
    ghost = shifted(mirrored, [(q, n - 1 - q) for q in range(n)])
    top_edges = edges.reshape(4, count, ny)[:, :, ny - 1:ny - 3:-1]
    ghost_east = shifted(top_edges[1::-1], [(q, (n - 2 - q) % n) for q in range(n)])
    ghost_west = shifted(top_edges[3:1:-1], [(q, (n - q) % n) for q in range(n)])
    place = picker(spare, [0, 1, spare - 2, spare - 1]).T
    side = contract(jnp.concatenate([east, west]), place, ((0,), (0,))).reshape(count, ny, spare)
    ghost_halo = jnp.concatenate([ghost_east, ghost_west]).reshape(4, count * 2)
    ghost_side = contract(ghost_halo, place, ((0,), (0,))).reshape(count, 2, spare)
    top = jnp.concatenate([fields, side], axis=-1)
    folded = jnp.concatenate([ghost, ghost_side], axis=-1)
    pad = jnp.zeros((count, rows - ny - 2, lanes), fields.dtype)
    return jnp.concatenate([top, folded, pad], axis=1)


def roll(x, shift, axis):
    return pltpu.roll(x, shift % x.shape[axis], axis)


class Planes:
    def __init__(self, ref, start, levels):
        self.ref = ref
        self.start = start
        self.levels = levels

    def __getitem__(self, index):
        c, k = index
        return self.ref[self.start + c * self.levels + k]


def diffusion_kernel(
    x_ref,
    fin_ref, adj_ref, grad_ref,
    wet_ref, ce_ref, cn_ref, cz_ref, src_ref, gem_ref, gnm_ref, u1_ref, a_ref, b_ref,
    du0e_ref, du0n_ref, du1e_ref, du1n_ref, dv1e_ref, dv1n_ref, dv2e_ref, dv2n_ref,
):
    levels, rows, lanes = wet_ref.shape
    chans, _, ny, width = fin_ref.shape
    row = lax.broadcasted_iota(jnp.int32, (rows, lanes), 0)
    lane = lax.broadcasted_iota(jnp.int32, (rows, lanes), 1)
    planes = chans * levels
    ue_ref = Planes(x_ref, 0, levels)
    ve_ref = Planes(x_ref, planes, levels)
    ke_ref = Planes(x_ref, 2 * planes, levels)
    lev = x_ref[2 * planes + 2 * levels]
    shelf = x_ref[2 * planes + 2 * levels + 1]

    def wet_of(k):
        return (lev > k.astype(jnp.float32)).astype(jnp.float32)

    cz_ref[0] = jnp.zeros((rows, lanes), jnp.float32)

    def setup(k, carry):
        w = wet_of(k)
        w_next = jnp.where(k + 1 < levels, wet_of(k + 1), 0.0)
        w_east = roll(w, -1, 1)
        w_north = roll(w, -1, 0)
        ke = ke_ref[0, k]
        ke_sel = jnp.where(row >= ny, roll(ke, -1, 1), ke)
        east_mask = w * w_east
        ce_ref[k] = ke_sel * east_mask
        kn = ke_ref[1, k]
        kn_up = roll(kn, -1, 0)
        kn_sel = jnp.where(
            row < ny - 1, kn, jnp.where(row == ny - 1, 0.5 * (kn + kn_up), jnp.where(row == ny, kn_up, 0.0))
        )
        north_mask = w * w_north
        cn_ref[k] = kn_sel * north_mask
        cz_ref[k + 1] = vertical_rate * w * w_next
        src_ref[k] = thaw_rate * shelf * w * (1.0 - w_next)
        wet_ref[k] = w
        gem_ref[k] = east_mask[:ny, :width]
        gnm_ref[k] = jnp.where(row < ny - 1, north_mask, 0.5 * north_mask)[:ny, :width]
        for c in range(chans):
            a_ref[c, k] = w * ve_ref[c, k]
        return carry

    lax.fori_loop(0, levels, setup, 0, unroll=4)

    def operate(x_ref, c, k, diffs=None):
        x = x_ref[c, k]
        above = x_ref[c, jnp.minimum(k + 1, levels - 1)]
        below = x_ref[c, jnp.maximum(k - 1, 0)]
        d_east = roll(x, -1, 1) - x
        d_north = roll(x, -1, 0) - x
        if diffs is not None:
            diffs[0][c, k] = d_east[:ny, :width]
            diffs[1][c, k] = d_north[:ny, :width]
        east = ce_ref[k] * d_east
        north = cn_ref[k] * d_north
        change = (east - roll(east, 1, 1)) + (north - roll(north, 1, 0))
        change = change + (cz_ref[k + 1] * (above - x) - cz_ref[k] * (x - below))
        return x, change

    def forward_first(ck, carry):
        c = ck // levels
        k = ck % levels
        x, change = operate(ue_ref, c, k, (du0e_ref, du0n_ref))
        heat = jnp.where(c == 0, 1.0, 0.0)
        u1_ref[c, k] = wet_ref[k] * (x + change + heat * src_ref[k])
        return carry

    lax.fori_loop(0, planes, forward_first, 0, unroll=8)

    def forward_second(ck, carry):
        c = ck // levels
        k = ck % levels
        x, change = operate(u1_ref, c, k, (du1e_ref, du1n_ref))
        heat = jnp.where(c == 0, 1.0, 0.0)
        out = wet_ref[k] * (x + change + heat * src_ref[k])
        fin_ref[c, k] = out[:ny, :width]
        return carry

    lax.fori_loop(0, planes, forward_second, 0, unroll=8)

    def backward_second(ck, carry):
        c = ck // levels
        k = ck % levels
        x, change = operate(a_ref, c, k, (dv2e_ref, dv2n_ref))
        b_ref[c, k] = wet_ref[k] * (x + change)
        return carry

    lax.fori_loop(0, planes, backward_second, 0, unroll=8)

    def backward_first(ck, carry):
        c = ck // levels
        k = ck % levels
        x, change = operate(b_ref, c, k, (dv1e_ref, dv1n_ref))
        adj_ref[c, k] = (x + change)[:ny, :width]
        return carry

    lax.fori_loop(0, planes, backward_first, 0, unroll=8)

    def gradient(k, carry):
        g_east = jnp.zeros((ny, width), jnp.float32)
        g_north = jnp.zeros((ny, width), jnp.float32)
        for c in range(chans):
            g_east = g_east - du0e_ref[c, k] * dv1e_ref[c, k] - du1e_ref[c, k] * dv2e_ref[c, k]
            g_north = g_north - du0n_ref[c, k] * dv1n_ref[c, k] - du1n_ref[c, k] * dv2n_ref[c, k]
        grad_ref[0, k] = gem_ref[k] * g_east
        grad_ref[1, k] = gnm_ref[k] * g_north
        return carry

    lax.fori_loop(0, levels, gradient, 0, unroll=4)


def on_device(tracers, diffusivity, level_count, shelf_mask, cotangent):
    _, chans, levels, ny, width = tracers.shape
    lanes = width + 128
    rows = -(-(ny + 2) // 8) * 8
    full_kappa = gathered_over_scen(diffusivity)
    fields = jnp.concatenate(
        [
            tracers[0].reshape(chans * levels, ny, width),
            cotangent[0].reshape(chans * levels, ny, width),
            full_kappa.reshape(2 * levels, ny, width),
            level_count.astype(jnp.float32)[None],
            shelf_mask.astype(jnp.float32)[None],
        ]
    )
    ext = extended(fields, lanes, rows)
    field = jax.ShapeDtypeStruct((chans, levels, ny, width), jnp.float32)
    plane = pltpu.VMEM((levels, rows, lanes), jnp.float32)
    planes_c = pltpu.VMEM((chans, levels, rows, lanes), jnp.float32)
    diff = pltpu.VMEM((chans, levels, ny, width), jnp.float32)
    mask = pltpu.VMEM((levels, ny, width), jnp.float32)
    final, adjoint, grad = pl.pallas_call(
        diffusion_kernel,
        out_shape=(field, field, jax.ShapeDtypeStruct((2, levels, ny, width), jnp.float32)),
        scratch_shapes=[
            plane,
            plane,
            plane,
            pltpu.VMEM((levels + 1, rows, lanes), jnp.float32),
            plane,
            mask,
            mask,
            planes_c,
            planes_c,
            planes_c,
        ]
        + [diff] * 8,
        compiler_params=pltpu.CompilerParams(vmem_limit_bytes=48 * 1024 * 1024),
        interpret=INTERPRET,
    )(ext)
    kappa_grad = summed_over_scen(grad)
    return (final[None], adjoint[None], kappa_grad)


def gathered_over_scen(block):
    parts = lax.axis_size("scen")
    if parts % 2:
        return lax.all_gather(block, "scen", axis=2, tiled=True)
    kinds, levels, rows, width = block.shape
    me = lax.axis_index("scen")
    core = me % 2
    chip = me // 2
    chips = parts // 2
    got = [block]
    for step in range(1, chips):
        got.append(
            lax.ppermute(block, "scen", [(q, ((q // 2 + step) % chips) * 2 + q % 2) for q in range(parts)])
        )
    same = jnp.stack(got)
    other = lax.ppermute(same, "scen", [(q, q ^ 1) for q in range(parts)])
    by_core = jnp.where(core == 0, jnp.stack([same, other], axis=1), jnp.stack([other, same], axis=1))
    order = (chip - jnp.arange(chips)) % chips
    by_chip = jnp.take(by_core, order, axis=0)
    return by_chip.transpose(2, 3, 0, 1, 4, 5).reshape(kinds, levels, parts * rows, width)


def summed_over_scen(grad):
    parts = lax.axis_size("scen")
    kinds, levels, ny, width = grad.shape
    if parts % 2:
        split = grad.reshape(kinds, levels, parts, ny // parts, width)
        return lax.all_to_all(split, "scen", 2, 2, tiled=True).sum(axis=2)
    me = lax.axis_index("scen")
    core = me % 2
    chip = me // 2
    chips = parts // 2
    split = grad.reshape(kinds, levels, chips, 2, ny // parts, width)
    mine = lax.dynamic_index_in_dim(split, core, axis=3, keepdims=False)
    other = lax.dynamic_index_in_dim(split, 1 - core, axis=3, keepdims=False)
    pair = lax.ppermute(other, "scen", [(q, q ^ 1) for q in range(parts)])
    chip_sum = mine + pair
    total = lax.dynamic_index_in_dim(chip_sum, chip, axis=2, keepdims=False)
    for step in range(1, chips):
        send = lax.dynamic_index_in_dim(chip_sum, (chip + step) % chips, axis=2, keepdims=False)
        total = total + lax.ppermute(
            send, "scen", [(q, ((q // 2 + step) % chips) * 2 + q % 2) for q in range(parts)]
        )
    return total


def solution(mesh):
    placed = (
        P("scen", None, None, None, "space"),
        P(None, None, "scen", "space"),
        P(None, "space"),
        P(None, "space"),
        P("scen", None, None, None, "space"),
    )
    return jax.shard_map(
        on_device,
        mesh=mesh,
        in_specs=placed,
        out_specs=(
            P("scen", None, None, None, "space"),
            P("scen", None, None, None, "space"),
            P(None, None, "scen", "space"),
        ),
        check_vma=False,
    )
```

```python
import jax
import jax.numpy as jnp
from jax import lax
from jax.experimental import pallas as pl
from jax.experimental.pallas import tpu as pltpu
from jax.sharding import PartitionSpec as P

STEPS = 2
HALO = 2

vertical_rate = 0.1
thaw_rate = 0.3

INTERPRET = False


def shifted(x, perm):
    return lax.ppermute(x, "space", perm)


def picker(size, positions):
    where = lax.broadcasted_iota(jnp.int32, (size, len(positions)), 0)
    slot = lax.broadcasted_iota(jnp.int32, (size, len(positions)), 1)
    hit = jnp.zeros((size, len(positions)), jnp.bool_)
    for p, at in enumerate(positions):
        hit = hit | ((slot == p) & (where == at))
    return hit.astype(jnp.float32)


def contract(a, b, dims):
    return lax.dot_general(
        a, b, (dims, ((), ())), precision=lax.Precision.HIGHEST, preferred_element_type=jnp.float32
    )


def extended(fields, lanes, rows):
    n = lax.axis_size("space")
    count, ny, width = fields.shape
    spare = lanes - width
    flat = fields.reshape(count * ny, width)
    edges = contract(picker(width, [width - 2, width - 1, 0, 1]), flat, ((0,), (1,)))
    west = shifted(edges[0:2], [(q, (q + 1) % n) for q in range(n)])
    east = shifted(edges[2:4], [(q, (q - 1) % n) for q in range(n)])
    mirrored = fields[:, ny - 1:ny - 3:-1, ::-1]
    ghost = shifted(mirrored, [(q, n - 1 - q) for q in range(n)])
    top_edges = edges.reshape(4, count, ny)[:, :, ny - 1:ny - 3:-1]
    ghost_east = shifted(top_edges[1::-1], [(q, (n - 2 - q) % n) for q in range(n)])
    ghost_west = shifted(top_edges[3:1:-1], [(q, (n - q) % n) for q in range(n)])
    place = picker(spare, [0, 1, spare - 2, spare - 1]).T
    side = contract(jnp.concatenate([east, west]), place, ((0,), (0,))).reshape(count, ny, spare)
    ghost_halo = jnp.concatenate([ghost_east, ghost_west]).reshape(4, count * 2)
    ghost_side = contract(ghost_halo, place, ((0,), (0,))).reshape(count, 2, spare)
    top = jnp.concatenate([fields, side], axis=-1)
    folded = jnp.concatenate([ghost, ghost_side], axis=-1)
    pad = jnp.zeros((count, rows - ny - 2, lanes), fields.dtype)
    return jnp.concatenate([top, folded, pad], axis=1)


def roll(x, shift, axis):
    return pltpu.roll(x, shift % x.shape[axis], axis)


class Planes:
    def __init__(self, ref, start, levels):
        self.ref = ref
        self.start = start
        self.levels = levels

    def __getitem__(self, index):
        c, k = index
        return self.ref[self.start + c * self.levels + k]


def diffusion_kernel(
    x_ref,
    fin_ref, adj_ref, grad_ref,
    wet_ref, ce_ref, cn_ref, cz_ref, src_ref, gem_ref, gnm_ref, u1_ref, a_ref, b_ref,
    du0e_ref, du0n_ref, du1e_ref, du1n_ref, dv1e_ref, dv1n_ref, dv2e_ref, dv2n_ref,
):
    levels, rows, lanes = wet_ref.shape
    chans, _, ny, width = fin_ref.shape
    row = lax.broadcasted_iota(jnp.int32, (rows, lanes), 0)
    lane = lax.broadcasted_iota(jnp.int32, (rows, lanes), 1)
    planes = chans * levels
    ue_ref = Planes(x_ref, 0, levels)
    ve_ref = Planes(x_ref, planes, levels)
    ke_ref = Planes(x_ref, 2 * planes, levels)
    lev = x_ref[2 * planes + 2 * levels]
    shelf = x_ref[2 * planes + 2 * levels + 1]

    def wet_of(k):
        return (lev > k.astype(jnp.float32)).astype(jnp.float32)

    cz_ref[0] = jnp.zeros((rows, lanes), jnp.float32)

    def setup(k, carry):
        w = wet_of(k)
        w_next = jnp.where(k + 1 < levels, wet_of(k + 1), 0.0)
        w_east = roll(w, -1, 1)
        w_north = roll(w, -1, 0)
        ke = ke_ref[0, k]
        ke_sel = jnp.where(row >= ny, roll(ke, -1, 1), ke)
        east_mask = w * w_east
        ce_ref[k] = ke_sel * east_mask
        kn = ke_ref[1, k]
        kn_up = roll(kn, -1, 0)
        kn_sel = jnp.where(
            row < ny - 1, kn, jnp.where(row == ny - 1, 0.5 * (kn + kn_up), jnp.where(row == ny, kn_up, 0.0))
        )
        north_mask = w * w_north
        cn_ref[k] = kn_sel * north_mask
        cz_ref[k + 1] = vertical_rate * w * w_next
        src_ref[k] = thaw_rate * shelf * w * (1.0 - w_next)
        wet_ref[k] = w
        gem_ref[k] = east_mask[:ny, :width]
        gnm_ref[k] = jnp.where(row < ny - 1, north_mask, 0.5 * north_mask)[:ny, :width]
        for c in range(chans):
            a_ref[c, k] = w * ve_ref[c, k]
        return carry

    lax.fori_loop(0, levels, setup, 0, unroll=4)

    def operate(x_ref, c, k, diffs=None):
        x = x_ref[c, k]
        above = x_ref[c, jnp.minimum(k + 1, levels - 1)]
        below = x_ref[c, jnp.maximum(k - 1, 0)]
        d_east = roll(x, -1, 1) - x
        d_north = roll(x, -1, 0) - x
        if diffs is not None:
            diffs[0][c, k] = d_east[:ny, :width]
            diffs[1][c, k] = d_north[:ny, :width]
        east = ce_ref[k] * d_east
        north = cn_ref[k] * d_north
        change = (east - roll(east, 1, 1)) + (north - roll(north, 1, 0))
        change = change + (cz_ref[k + 1] * (above - x) - cz_ref[k] * (x - below))
        return x, change

    def forward_first(ck, carry):
        c = ck // levels
        k = ck % levels
        x, change = operate(ue_ref, c, k, (du0e_ref, du0n_ref))
        heat = jnp.where(c == 0, 1.0, 0.0)
        u1_ref[c, k] = wet_ref[k] * (x + change + heat * src_ref[k])
        return carry

    lax.fori_loop(0, planes, forward_first, 0, unroll=8)

    def forward_second(ck, carry):
        c = ck // levels
        k = ck % levels
        x, change = operate(u1_ref, c, k, (du1e_ref, du1n_ref))
        heat = jnp.where(c == 0, 1.0, 0.0)
        out = wet_ref[k] * (x + change + heat * src_ref[k])
        fin_ref[c, k] = out[:ny, :width]
        return carry

    lax.fori_loop(0, planes, forward_second, 0, unroll=8)

    def backward_second(ck, carry):
        c = ck // levels
        k = ck % levels
        x, change = operate(a_ref, c, k, (dv2e_ref, dv2n_ref))
        b_ref[c, k] = wet_ref[k] * (x + change)
        return carry

    lax.fori_loop(0, planes, backward_second, 0, unroll=8)

    def backward_first(ck, carry):
        c = ck // levels
        k = ck % levels
        x, change = operate(b_ref, c, k, (dv1e_ref, dv1n_ref))
        adj_ref[c, k] = (x + change)[:ny, :width]
        return carry

    lax.fori_loop(0, planes, backward_first, 0, unroll=8)

    def gradient(k, carry):
        g_east = jnp.zeros((ny, width), jnp.float32)
        g_north = jnp.zeros((ny, width), jnp.float32)
        for c in range(chans):
            g_east = g_east - du0e_ref[c, k] * dv1e_ref[c, k] - du1e_ref[c, k] * dv2e_ref[c, k]
            g_north = g_north - du0n_ref[c, k] * dv1n_ref[c, k] - du1n_ref[c, k] * dv2n_ref[c, k]
        grad_ref[0, k] = gem_ref[k] * g_east
        grad_ref[1, k] = gnm_ref[k] * g_north
        return carry

    lax.fori_loop(0, levels, gradient, 0, unroll=4)


def on_device(tracers, diffusivity, level_count, shelf_mask, cotangent):
    _, chans, levels, ny, width = tracers.shape
    lanes = width + 128
    rows = -(-(ny + 2) // 8) * 8
    full_kappa = gathered_over_scen(diffusivity)
    fields = jnp.concatenate(
        [
            tracers[0].reshape(chans * levels, ny, width),
            cotangent[0].reshape(chans * levels, ny, width),
            full_kappa.reshape(2 * levels, ny, width),
            level_count.astype(jnp.float32)[None],
            shelf_mask.astype(jnp.float32)[None],
        ]
    )
    ext = extended(fields, lanes, rows)
    field = jax.ShapeDtypeStruct((chans, levels, ny, width), jnp.float32)
    plane = pltpu.VMEM((levels, rows, lanes), jnp.float32)
    planes_c = pltpu.VMEM((chans, levels, rows, lanes), jnp.float32)
    diff = pltpu.VMEM((chans, levels, ny, width), jnp.float32)
    mask = pltpu.VMEM((levels, ny, width), jnp.float32)
    final, adjoint, grad = pl.pallas_call(
        diffusion_kernel,
        out_shape=(field, field, jax.ShapeDtypeStruct((2, levels, ny, width), jnp.float32)),
        scratch_shapes=[
            plane,
            plane,
            plane,
            pltpu.VMEM((levels + 1, rows, lanes), jnp.float32),
            plane,
            mask,
            mask,
            planes_c,
            planes_c,
            planes_c,
        ]
        + [diff] * 8,
        compiler_params=pltpu.CompilerParams(vmem_limit_bytes=48 * 1024 * 1024),
        interpret=INTERPRET,
    )(ext)
    kappa_grad = summed_over_scen(grad)
    return (final[None], adjoint[None], kappa_grad)


def gathered_over_scen(block):
    parts = lax.axis_size("scen")
    if parts % 2:
        return lax.all_gather(block, "scen", axis=2, tiled=True)
    kinds, levels, rows, width = block.shape
    me = lax.axis_index("scen")
    core = me % 2
    chip = me // 2
    chips = parts // 2
    got = [block]
    for step in range(1, chips):
        got.append(
            lax.ppermute(block, "scen", [(q, ((q // 2 + step) % chips) * 2 + q % 2) for q in range(parts)])
        )
    same = jnp.stack(got)
    other = lax.ppermute(same, "scen", [(q, q ^ 1) for q in range(parts)])
    by_core = jnp.where(core == 0, jnp.stack([same, other], axis=1), jnp.stack([other, same], axis=1))
    order = (chip - jnp.arange(chips)) % chips
    by_chip = jnp.take(by_core, order, axis=0)
    return by_chip.transpose(2, 3, 0, 1, 4, 5).reshape(kinds, levels, parts * rows, width)


def summed_over_scen(grad):
    parts = lax.axis_size("scen")
    kinds, levels, ny, width = grad.shape
    if parts % 2:
        split = grad.reshape(kinds, levels, parts, ny // parts, width)
        return lax.all_to_all(split, "scen", 2, 2, tiled=True).sum(axis=2)
    me = lax.axis_index("scen")
    core = me % 2
    chip = me // 2
    chips = parts // 2
    split = grad.reshape(kinds, levels, chips, 2, ny // parts, width)
    mine = lax.dynamic_index_in_dim(split, core, axis=3, keepdims=False)
    other = lax.dynamic_index_in_dim(split, 1 - core, axis=3, keepdims=False)
    pair = lax.ppermute(other, "scen", [(q, q ^ 1) for q in range(parts)])
    chip_sum = mine + pair
    if chips & (chips - 1):
        total = lax.dynamic_index_in_dim(chip_sum, chip, axis=2, keepdims=False)
        for step in range(1, chips):
            send = lax.dynamic_index_in_dim(chip_sum, (chip + step) % chips, axis=2, keepdims=False)
            total = total + lax.ppermute(
                send, "scen", [(q, ((q // 2 + step) % chips) * 2 + q % 2) for q in range(parts)]
            )
        return total
    part = chip_sum
    bit = chips // 2
    while bit:
        low, high = part[:, :, :bit], part[:, :, bit:]
        upper = (chip & bit) != 0
        keep = jnp.where(upper, high, low)
        send = jnp.where(upper, low, high)
        part = keep + lax.ppermute(
            send, "scen", [(q, ((q // 2) ^ bit) * 2 + q % 2) for q in range(parts)]
        )
        bit //= 2
    return part[:, :, 0]


def solution(mesh):
    placed = (
        P("scen", None, None, None, "space"),
        P(None, None, "scen", "space"),
        P(None, "space"),
        P(None, "space"),
        P("scen", None, None, None, "space"),
    )
    return jax.shard_map(
        on_device,
        mesh=mesh,
        in_specs=placed,
        out_specs=(
            P("scen", None, None, None, "space"),
            P("scen", None, None, None, "space"),
            P(None, None, "scen", "space"),
        ),
        check_vma=False,
    )
```

```python
import jax
import jax.numpy as jnp
from jax import lax
from jax.experimental import pallas as pl
from jax.experimental.pallas import tpu as pltpu
from jax.sharding import PartitionSpec as P

STEPS = 2
HALO = 2

vertical_rate = 0.1
thaw_rate = 0.3

INTERPRET = False


def shifted(x, perm):
    return lax.ppermute(x, "space", perm)


def picker(size, positions):
    where = lax.broadcasted_iota(jnp.int32, (size, len(positions)), 0)
    slot = lax.broadcasted_iota(jnp.int32, (size, len(positions)), 1)
    hit = jnp.zeros((size, len(positions)), jnp.bool_)
    for p, at in enumerate(positions):
        hit = hit | ((slot == p) & (where == at))
    return hit.astype(jnp.float32)


def contract(a, b, dims):
    return lax.dot_general(
        a, b, (dims, ((), ())), precision=lax.Precision.HIGHEST, preferred_element_type=jnp.float32
    )


def extended(fields, lanes, rows):
    n = lax.axis_size("space")
    count, ny, width = fields.shape
    spare = lanes - width
    flat = fields.reshape(count * ny, width)
    edges = contract(picker(width, [width - 2, width - 1, 0, 1]), flat, ((0,), (1,)))
    west = shifted(edges[0:2], [(q, (q + 1) % n) for q in range(n)])
    east = shifted(edges[2:4], [(q, (q - 1) % n) for q in range(n)])
    mirrored = fields[:, ny - 1:ny - 3:-1, ::-1]
    ghost = shifted(mirrored, [(q, n - 1 - q) for q in range(n)])
    top_edges = edges.reshape(4, count, ny)[:, :, ny - 1:ny - 3:-1]
    ghost_east = shifted(top_edges[1::-1], [(q, (n - 2 - q) % n) for q in range(n)])
    ghost_west = shifted(top_edges[3:1:-1], [(q, (n - q) % n) for q in range(n)])
    place = picker(spare, [0, 1, spare - 2, spare - 1]).T
    side = contract(jnp.concatenate([east, west]), place, ((0,), (0,))).reshape(count, ny, spare)
    ghost_halo = jnp.concatenate([ghost_east, ghost_west]).reshape(4, count * 2)
    ghost_side = contract(ghost_halo, place, ((0,), (0,))).reshape(count, 2, spare)
    top = jnp.concatenate([fields, side], axis=-1)
    folded = jnp.concatenate([ghost, ghost_side], axis=-1)
    pad = jnp.zeros((count, rows - ny - 2, lanes), fields.dtype)
    return jnp.concatenate([top, folded, pad], axis=1)


def roll(x, shift, axis):
    return pltpu.roll(x, shift % x.shape[axis], axis)


class Planes:
    def __init__(self, ref, start, levels):
        self.ref = ref
        self.start = start
        self.levels = levels

    def __getitem__(self, index):
        c, k = index
        return self.ref[self.start + c * self.levels + k]


def diffusion_kernel(
    x_ref,
    fin_ref, adj_ref, grad_ref,
    wet_ref, ce_ref, cn_ref, cz_ref, src_ref, gem_ref, gnm_ref, u1_ref, a_ref, b_ref,
    du0e_ref, du0n_ref, du1e_ref, du1n_ref, dv1e_ref, dv1n_ref, dv2e_ref, dv2n_ref,
):
    levels, rows, lanes = wet_ref.shape
    chans, _, ny, width = fin_ref.shape
    row = lax.broadcasted_iota(jnp.int32, (rows, lanes), 0)
    lane = lax.broadcasted_iota(jnp.int32, (rows, lanes), 1)
    planes = chans * levels
    ue_ref = Planes(x_ref, 0, levels)
    ve_ref = Planes(x_ref, planes, levels)
    ke_ref = Planes(x_ref, 2 * planes, levels)
    lev = x_ref[2 * planes + 2 * levels]
    shelf = x_ref[2 * planes + 2 * levels + 1]

    def wet_of(k):
        return (lev > k.astype(jnp.float32)).astype(jnp.float32)

    cz_ref[0] = jnp.zeros((rows, lanes), jnp.float32)

    def setup(k, carry):
        w = wet_of(k)
        w_next = jnp.where(k + 1 < levels, wet_of(k + 1), 0.0)
        w_east = roll(w, -1, 1)
        w_north = roll(w, -1, 0)
        ke = ke_ref[0, k]
        ke_sel = jnp.where(row >= ny, roll(ke, -1, 1), ke)
        east_mask = w * w_east
        ce_ref[k] = ke_sel * east_mask
        kn = ke_ref[1, k]
        kn_up = roll(kn, -1, 0)
        kn_sel = jnp.where(
            row < ny - 1, kn, jnp.where(row == ny - 1, 0.5 * (kn + kn_up), jnp.where(row == ny, kn_up, 0.0))
        )
        north_mask = w * w_north
        cn_ref[k] = kn_sel * north_mask
        cz_ref[k + 1] = vertical_rate * w * w_next
        src_ref[k] = thaw_rate * shelf * w * (1.0 - w_next)
        wet_ref[k] = w
        gem_ref[k] = east_mask[:ny, :width]
        gnm_ref[k] = jnp.where(row < ny - 1, north_mask, 0.5 * north_mask)[:ny, :width]
        for c in range(chans):
            a_ref[c, k] = w * ve_ref[c, k]
        return carry

    lax.fori_loop(0, levels, setup, 0, unroll=10)

    def operate(x_ref, c, k, diffs=None):
        x = x_ref[c, k]
        above = x_ref[c, jnp.minimum(k + 1, levels - 1)]
        below = x_ref[c, jnp.maximum(k - 1, 0)]
        d_east = roll(x, -1, 1) - x
        d_north = roll(x, -1, 0) - x
        if diffs is not None:
            diffs[0][c, k] = d_east[:ny, :width]
            diffs[1][c, k] = d_north[:ny, :width]
        east = ce_ref[k] * d_east
        north = cn_ref[k] * d_north
        change = (east - roll(east, 1, 1)) + (north - roll(north, 1, 0))
        change = change + (cz_ref[k + 1] * (above - x) - cz_ref[k] * (x - below))
        return x, change

    def forward_first(ck, carry):
        c = ck // levels
        k = ck % levels
        x, change = operate(ue_ref, c, k, (du0e_ref, du0n_ref))
        heat = jnp.where(c == 0, 1.0, 0.0)
        u1_ref[c, k] = wet_ref[k] * (x + change + heat * src_ref[k])
        return carry

    lax.fori_loop(0, planes, forward_first, 0, unroll=10)

    def forward_second(ck, carry):
        c = ck // levels
        k = ck % levels
        x, change = operate(u1_ref, c, k, (du1e_ref, du1n_ref))
        heat = jnp.where(c == 0, 1.0, 0.0)
        out = wet_ref[k] * (x + change + heat * src_ref[k])
        fin_ref[c, k] = out[:ny, :width]
        return carry

    lax.fori_loop(0, planes, forward_second, 0, unroll=10)

    def backward_second(ck, carry):
        c = ck // levels
        k = ck % levels
        x, change = operate(a_ref, c, k, (dv2e_ref, dv2n_ref))
        b_ref[c, k] = wet_ref[k] * (x + change)
        return carry

    lax.fori_loop(0, planes, backward_second, 0, unroll=10)

    def backward_first(ck, carry):
        c = ck // levels
        k = ck % levels
        x, change = operate(b_ref, c, k, (dv1e_ref, dv1n_ref))
        adj_ref[c, k] = (x + change)[:ny, :width]
        return carry

    lax.fori_loop(0, planes, backward_first, 0, unroll=10)

    def gradient(k, carry):
        g_east = jnp.zeros((ny, width), jnp.float32)
        g_north = jnp.zeros((ny, width), jnp.float32)
        for c in range(chans):
            g_east = g_east - du0e_ref[c, k] * dv1e_ref[c, k] - du1e_ref[c, k] * dv2e_ref[c, k]
            g_north = g_north - du0n_ref[c, k] * dv1n_ref[c, k] - du1n_ref[c, k] * dv2n_ref[c, k]
        grad_ref[0, k] = gem_ref[k] * g_east
        grad_ref[1, k] = gnm_ref[k] * g_north
        return carry

    lax.fori_loop(0, levels, gradient, 0, unroll=10)


def on_device(tracers, diffusivity, level_count, shelf_mask, cotangent):
    _, chans, levels, ny, width = tracers.shape
    lanes = width + 128
    rows = -(-(ny + 2) // 8) * 8
    full_kappa = gathered_over_scen(diffusivity)
    fields = jnp.concatenate(
        [
            tracers[0].reshape(chans * levels, ny, width),
            cotangent[0].reshape(chans * levels, ny, width),
            full_kappa.reshape(2 * levels, ny, width),
            level_count.astype(jnp.float32)[None],
            shelf_mask.astype(jnp.float32)[None],
        ]
    )
    ext = extended(fields, lanes, rows)
    field = jax.ShapeDtypeStruct((chans, levels, ny, width), jnp.float32)
    plane = pltpu.VMEM((levels, rows, lanes), jnp.float32)
    planes_c = pltpu.VMEM((chans, levels, rows, lanes), jnp.float32)
    diff = pltpu.VMEM((chans, levels, ny, width), jnp.float32)
    mask = pltpu.VMEM((levels, ny, width), jnp.float32)
    final, adjoint, grad = pl.pallas_call(
        diffusion_kernel,
        out_shape=(field, field, jax.ShapeDtypeStruct((2, levels, ny, width), jnp.float32)),
        scratch_shapes=[
            plane,
            plane,
            plane,
            pltpu.VMEM((levels + 1, rows, lanes), jnp.float32),
            plane,
            mask,
            mask,
            planes_c,
            planes_c,
            planes_c,
        ]
        + [diff] * 8,
        compiler_params=pltpu.CompilerParams(vmem_limit_bytes=48 * 1024 * 1024),
        interpret=INTERPRET,
    )(ext)
    kappa_grad = summed_over_scen(grad)
    return (final[None], adjoint[None], kappa_grad)


def gathered_over_scen(block):
    parts = lax.axis_size("scen")
    if parts % 2:
        return lax.all_gather(block, "scen", axis=2, tiled=True)
    kinds, levels, rows, width = block.shape
    me = lax.axis_index("scen")
    core = me % 2
    chip = me // 2
    chips = parts // 2
    got = [block]
    for step in range(1, chips):
        got.append(
            lax.ppermute(block, "scen", [(q, ((q // 2 + step) % chips) * 2 + q % 2) for q in range(parts)])
        )
    same = jnp.stack(got)
    other = lax.ppermute(same, "scen", [(q, q ^ 1) for q in range(parts)])
    by_core = jnp.where(core == 0, jnp.stack([same, other], axis=1), jnp.stack([other, same], axis=1))
    order = (chip - jnp.arange(chips)) % chips
    by_chip = jnp.take(by_core, order, axis=0)
    return by_chip.transpose(2, 3, 0, 1, 4, 5).reshape(kinds, levels, parts * rows, width)


def summed_over_scen(grad):
    parts = lax.axis_size("scen")
    kinds, levels, ny, width = grad.shape
    if parts % 2:
        split = grad.reshape(kinds, levels, parts, ny // parts, width)
        return lax.all_to_all(split, "scen", 2, 2, tiled=True).sum(axis=2)
    me = lax.axis_index("scen")
    core = me % 2
    chip = me // 2
    chips = parts // 2
    split = grad.reshape(kinds, levels, chips, 2, ny // parts, width)
    mine = lax.dynamic_index_in_dim(split, core, axis=3, keepdims=False)
    other = lax.dynamic_index_in_dim(split, 1 - core, axis=3, keepdims=False)
    pair = lax.ppermute(other, "scen", [(q, q ^ 1) for q in range(parts)])
    chip_sum = mine + pair
    total = lax.dynamic_index_in_dim(chip_sum, chip, axis=2, keepdims=False)
    for step in range(1, chips):
        send = lax.dynamic_index_in_dim(chip_sum, (chip + step) % chips, axis=2, keepdims=False)
        total = total + lax.ppermute(
            send, "scen", [(q, ((q // 2 + step) % chips) * 2 + q % 2) for q in range(parts)]
        )
    return total


def solution(mesh):
    placed = (
        P("scen", None, None, None, "space"),
        P(None, None, "scen", "space"),
        P(None, "space"),
        P(None, "space"),
        P("scen", None, None, None, "space"),
    )
    return jax.shard_map(
        on_device,
        mesh=mesh,
        in_specs=placed,
        out_specs=(
            P("scen", None, None, None, "space"),
            P("scen", None, None, None, "space"),
            P(None, None, "scen", "space"),
        ),
        check_vma=False,
    )
```

```python
import jax
import jax.numpy as jnp
from jax import lax
from jax.experimental import pallas as pl
from jax.experimental.pallas import tpu as pltpu
from jax.sharding import PartitionSpec as P

STEPS = 2
HALO = 2

vertical_rate = 0.1
thaw_rate = 0.3

INTERPRET = False


def shifted(x, perm):
    return lax.ppermute(x, "space", perm)


def picker(size, positions):
    where = lax.broadcasted_iota(jnp.int32, (size, len(positions)), 0)
    slot = lax.broadcasted_iota(jnp.int32, (size, len(positions)), 1)
    hit = jnp.zeros((size, len(positions)), jnp.bool_)
    for p, at in enumerate(positions):
        hit = hit | ((slot == p) & (where == at))
    return hit.astype(jnp.float32)


def contract(a, b, dims):
    return lax.dot_general(
        a, b, (dims, ((), ())), precision=lax.Precision.HIGHEST, preferred_element_type=jnp.float32
    )


def extended(fields, lanes, rows):
    n = lax.axis_size("space")
    count, ny, width = fields.shape
    spare = lanes - width
    flat = fields.reshape(count * ny, width)
    edges = contract(picker(width, [width - 2, width - 1, 0, 1]), flat, ((0,), (1,)))
    west = shifted(edges[0:2], [(q, (q + 1) % n) for q in range(n)])
    east = shifted(edges[2:4], [(q, (q - 1) % n) for q in range(n)])
    mirrored = fields[:, ny - 1:ny - 3:-1, ::-1]
    ghost = shifted(mirrored, [(q, n - 1 - q) for q in range(n)])
    top_edges = edges.reshape(4, count, ny)[:, :, ny - 1:ny - 3:-1]
    ghost_east = shifted(top_edges[1::-1].reshape(2, count * 2), [(q, (n - 2 - q) % n) for q in range(n)])
    ghost_west = shifted(top_edges[3:1:-1].reshape(2, count * 2), [(q, (n - q) % n) for q in range(n)])
    place = picker(spare, [0, 1, spare - 2, spare - 1]).T
    side = contract(jnp.concatenate([east, west]), place, ((0,), (0,))).reshape(count, ny, spare)
    ghost_halo = jnp.concatenate([ghost_east, ghost_west]).reshape(4, count * 2)
    ghost_side = contract(ghost_halo, place, ((0,), (0,))).reshape(count, 2, spare)
    top = jnp.concatenate([fields, side], axis=-1)
    folded = jnp.concatenate([ghost, ghost_side], axis=-1)
    pad = jnp.zeros((count, rows - ny - 2, lanes), fields.dtype)
    return jnp.concatenate([top, folded, pad], axis=1)


def roll(x, shift, axis):
    return pltpu.roll(x, shift % x.shape[axis], axis)


class Planes:
    def __init__(self, ref, start, levels):
        self.ref = ref
        self.start = start
        self.levels = levels

    def __getitem__(self, index):
        c, k = index
        return self.ref[self.start + c * self.levels + k]


def diffusion_kernel(
    x_ref,
    fin_ref, adj_ref, grad_ref,
    wet_ref, ce_ref, cn_ref, cz_ref, src_ref, gem_ref, gnm_ref, u1_ref, a_ref, b_ref,
    du0e_ref, du0n_ref, du1e_ref, du1n_ref, dv1e_ref, dv1n_ref, dv2e_ref, dv2n_ref,
):
    levels, rows, lanes = wet_ref.shape
    chans, _, ny, width = fin_ref.shape
    row = lax.broadcasted_iota(jnp.int32, (rows, lanes), 0)
    lane = lax.broadcasted_iota(jnp.int32, (rows, lanes), 1)
    planes = chans * levels
    ue_ref = Planes(x_ref, 0, levels)
    ve_ref = Planes(x_ref, planes, levels)
    ke_ref = Planes(x_ref, 2 * planes, levels)
    lev = x_ref[2 * planes + 2 * levels]
    shelf = x_ref[2 * planes + 2 * levels + 1]

    def wet_of(k):
        return (lev > k.astype(jnp.float32)).astype(jnp.float32)

    cz_ref[0] = jnp.zeros((rows, lanes), jnp.float32)

    def setup(k, carry):
        w = wet_of(k)
        w_next = jnp.where(k + 1 < levels, wet_of(k + 1), 0.0)
        w_east = roll(w, -1, 1)
        w_north = roll(w, -1, 0)
        ke = ke_ref[0, k]
        ke_sel = jnp.where(row >= ny, roll(ke, -1, 1), ke)
        east_mask = w * w_east
        ce_ref[k] = ke_sel * east_mask
        kn = ke_ref[1, k]
        kn_up = roll(kn, -1, 0)
        kn_sel = jnp.where(
            row < ny - 1, kn, jnp.where(row == ny - 1, 0.5 * (kn + kn_up), jnp.where(row == ny, kn_up, 0.0))
        )
        north_mask = w * w_north
        cn_ref[k] = kn_sel * north_mask
        cz_ref[k + 1] = vertical_rate * w * w_next
        src_ref[k] = thaw_rate * shelf * w * (1.0 - w_next)
        wet_ref[k] = w
        gem_ref[k] = east_mask[:ny, :width]
        gnm_ref[k] = jnp.where(row < ny - 1, north_mask, 0.5 * north_mask)[:ny, :width]
        for c in range(chans):
            a_ref[c, k] = w * ve_ref[c, k]
        return carry

    lax.fori_loop(0, levels, setup, 0, unroll=4)

    def operate(x_ref, c, k, diffs=None):
        x = x_ref[c, k]
        above = x_ref[c, jnp.minimum(k + 1, levels - 1)]
        below = x_ref[c, jnp.maximum(k - 1, 0)]
        d_east = roll(x, -1, 1) - x
        d_north = roll(x, -1, 0) - x
        if diffs is not None:
            diffs[0][c, k] = d_east[:ny, :width]
            diffs[1][c, k] = d_north[:ny, :width]
        east = ce_ref[k] * d_east
        north = cn_ref[k] * d_north
        change = (east - roll(east, 1, 1)) + (north - roll(north, 1, 0))
        change = change + (cz_ref[k + 1] * (above - x) - cz_ref[k] * (x - below))
        return x, change

    def forward_first(ck, carry):
        c = ck // levels
        k = ck % levels
        x, change = operate(ue_ref, c, k, (du0e_ref, du0n_ref))
        heat = jnp.where(c == 0, 1.0, 0.0)
        u1_ref[c, k] = wet_ref[k] * (x + change + heat * src_ref[k])
        return carry

    lax.fori_loop(0, planes, forward_first, 0, unroll=8)

    def forward_second(ck, carry):
        c = ck // levels
        k = ck % levels
        x, change = operate(u1_ref, c, k, (du1e_ref, du1n_ref))
        heat = jnp.where(c == 0, 1.0, 0.0)
        out = wet_ref[k] * (x + change + heat * src_ref[k])
        fin_ref[c, k] = out[:ny, :width]
        return carry

    lax.fori_loop(0, planes, forward_second, 0, unroll=8)

    def backward_second(ck, carry):
        c = ck // levels
        k = ck % levels
        x, change = operate(a_ref, c, k, (dv2e_ref, dv2n_ref))
        b_ref[c, k] = wet_ref[k] * (x + change)
        return carry

    lax.fori_loop(0, planes, backward_second, 0, unroll=8)

    def backward_first(ck, carry):
        c = ck // levels
        k = ck % levels
        x, change = operate(b_ref, c, k, (dv1e_ref, dv1n_ref))
        adj_ref[c, k] = (x + change)[:ny, :width]
        return carry

    lax.fori_loop(0, planes, backward_first, 0, unroll=8)

    def gradient(k, carry):
        g_east = jnp.zeros((ny, width), jnp.float32)
        g_north = jnp.zeros((ny, width), jnp.float32)
        for c in range(chans):
            g_east = g_east - du0e_ref[c, k] * dv1e_ref[c, k] - du1e_ref[c, k] * dv2e_ref[c, k]
            g_north = g_north - du0n_ref[c, k] * dv1n_ref[c, k] - du1n_ref[c, k] * dv2n_ref[c, k]
        grad_ref[0, k] = gem_ref[k] * g_east
        grad_ref[1, k] = gnm_ref[k] * g_north
        return carry

    lax.fori_loop(0, levels, gradient, 0, unroll=4)


def on_device(tracers, diffusivity, level_count, shelf_mask, cotangent):
    _, chans, levels, ny, width = tracers.shape
    lanes = width + 128
    rows = -(-(ny + 2) // 8) * 8
    full_kappa = gathered_over_scen(diffusivity)
    fields = jnp.concatenate(
        [
            tracers[0].reshape(chans * levels, ny, width),
            cotangent[0].reshape(chans * levels, ny, width),
            full_kappa.reshape(2 * levels, ny, width),
            level_count.astype(jnp.float32)[None],
            shelf_mask.astype(jnp.float32)[None],
        ]
    )
    ext = extended(fields, lanes, rows)
    field = jax.ShapeDtypeStruct((chans, levels, ny, width), jnp.float32)
    plane = pltpu.VMEM((levels, rows, lanes), jnp.float32)
    planes_c = pltpu.VMEM((chans, levels, rows, lanes), jnp.float32)
    diff = pltpu.VMEM((chans, levels, ny, width), jnp.float32)
    mask = pltpu.VMEM((levels, ny, width), jnp.float32)
    final, adjoint, grad = pl.pallas_call(
        diffusion_kernel,
        out_shape=(field, field, jax.ShapeDtypeStruct((2, levels, ny, width), jnp.float32)),
        scratch_shapes=[
            plane,
            plane,
            plane,
            pltpu.VMEM((levels + 1, rows, lanes), jnp.float32),
            plane,
            mask,
            mask,
            planes_c,
            planes_c,
            planes_c,
        ]
        + [diff] * 8,
        compiler_params=pltpu.CompilerParams(vmem_limit_bytes=48 * 1024 * 1024),
        interpret=INTERPRET,
    )(ext)
    kappa_grad = summed_over_scen(grad)
    return (final[None], adjoint[None], kappa_grad)


def gathered_over_scen(block):
    parts = lax.axis_size("scen")
    if parts % 2:
        return lax.all_gather(block, "scen", axis=2, tiled=True)
    kinds, levels, rows, width = block.shape
    me = lax.axis_index("scen")
    core = me % 2
    chip = me // 2
    chips = parts // 2
    got = [block]
    for step in range(1, chips):
        got.append(
            lax.ppermute(block, "scen", [(q, ((q // 2 + step) % chips) * 2 + q % 2) for q in range(parts)])
        )
    same = jnp.stack(got)
    other = lax.ppermute(same, "scen", [(q, q ^ 1) for q in range(parts)])
    by_core = jnp.where(core == 0, jnp.stack([same, other], axis=1), jnp.stack([other, same], axis=1))
    order = (chip - jnp.arange(chips)) % chips
    by_chip = jnp.take(by_core, order, axis=0)
    return by_chip.transpose(2, 3, 0, 1, 4, 5).reshape(kinds, levels, parts * rows, width)


def summed_over_scen(grad):
    parts = lax.axis_size("scen")
    kinds, levels, ny, width = grad.shape
    if parts % 2:
        split = grad.reshape(kinds, levels, parts, ny // parts, width)
        return lax.all_to_all(split, "scen", 2, 2, tiled=True).sum(axis=2)
    me = lax.axis_index("scen")
    core = me % 2
    chip = me // 2
    chips = parts // 2
    split = grad.reshape(kinds, levels, chips, 2, ny // parts, width)
    mine = lax.dynamic_index_in_dim(split, core, axis=3, keepdims=False)
    other = lax.dynamic_index_in_dim(split, 1 - core, axis=3, keepdims=False)
    pair = lax.ppermute(other, "scen", [(q, q ^ 1) for q in range(parts)])
    chip_sum = mine + pair
    total = lax.dynamic_index_in_dim(chip_sum, chip, axis=2, keepdims=False)
    for step in range(1, chips):
        send = lax.dynamic_index_in_dim(chip_sum, (chip + step) % chips, axis=2, keepdims=False)
        total = total + lax.ppermute(
            send, "scen", [(q, ((q // 2 + step) % chips) * 2 + q % 2) for q in range(parts)]
        )
    return total


def solution(mesh):
    placed = (
        P("scen", None, None, None, "space"),
        P(None, None, "scen", "space"),
        P(None, "space"),
        P(None, "space"),
        P("scen", None, None, None, "space"),
    )
    return jax.shard_map(
        on_device,
        mesh=mesh,
        in_specs=placed,
        out_specs=(
            P("scen", None, None, None, "space"),
            P("scen", None, None, None, "space"),
            P(None, None, "scen", "space"),
        ),
        check_vma=False,
    )
```

```python
import jax
import jax.numpy as jnp
from jax import lax
from jax.experimental import pallas as pl
from jax.experimental.pallas import tpu as pltpu
from jax.sharding import PartitionSpec as P

STEPS = 2
HALO = 2

vertical_rate = 0.1
thaw_rate = 0.3

INTERPRET = False


def shifted(x, perm):
    return lax.ppermute(x, "space", perm)


def picker(size, positions):
    where = lax.broadcasted_iota(jnp.int32, (size, len(positions)), 0)
    slot = lax.broadcasted_iota(jnp.int32, (size, len(positions)), 1)
    hit = jnp.zeros((size, len(positions)), jnp.bool_)
    for p, at in enumerate(positions):
        hit = hit | ((slot == p) & (where == at))
    return hit.astype(jnp.float32)


def contract(a, b, dims):
    return lax.dot_general(
        a, b, (dims, ((), ())), precision=lax.Precision.HIGHEST, preferred_element_type=jnp.float32
    )


def extended(fields, lanes, rows):
    n = lax.axis_size("space")
    count, ny, width = fields.shape
    spare = lanes - width
    flat = fields.reshape(count * ny, width)
    edges = contract(picker(width, [width - 2, width - 1, 0, 1]), flat, ((0,), (1,)))
    west = shifted(edges[0:2], [(q, (q + 1) % n) for q in range(n)])
    east = shifted(edges[2:4], [(q, (q - 1) % n) for q in range(n)])
    mirrored = fields[:, ny - 1:ny - 3:-1, ::-1]
    ghost = shifted(mirrored, [(q, n - 1 - q) for q in range(n)])
    top_edges = edges.reshape(4, count, ny)[:, :, ny - 1:ny - 3:-1]
    ghost_east = shifted(top_edges[1::-1], [(q, (n - 2 - q) % n) for q in range(n)])
    ghost_west = shifted(top_edges[3:1:-1], [(q, (n - q) % n) for q in range(n)])
    place = picker(spare, [0, 1, spare - 2, spare - 1]).T
    side = contract(jnp.concatenate([east, west]), place, ((0,), (0,))).reshape(count, ny, spare)
    ghost_halo = jnp.concatenate([ghost_east, ghost_west]).reshape(4, count * 2)
    ghost_side = contract(ghost_halo, place, ((0,), (0,))).reshape(count, 2, spare)
    top = jnp.concatenate([fields, side], axis=-1)
    folded = jnp.concatenate([ghost, ghost_side], axis=-1)
    pad = jnp.zeros((count, rows - ny - 2, lanes), fields.dtype)
    return jnp.concatenate([top, folded, pad], axis=1)


def roll(x, shift, axis):
    return pltpu.roll(x, shift % x.shape[axis], axis)


class Planes:
    def __init__(self, ref, start, levels):
        self.ref = ref
        self.start = start
        self.levels = levels

    def __getitem__(self, index):
        c, k = index
        return self.ref[self.start + c * self.levels + k]


def diffusion_kernel(
    x_ref,
    fin_ref, adj_ref, grad_ref,
    wet_ref, ce_ref, cn_ref, cz_ref, src_ref, gem_ref, gnm_ref, u1_ref, a_ref, b_ref,
    du0e_ref, du0n_ref, du1e_ref, du1n_ref, dv1e_ref, dv1n_ref, dv2e_ref, dv2n_ref,
):
    levels, rows, lanes = wet_ref.shape
    chans, _, ny, width = fin_ref.shape
    row = lax.broadcasted_iota(jnp.int32, (rows, lanes), 0)
    lane = lax.broadcasted_iota(jnp.int32, (rows, lanes), 1)
    planes = chans * levels
    ue_ref = Planes(x_ref, 0, levels)
    ve_ref = Planes(x_ref, planes, levels)
    ke_ref = Planes(x_ref, 2 * planes, levels)
    lev = x_ref[2 * planes + 2 * levels]
    shelf = x_ref[2 * planes + 2 * levels + 1]

    def wet_of(k):
        return (lev > k.astype(jnp.float32)).astype(jnp.float32)

    cz_ref[0] = jnp.zeros((rows, lanes), jnp.float32)

    def setup(k, carry):
        w = wet_of(k)
        w_next = jnp.where(k + 1 < levels, wet_of(k + 1), 0.0)
        w_east = roll(w, -1, 1)
        w_north = roll(w, -1, 0)
        ke = ke_ref[0, k]
        ke_sel = jnp.where(row >= ny, roll(ke, -1, 1), ke)
        east_mask = w * w_east
        ce_ref[k] = ke_sel * east_mask
        kn = ke_ref[1, k]
        kn_up = roll(kn, -1, 0)
        kn_sel = jnp.where(
            row < ny - 1, kn, jnp.where(row == ny - 1, 0.5 * (kn + kn_up), jnp.where(row == ny, kn_up, 0.0))
        )
        north_mask = w * w_north
        cn_ref[k] = kn_sel * north_mask
        cz_ref[k + 1] = vertical_rate * w * w_next
        src_ref[k] = thaw_rate * shelf * w * (1.0 - w_next)
        wet_ref[k] = w
        gem_ref[k] = east_mask[:ny, :width]
        gnm_ref[k] = jnp.where(row < ny - 1, north_mask, 0.5 * north_mask)[:ny, :width]
        for c in range(chans):
            a_ref[c, k] = w * ve_ref[c, k]
        return carry

    lax.fori_loop(0, levels, setup, 0, unroll=4)

    def operate(x_ref, c, k, diffs=None):
        x = x_ref[c, k]
        above = x_ref[c, jnp.minimum(k + 1, levels - 1)]
        below = x_ref[c, jnp.maximum(k - 1, 0)]
        d_east = roll(x, -1, 1) - x
        d_north = roll(x, -1, 0) - x
        if diffs is not None:
            diffs[0][c, k] = d_east[:ny, :width]
            diffs[1][c, k] = d_north[:ny, :width]
        east = ce_ref[k] * d_east
        north = cn_ref[k] * d_north
        change = (east - roll(east, 1, 1)) + (north - roll(north, 1, 0))
        change = change + (cz_ref[k + 1] * (above - x) - cz_ref[k] * (x - below))
        return x, change

    def forward_first(ck, carry):
        c = ck // levels
        k = ck % levels
        x, change = operate(ue_ref, c, k, (du0e_ref, du0n_ref))
        heat = jnp.where(c == 0, 1.0, 0.0)
        u1_ref[c, k] = wet_ref[k] * (x + change + heat * src_ref[k])
        return carry

    lax.fori_loop(0, planes, forward_first, 0, unroll=8)

    def forward_second(ck, carry):
        c = ck // levels
        k = ck % levels
        x, change = operate(u1_ref, c, k, (du1e_ref, du1n_ref))
        heat = jnp.where(c == 0, 1.0, 0.0)
        out = wet_ref[k] * (x + change + heat * src_ref[k])
        fin_ref[c, k] = out[:ny, :width]
        return carry

    lax.fori_loop(0, planes, forward_second, 0, unroll=8)

    def backward_second(ck, carry):
        c = ck // levels
        k = ck % levels
        x, change = operate(a_ref, c, k, (dv2e_ref, dv2n_ref))
        b_ref[c, k] = wet_ref[k] * (x + change)
        return carry

    lax.fori_loop(0, planes, backward_second, 0, unroll=8)

    def backward_first(ck, carry):
        c = ck // levels
        k = ck % levels
        x, change = operate(b_ref, c, k, (dv1e_ref, dv1n_ref))
        adj_ref[c, k] = (x + change)[:ny, :width]
        return carry

    lax.fori_loop(0, planes, backward_first, 0, unroll=8)

    def gradient(k, carry):
        g_east = jnp.zeros((ny, width), jnp.float32)
        g_north = jnp.zeros((ny, width), jnp.float32)
        for c in range(chans):
            g_east = g_east - du0e_ref[c, k] * dv1e_ref[c, k] - du1e_ref[c, k] * dv2e_ref[c, k]
            g_north = g_north - du0n_ref[c, k] * dv1n_ref[c, k] - du1n_ref[c, k] * dv2n_ref[c, k]
        grad_ref[0, k] = gem_ref[k] * g_east
        grad_ref[1, k] = gnm_ref[k] * g_north
        return carry

    lax.fori_loop(0, levels, gradient, 0, unroll=4)


def on_device(tracers, diffusivity, level_count, shelf_mask, cotangent):
    _, chans, levels, ny, width = tracers.shape
    lanes = width + 128
    rows = -(-(ny + 2) // 8) * 8
    full_kappa = gathered_over_scen(diffusivity)
    fields = jnp.concatenate(
        [
            tracers[0].reshape(chans * levels, ny, width),
            cotangent[0].reshape(chans * levels, ny, width),
            full_kappa.reshape(2 * levels, ny, width),
            level_count.astype(jnp.float32)[None],
            shelf_mask.astype(jnp.float32)[None],
        ]
    )
    ext = extended(fields, lanes, rows)
    field = jax.ShapeDtypeStruct((chans, levels, ny, width), jnp.float32)
    plane = pltpu.VMEM((levels, rows, lanes), jnp.float32)
    planes_c = pltpu.VMEM((chans, levels, rows, lanes), jnp.float32)
    diff = pltpu.VMEM((chans, levels, ny, width), jnp.float32)
    mask = pltpu.VMEM((levels, ny, width), jnp.float32)
    final, adjoint, grad = pl.pallas_call(
        diffusion_kernel,
        out_shape=(field, field, jax.ShapeDtypeStruct((2, levels, ny, width), jnp.float32)),
        scratch_shapes=[
            plane,
            plane,
            plane,
            pltpu.VMEM((levels + 1, rows, lanes), jnp.float32),
            plane,
            mask,
            mask,
            planes_c,
            planes_c,
            planes_c,
        ]
        + [diff] * 8,
        compiler_params=pltpu.CompilerParams(vmem_limit_bytes=48 * 1024 * 1024),
        interpret=INTERPRET,
    )(ext)
    kappa_grad = summed_over_scen(grad)
    return (final[None], adjoint[None], kappa_grad)


def gathered_over_scen(block):
    parts = lax.axis_size("scen")
    kinds, levels, rows, width = block.shape
    me = lax.axis_index("scen")
    got = [block]
    for step in range(1, parts):
        got.append(lax.ppermute(block, "scen", [(q, (q + step) % parts) for q in range(parts)]))
    order = (me - jnp.arange(parts)) % parts
    by_owner = jnp.take(jnp.stack(got), order, axis=0)
    return by_owner.transpose(1, 2, 0, 3, 4).reshape(kinds, levels, parts * rows, width)


def summed_over_scen(grad):
    parts = lax.axis_size("scen")
    kinds, levels, ny, width = grad.shape
    if parts % 2:
        split = grad.reshape(kinds, levels, parts, ny // parts, width)
        return lax.all_to_all(split, "scen", 2, 2, tiled=True).sum(axis=2)
    me = lax.axis_index("scen")
    core = me % 2
    chip = me // 2
    chips = parts // 2
    split = grad.reshape(kinds, levels, chips, 2, ny // parts, width)
    mine = lax.dynamic_index_in_dim(split, core, axis=3, keepdims=False)
    other = lax.dynamic_index_in_dim(split, 1 - core, axis=3, keepdims=False)
    pair = lax.ppermute(other, "scen", [(q, q ^ 1) for q in range(parts)])
    chip_sum = mine + pair
    total = lax.dynamic_index_in_dim(chip_sum, chip, axis=2, keepdims=False)
    for step in range(1, chips):
        send = lax.dynamic_index_in_dim(chip_sum, (chip + step) % chips, axis=2, keepdims=False)
        total = total + lax.ppermute(
            send, "scen", [(q, ((q // 2 + step) % chips) * 2 + q % 2) for q in range(parts)]
        )
    return total


def solution(mesh):
    placed = (
        P("scen", None, None, None, "space"),
        P(None, None, "scen", "space"),
        P(None, "space"),
        P(None, "space"),
        P("scen", None, None, None, "space"),
    )
    return jax.shard_map(
        on_device,
        mesh=mesh,
        in_specs=placed,
        out_specs=(
            P("scen", None, None, None, "space"),
            P("scen", None, None, None, "space"),
            P(None, None, "scen", "space"),
        ),
        check_vma=False,
    )
```

```python
import jax
import jax.numpy as jnp
from jax import lax
from jax.experimental import pallas as pl
from jax.experimental.pallas import tpu as pltpu
from jax.sharding import PartitionSpec as P

STEPS = 2
HALO = 2

vertical_rate = 0.1
thaw_rate = 0.3

INTERPRET = False


def shifted(x, perm):
    return lax.ppermute(x, "space", perm)


def picker(size, positions):
    where = lax.broadcasted_iota(jnp.int32, (size, len(positions)), 0)
    slot = lax.broadcasted_iota(jnp.int32, (size, len(positions)), 1)
    hit = jnp.zeros((size, len(positions)), jnp.bool_)
    for p, at in enumerate(positions):
        hit = hit | ((slot == p) & (where == at))
    return hit.astype(jnp.float32)


def contract(a, b, dims):
    return lax.dot_general(
        a, b, (dims, ((), ())), precision=lax.Precision.HIGHEST, preferred_element_type=jnp.float32
    )


def extended(fields, lanes, rows):
    n = lax.axis_size("space")
    count, ny, width = fields.shape
    spare = lanes - width
    flat = fields.reshape(count * ny, width)
    edges = contract(picker(width, [width - 2, width - 1, 0, 1]), flat, ((0,), (1,)))
    west = shifted(edges[0:2], [(q, (q + 1) % n) for q in range(n)])
    east = shifted(edges[2:4], [(q, (q - 1) % n) for q in range(n)])
    mirrored = fields[:, ny - 1:ny - 3:-1, ::-1]
    ghost = shifted(mirrored, [(q, n - 1 - q) for q in range(n)])
    top_edges = edges.reshape(4, count, ny)[:, :, ny - 1:ny - 3:-1]
    ghost_east = shifted(top_edges[1::-1], [(q, (n - 2 - q) % n) for q in range(n)])
    ghost_west = shifted(top_edges[3:1:-1], [(q, (n - q) % n) for q in range(n)])
    place = picker(spare, [0, 1, spare - 2, spare - 1]).T
    side = contract(jnp.concatenate([east, west]), place, ((0,), (0,))).reshape(count, ny, spare)
    ghost_halo = jnp.concatenate([ghost_east, ghost_west]).reshape(4, count * 2)
    ghost_side = contract(ghost_halo, place, ((0,), (0,))).reshape(count, 2, spare)
    top = jnp.concatenate([fields, side], axis=-1)
    folded = jnp.concatenate([ghost, ghost_side], axis=-1)
    pad = jnp.zeros((count, rows - ny - 2, lanes), fields.dtype)
    return jnp.concatenate([top, folded, pad], axis=1)


def roll(x, shift, axis):
    return pltpu.roll(x, shift % x.shape[axis], axis)


class Planes:
    def __init__(self, ref, start, levels):
        self.ref = ref
        self.start = start
        self.levels = levels

    def __getitem__(self, index):
        c, k = index
        return self.ref[self.start + c * self.levels + k]


def diffusion_kernel(
    x_ref,
    fin_ref, adj_ref, grad_ref,
    wet_ref, ce_ref, cn_ref, cz_ref, src_ref, gem_ref, gnm_ref, u1_ref, a_ref, b_ref,
    du0e_ref, du0n_ref, du1e_ref, du1n_ref, dv1e_ref, dv1n_ref, dv2e_ref, dv2n_ref,
):
    levels, rows, lanes = wet_ref.shape
    chans, _, ny, width = fin_ref.shape
    row = lax.broadcasted_iota(jnp.int32, (rows, lanes), 0)
    lane = lax.broadcasted_iota(jnp.int32, (rows, lanes), 1)
    planes = chans * levels
    ue_ref = Planes(x_ref, 0, levels)
    ve_ref = Planes(x_ref, planes, levels)
    ke_ref = Planes(x_ref, 2 * planes, levels)
    lev = x_ref[2 * planes + 2 * levels]
    shelf = x_ref[2 * planes + 2 * levels + 1]

    def wet_of(k):
        return (lev > k.astype(jnp.float32)).astype(jnp.float32)

    cz_ref[0] = jnp.zeros((rows, lanes), jnp.float32)

    def setup(k, carry):
        w = wet_of(k)
        w_next = jnp.where(k + 1 < levels, wet_of(k + 1), 0.0)
        w_east = roll(w, -1, 1)
        w_north = roll(w, -1, 0)
        ke = ke_ref[0, k]
        ke_sel = jnp.where(row >= ny, roll(ke, -1, 1), ke)
        east_mask = w * w_east
        ce_ref[k] = ke_sel * east_mask
        kn = ke_ref[1, k]
        kn_up = roll(kn, -1, 0)
        kn_sel = jnp.where(
            row < ny - 1, kn, jnp.where(row == ny - 1, 0.5 * (kn + kn_up), jnp.where(row == ny, kn_up, 0.0))
        )
        north_mask = w * w_north
        cn_ref[k] = kn_sel * north_mask
        cz_ref[k + 1] = vertical_rate * w * w_next
        src_ref[k] = thaw_rate * shelf * w * (1.0 - w_next)
        wet_ref[k] = w
        gem_ref[k] = east_mask[:ny, :width]
        gnm_ref[k] = jnp.where(row < ny - 1, north_mask, 0.5 * north_mask)[:ny, :width]
        for c in range(chans):
            a_ref[c, k] = w * ve_ref[c, k]
        return carry

    lax.fori_loop(0, levels, setup, 0, unroll=True)

    def operate(x_ref, c, k, diffs=None):
        x = x_ref[c, k]
        above = x_ref[c, jnp.minimum(k + 1, levels - 1)]
        below = x_ref[c, jnp.maximum(k - 1, 0)]
        d_east = roll(x, -1, 1) - x
        d_north = roll(x, -1, 0) - x
        if diffs is not None:
            diffs[0][c, k] = d_east[:ny, :width]
            diffs[1][c, k] = d_north[:ny, :width]
        east = ce_ref[k] * d_east
        north = cn_ref[k] * d_north
        change = (east - roll(east, 1, 1)) + (north - roll(north, 1, 0))
        change = change + (cz_ref[k + 1] * (above - x) - cz_ref[k] * (x - below))
        return x, change

    def forward_first(ck, carry):
        c = ck // levels
        k = ck % levels
        x, change = operate(ue_ref, c, k, (du0e_ref, du0n_ref))
        heat = jnp.where(c == 0, 1.0, 0.0)
        u1_ref[c, k] = wet_ref[k] * (x + change + heat * src_ref[k])
        return carry

    lax.fori_loop(0, planes, forward_first, 0, unroll=8)

    def forward_second(ck, carry):
        c = ck // levels
        k = ck % levels
        x, change = operate(u1_ref, c, k, (du1e_ref, du1n_ref))
        heat = jnp.where(c == 0, 1.0, 0.0)
        out = wet_ref[k] * (x + change + heat * src_ref[k])
        fin_ref[c, k] = out[:ny, :width]
        return carry

    lax.fori_loop(0, planes, forward_second, 0, unroll=8)

    def backward_second(ck, carry):
        c = ck // levels
        k = ck % levels
        x, change = operate(a_ref, c, k, (dv2e_ref, dv2n_ref))
        b_ref[c, k] = wet_ref[k] * (x + change)
        return carry

    lax.fori_loop(0, planes, backward_second, 0, unroll=8)

    def backward_first(ck, carry):
        c = ck // levels
        k = ck % levels
        x, change = operate(b_ref, c, k, (dv1e_ref, dv1n_ref))
        adj_ref[c, k] = (x + change)[:ny, :width]
        return carry

    lax.fori_loop(0, planes, backward_first, 0, unroll=8)

    def gradient(k, carry):
        g_east = jnp.zeros((ny, width), jnp.float32)
        g_north = jnp.zeros((ny, width), jnp.float32)
        for c in range(chans):
            g_east = g_east - du0e_ref[c, k] * dv1e_ref[c, k] - du1e_ref[c, k] * dv2e_ref[c, k]
            g_north = g_north - du0n_ref[c, k] * dv1n_ref[c, k] - du1n_ref[c, k] * dv2n_ref[c, k]
        grad_ref[0, k] = gem_ref[k] * g_east
        grad_ref[1, k] = gnm_ref[k] * g_north
        return carry

    lax.fori_loop(0, levels, gradient, 0, unroll=True)


def on_device(tracers, diffusivity, level_count, shelf_mask, cotangent):
    _, chans, levels, ny, width = tracers.shape
    lanes = width + 128
    rows = -(-(ny + 2) // 8) * 8
    full_kappa = gathered_over_scen(diffusivity)
    fields = jnp.concatenate(
        [
            tracers[0].reshape(chans * levels, ny, width),
            cotangent[0].reshape(chans * levels, ny, width),
            full_kappa.reshape(2 * levels, ny, width),
            level_count.astype(jnp.float32)[None],
            shelf_mask.astype(jnp.float32)[None],
        ]
    )
    ext = extended(fields, lanes, rows)
    field = jax.ShapeDtypeStruct((chans, levels, ny, width), jnp.float32)
    plane = pltpu.VMEM((levels, rows, lanes), jnp.float32)
    planes_c = pltpu.VMEM((chans, levels, rows, lanes), jnp.float32)
    diff = pltpu.VMEM((chans, levels, ny, width), jnp.float32)
    mask = pltpu.VMEM((levels, ny, width), jnp.float32)
    final, adjoint, grad = pl.pallas_call(
        diffusion_kernel,
        out_shape=(field, field, jax.ShapeDtypeStruct((2, levels, ny, width), jnp.float32)),
        scratch_shapes=[
            plane,
            plane,
            plane,
            pltpu.VMEM((levels + 1, rows, lanes), jnp.float32),
            plane,
            mask,
            mask,
            planes_c,
            planes_c,
            planes_c,
        ]
        + [diff] * 8,
        compiler_params=pltpu.CompilerParams(vmem_limit_bytes=48 * 1024 * 1024),
        interpret=INTERPRET,
    )(ext)
    kappa_grad = summed_over_scen(grad)
    return (final[None], adjoint[None], kappa_grad)


def gathered_over_scen(block):
    parts = lax.axis_size("scen")
    if parts % 2:
        return lax.all_gather(block, "scen", axis=2, tiled=True)
    kinds, levels, rows, width = block.shape
    me = lax.axis_index("scen")
    core = me % 2
    chip = me // 2
    chips = parts // 2
    got = [block]
    for step in range(1, chips):
        got.append(
            lax.ppermute(block, "scen", [(q, ((q // 2 + step) % chips) * 2 + q % 2) for q in range(parts)])
        )
    same = jnp.stack(got)
    other = lax.ppermute(same, "scen", [(q, q ^ 1) for q in range(parts)])
    by_core = jnp.where(core == 0, jnp.stack([same, other], axis=1), jnp.stack([other, same], axis=1))
    order = (chip - jnp.arange(chips)) % chips
    by_chip = jnp.take(by_core, order, axis=0)
    return by_chip.transpose(2, 3, 0, 1, 4, 5).reshape(kinds, levels, parts * rows, width)


def summed_over_scen(grad):
    parts = lax.axis_size("scen")
    kinds, levels, ny, width = grad.shape
    if parts % 2:
        split = grad.reshape(kinds, levels, parts, ny // parts, width)
        return lax.all_to_all(split, "scen", 2, 2, tiled=True).sum(axis=2)
    me = lax.axis_index("scen")
    core = me % 2
    chip = me // 2
    chips = parts // 2
    split = grad.reshape(kinds, levels, chips, 2, ny // parts, width)
    mine = lax.dynamic_index_in_dim(split, core, axis=3, keepdims=False)
    other = lax.dynamic_index_in_dim(split, 1 - core, axis=3, keepdims=False)
    pair = lax.ppermute(other, "scen", [(q, q ^ 1) for q in range(parts)])
    chip_sum = mine + pair
    total = lax.dynamic_index_in_dim(chip_sum, chip, axis=2, keepdims=False)
    for step in range(1, chips):
        send = lax.dynamic_index_in_dim(chip_sum, (chip + step) % chips, axis=2, keepdims=False)
        total = total + lax.ppermute(
            send, "scen", [(q, ((q // 2 + step) % chips) * 2 + q % 2) for q in range(parts)]
        )
    return total


def solution(mesh):
    placed = (
        P("scen", None, None, None, "space"),
        P(None, None, "scen", "space"),
        P(None, "space"),
        P(None, "space"),
        P("scen", None, None, None, "space"),
    )
    return jax.shard_map(
        on_device,
        mesh=mesh,
        in_specs=placed,
        out_specs=(
            P("scen", None, None, None, "space"),
            P("scen", None, None, None, "space"),
            P(None, None, "scen", "space"),
        ),
        check_vma=False,
    )
```

```python
import jax
import jax.numpy as jnp
from jax import lax
from jax.experimental import pallas as pl
from jax.experimental.pallas import tpu as pltpu
from jax.sharding import PartitionSpec as P

STEPS = 2
HALO = 2

vertical_rate = 0.1
thaw_rate = 0.3

INTERPRET = False


def shifted(x, perm):
    return lax.ppermute(x, "space", perm)


def picker(size, positions):
    where = lax.broadcasted_iota(jnp.int32, (size, len(positions)), 0)
    slot = lax.broadcasted_iota(jnp.int32, (size, len(positions)), 1)
    hit = jnp.zeros((size, len(positions)), jnp.bool_)
    for p, at in enumerate(positions):
        hit = hit | ((slot == p) & (where == at))
    return hit.astype(jnp.float32)


def contract(a, b, dims):
    return lax.dot_general(
        a, b, (dims, ((), ())), precision=lax.Precision.HIGHEST, preferred_element_type=jnp.float32
    )


def placed(values, place):
    hi = lax.reduce_precision(values, exponent_bits=8, mantissa_bits=7)
    rest = values - hi
    mid = lax.reduce_precision(rest, exponent_bits=8, mantissa_bits=7)
    parts = jnp.concatenate([hi, mid, rest - mid])
    return lax.dot_general(
        parts, jnp.concatenate([place] * 3), (((0,), (0,)), ((), ())), preferred_element_type=jnp.float32
    )


def extended(fields, lanes, rows):
    n = lax.axis_size("space")
    count, ny, width = fields.shape
    spare = lanes - width
    flat = fields.reshape(count * ny, width)
    edges = contract(picker(width, [width - 2, width - 1, 0, 1]), flat, ((0,), (1,)))
    west = shifted(edges[0:2], [(q, (q + 1) % n) for q in range(n)])
    east = shifted(edges[2:4], [(q, (q - 1) % n) for q in range(n)])
    mirrored = fields[:, ny - 1:ny - 3:-1, ::-1]
    ghost = shifted(mirrored, [(q, n - 1 - q) for q in range(n)])
    top_edges = edges.reshape(4, count, ny)[:, :, ny - 1:ny - 3:-1]
    ghost_east = shifted(top_edges[1::-1], [(q, (n - 2 - q) % n) for q in range(n)])
    ghost_west = shifted(top_edges[3:1:-1], [(q, (n - q) % n) for q in range(n)])
    place = picker(spare, [0, 1, spare - 2, spare - 1]).T
    side = placed(jnp.concatenate([east, west]), place).reshape(count, ny, spare)
    ghost_halo = jnp.concatenate([ghost_east, ghost_west]).reshape(4, count * 2)
    ghost_side = placed(ghost_halo, place).reshape(count, 2, spare)
    top = jnp.concatenate([fields, side], axis=-1)
    folded = jnp.concatenate([ghost, ghost_side], axis=-1)
    pad = jnp.zeros((count, rows - ny - 2, lanes), fields.dtype)
    return jnp.concatenate([top, folded, pad], axis=1)


def roll(x, shift, axis):
    return pltpu.roll(x, shift % x.shape[axis], axis)


class Planes:
    def __init__(self, ref, start, levels):
        self.ref = ref
        self.start = start
        self.levels = levels

    def __getitem__(self, index):
        c, k = index
        return self.ref[self.start + c * self.levels + k]


def diffusion_kernel(
    x_ref,
    fin_ref, adj_ref, grad_ref,
    wet_ref, ce_ref, cn_ref, cz_ref, src_ref, gem_ref, gnm_ref, u1_ref, a_ref, b_ref,
    du0e_ref, du0n_ref, du1e_ref, du1n_ref, dv1e_ref, dv1n_ref, dv2e_ref, dv2n_ref,
):
    levels, rows, lanes = wet_ref.shape
    chans, _, ny, width = fin_ref.shape
    row = lax.broadcasted_iota(jnp.int32, (rows, lanes), 0)
    lane = lax.broadcasted_iota(jnp.int32, (rows, lanes), 1)
    planes = chans * levels
    ue_ref = Planes(x_ref, 0, levels)
    ve_ref = Planes(x_ref, planes, levels)
    ke_ref = Planes(x_ref, 2 * planes, levels)
    lev = x_ref[2 * planes + 2 * levels]
    shelf = x_ref[2 * planes + 2 * levels + 1]

    def wet_of(k):
        return (lev > k.astype(jnp.float32)).astype(jnp.float32)

    cz_ref[0] = jnp.zeros((rows, lanes), jnp.float32)

    def setup(k, carry):
        w = wet_of(k)
        w_next = jnp.where(k + 1 < levels, wet_of(k + 1), 0.0)
        w_east = roll(w, -1, 1)
        w_north = roll(w, -1, 0)
        ke = ke_ref[0, k]
        ke_sel = jnp.where(row >= ny, roll(ke, -1, 1), ke)
        east_mask = w * w_east
        ce_ref[k] = ke_sel * east_mask
        kn = ke_ref[1, k]
        kn_up = roll(kn, -1, 0)
        kn_sel = jnp.where(
            row < ny - 1, kn, jnp.where(row == ny - 1, 0.5 * (kn + kn_up), jnp.where(row == ny, kn_up, 0.0))
        )
        north_mask = w * w_north
        cn_ref[k] = kn_sel * north_mask
        cz_ref[k + 1] = vertical_rate * w * w_next
        src_ref[k] = thaw_rate * shelf * w * (1.0 - w_next)
        wet_ref[k] = w
        gem_ref[k] = east_mask[:ny, :width]
        gnm_ref[k] = jnp.where(row < ny - 1, north_mask, 0.5 * north_mask)[:ny, :width]
        for c in range(chans):
            a_ref[c, k] = w * ve_ref[c, k]
        return carry

    lax.fori_loop(0, levels, setup, 0, unroll=True)

    def operate(x_ref, c, k, diffs=None):
        x = x_ref[c, k]
        above = x_ref[c, jnp.minimum(k + 1, levels - 1)]
        below = x_ref[c, jnp.maximum(k - 1, 0)]
        d_east = roll(x, -1, 1) - x
        d_north = roll(x, -1, 0) - x
        if diffs is not None:
            diffs[0][c, k] = d_east[:ny, :width]
            diffs[1][c, k] = d_north[:ny, :width]
        east = ce_ref[k] * d_east
        north = cn_ref[k] * d_north
        change = (east - roll(east, 1, 1)) + (north - roll(north, 1, 0))
        change = change + (cz_ref[k + 1] * (above - x) - cz_ref[k] * (x - below))
        return x, change

    def forward_first(ck, carry):
        c = ck // levels
        k = ck % levels
        x, change = operate(ue_ref, c, k, (du0e_ref, du0n_ref))
        heat = jnp.where(c == 0, 1.0, 0.0)
        u1_ref[c, k] = wet_ref[k] * (x + change + heat * src_ref[k])
        return carry

    lax.fori_loop(0, planes, forward_first, 0, unroll=8)

    def forward_second(ck, carry):
        c = ck // levels
        k = ck % levels
        x, change = operate(u1_ref, c, k, (du1e_ref, du1n_ref))
        heat = jnp.where(c == 0, 1.0, 0.0)
        out = wet_ref[k] * (x + change + heat * src_ref[k])
        fin_ref[c, k] = out[:ny, :width]
        return carry

    lax.fori_loop(0, planes, forward_second, 0, unroll=8)

    def backward_second(ck, carry):
        c = ck // levels
        k = ck % levels
        x, change = operate(a_ref, c, k, (dv2e_ref, dv2n_ref))
        b_ref[c, k] = wet_ref[k] * (x + change)
        return carry

    lax.fori_loop(0, planes, backward_second, 0, unroll=8)

    def backward_first(ck, carry):
        c = ck // levels
        k = ck % levels
        x, change = operate(b_ref, c, k, (dv1e_ref, dv1n_ref))
        adj_ref[c, k] = (x + change)[:ny, :width]
        return carry

    lax.fori_loop(0, planes, backward_first, 0, unroll=8)

    def gradient(k, carry):
        g_east = jnp.zeros((ny, width), jnp.float32)
        g_north = jnp.zeros((ny, width), jnp.float32)
        for c in range(chans):
            g_east = g_east - du0e_ref[c, k] * dv1e_ref[c, k] - du1e_ref[c, k] * dv2e_ref[c, k]
            g_north = g_north - du0n_ref[c, k] * dv1n_ref[c, k] - du1n_ref[c, k] * dv2n_ref[c, k]
        grad_ref[0, k] = gem_ref[k] * g_east
        grad_ref[1, k] = gnm_ref[k] * g_north
        return carry

    lax.fori_loop(0, levels, gradient, 0, unroll=True)


def on_device(tracers, diffusivity, level_count, shelf_mask, cotangent):
    _, chans, levels, ny, width = tracers.shape
    lanes = width + 128
    rows = -(-(ny + 2) // 8) * 8
    full_kappa = gathered_over_scen(diffusivity)
    fields = jnp.concatenate(
        [
            tracers[0].reshape(chans * levels, ny, width),
            cotangent[0].reshape(chans * levels, ny, width),
            full_kappa.reshape(2 * levels, ny, width),
            level_count.astype(jnp.float32)[None],
            shelf_mask.astype(jnp.float32)[None],
        ]
    )
    ext = extended(fields, lanes, rows)
    field = jax.ShapeDtypeStruct((chans, levels, ny, width), jnp.float32)
    plane = pltpu.VMEM((levels, rows, lanes), jnp.float32)
    planes_c = pltpu.VMEM((chans, levels, rows, lanes), jnp.float32)
    diff = pltpu.VMEM((chans, levels, ny, width), jnp.float32)
    mask = pltpu.VMEM((levels, ny, width), jnp.float32)
    final, adjoint, grad = pl.pallas_call(
        diffusion_kernel,
        out_shape=(field, field, jax.ShapeDtypeStruct((2, levels, ny, width), jnp.float32)),
        scratch_shapes=[
            plane,
            plane,
            plane,
            pltpu.VMEM((levels + 1, rows, lanes), jnp.float32),
            plane,
            mask,
            mask,
            planes_c,
            planes_c,
            planes_c,
        ]
        + [diff] * 8,
        compiler_params=pltpu.CompilerParams(vmem_limit_bytes=48 * 1024 * 1024),
        interpret=INTERPRET,
    )(ext)
    kappa_grad = summed_over_scen(grad)
    return (final[None], adjoint[None], kappa_grad)


def gathered_over_scen(block):
    parts = lax.axis_size("scen")
    if parts % 2:
        return lax.all_gather(block, "scen", axis=2, tiled=True)
    kinds, levels, rows, width = block.shape
    me = lax.axis_index("scen")
    core = me % 2
    chip = me // 2
    chips = parts // 2
    got = [block]
    for step in range(1, chips):
        got.append(
            lax.ppermute(block, "scen", [(q, ((q // 2 + step) % chips) * 2 + q % 2) for q in range(parts)])
        )
    same = jnp.stack(got)
    other = lax.ppermute(same, "scen", [(q, q ^ 1) for q in range(parts)])
    by_core = jnp.where(core == 0, jnp.stack([same, other], axis=1), jnp.stack([other, same], axis=1))
    order = (chip - jnp.arange(chips)) % chips
    by_chip = jnp.take(by_core, order, axis=0)
    return by_chip.transpose(2, 3, 0, 1, 4, 5).reshape(kinds, levels, parts * rows, width)


def summed_over_scen(grad):
    parts = lax.axis_size("scen")
    kinds, levels, ny, width = grad.shape
    if parts % 2:
        split = grad.reshape(kinds, levels, parts, ny // parts, width)
        return lax.all_to_all(split, "scen", 2, 2, tiled=True).sum(axis=2)
    me = lax.axis_index("scen")
    core = me % 2
    chip = me // 2
    chips = parts // 2
    split = grad.reshape(kinds, levels, chips, 2, ny // parts, width)
    mine = lax.dynamic_index_in_dim(split, core, axis=3, keepdims=False)
    other = lax.dynamic_index_in_dim(split, 1 - core, axis=3, keepdims=False)
    pair = lax.ppermute(other, "scen", [(q, q ^ 1) for q in range(parts)])
    chip_sum = mine + pair
    total = lax.dynamic_index_in_dim(chip_sum, chip, axis=2, keepdims=False)
    for step in range(1, chips):
        send = lax.dynamic_index_in_dim(chip_sum, (chip + step) % chips, axis=2, keepdims=False)
        total = total + lax.ppermute(
            send, "scen", [(q, ((q // 2 + step) % chips) * 2 + q % 2) for q in range(parts)]
        )
    return total


def solution(mesh):
    placed = (
        P("scen", None, None, None, "space"),
        P(None, None, "scen", "space"),
        P(None, "space"),
        P(None, "space"),
        P("scen", None, None, None, "space"),
    )
    return jax.shard_map(
        on_device,
        mesh=mesh,
        in_specs=placed,
        out_specs=(
            P("scen", None, None, None, "space"),
            P("scen", None, None, None, "space"),
            P(None, None, "scen", "space"),
        ),
        check_vma=False,
    )
```

```python
import jax
import jax.numpy as jnp
from jax import lax
from jax.experimental import pallas as pl
from jax.experimental.pallas import tpu as pltpu
from jax.sharding import PartitionSpec as P

STEPS = 2
HALO = 2

vertical_rate = 0.1
thaw_rate = 0.3

INTERPRET = False


def shifted(x, perm):
    return lax.ppermute(x, "space", perm)


def picker(size, positions):
    where = lax.broadcasted_iota(jnp.int32, (size, len(positions)), 0)
    slot = lax.broadcasted_iota(jnp.int32, (size, len(positions)), 1)
    hit = jnp.zeros((size, len(positions)), jnp.bool_)
    for p, at in enumerate(positions):
        hit = hit | ((slot == p) & (where == at))
    return hit.astype(jnp.float32)


def contract(a, b, dims):
    return lax.dot_general(
        a, b, (dims, ((), ())), precision=lax.Precision.HIGHEST, preferred_element_type=jnp.float32
    )


def mirrored_rows(fields):
    ny = fields.shape[1]
    n = lax.axis_size("space")
    return shifted(fields[:, ny - 1:ny - 3:-1, ::-1], [(q, n - 1 - q) for q in range(n)])


def extended(fields, lanes, rows, ghost):
    n = lax.axis_size("space")
    count, ny, width = fields.shape
    spare = lanes - width
    flat = fields.reshape(count * ny, width)
    edges = contract(picker(width, [width - 2, width - 1, 0, 1]), flat, ((0,), (1,)))
    west = shifted(edges[0:2], [(q, (q + 1) % n) for q in range(n)])
    east = shifted(edges[2:4], [(q, (q - 1) % n) for q in range(n)])
    top_edges = edges.reshape(4, count, ny)[:, :, ny - 1:ny - 3:-1]
    ghost_east = shifted(top_edges[1::-1], [(q, (n - 2 - q) % n) for q in range(n)])
    ghost_west = shifted(top_edges[3:1:-1], [(q, (n - q) % n) for q in range(n)])
    place = picker(spare, [0, 1, spare - 2, spare - 1]).T
    side = contract(jnp.concatenate([east, west]), place, ((0,), (0,))).reshape(count, ny, spare)
    ghost_halo = jnp.concatenate([ghost_east, ghost_west]).reshape(4, count * 2)
    ghost_side = contract(ghost_halo, place, ((0,), (0,))).reshape(count, 2, spare)
    top = jnp.concatenate([fields, side], axis=-1)
    folded = jnp.concatenate([ghost, ghost_side], axis=-1)
    pad = jnp.zeros((count, rows - ny - 2, lanes), fields.dtype)
    return jnp.concatenate([top, folded, pad], axis=1)


def roll(x, shift, axis):
    return pltpu.roll(x, shift % x.shape[axis], axis)


class Planes:
    def __init__(self, ref, start, levels):
        self.ref = ref
        self.start = start
        self.levels = levels

    def __getitem__(self, index):
        c, k = index
        return self.ref[self.start + c * self.levels + k]


def diffusion_kernel(
    x_ref,
    fin_ref, adj_ref, grad_ref,
    wet_ref, ce_ref, cn_ref, cz_ref, src_ref, gem_ref, gnm_ref, u1_ref, a_ref, b_ref,
    du0e_ref, du0n_ref, du1e_ref, du1n_ref, dv1e_ref, dv1n_ref, dv2e_ref, dv2n_ref,
):
    levels, rows, lanes = wet_ref.shape
    chans, _, ny, width = fin_ref.shape
    row = lax.broadcasted_iota(jnp.int32, (rows, lanes), 0)
    lane = lax.broadcasted_iota(jnp.int32, (rows, lanes), 1)
    planes = chans * levels
    ue_ref = Planes(x_ref, 0, levels)
    ve_ref = Planes(x_ref, planes, levels)
    ke_ref = Planes(x_ref, 2 * planes, levels)
    lev = x_ref[2 * planes + 2 * levels]
    shelf = x_ref[2 * planes + 2 * levels + 1]

    def wet_of(k):
        return (lev > k.astype(jnp.float32)).astype(jnp.float32)

    cz_ref[0] = jnp.zeros((rows, lanes), jnp.float32)

    def setup(k, carry):
        w = wet_of(k)
        w_next = jnp.where(k + 1 < levels, wet_of(k + 1), 0.0)
        w_east = roll(w, -1, 1)
        w_north = roll(w, -1, 0)
        ke = ke_ref[0, k]
        ke_sel = jnp.where(row >= ny, roll(ke, -1, 1), ke)
        east_mask = w * w_east
        ce_ref[k] = ke_sel * east_mask
        kn = ke_ref[1, k]
        kn_up = roll(kn, -1, 0)
        kn_sel = jnp.where(
            row < ny - 1, kn, jnp.where(row == ny - 1, 0.5 * (kn + kn_up), jnp.where(row == ny, kn_up, 0.0))
        )
        north_mask = w * w_north
        cn_ref[k] = kn_sel * north_mask
        cz_ref[k + 1] = vertical_rate * w * w_next
        src_ref[k] = thaw_rate * shelf * w * (1.0 - w_next)
        wet_ref[k] = w
        gem_ref[k] = east_mask[:ny, :width]
        gnm_ref[k] = jnp.where(row < ny - 1, north_mask, 0.5 * north_mask)[:ny, :width]
        for c in range(chans):
            a_ref[c, k] = w * ve_ref[c, k]
        return carry

    lax.fori_loop(0, levels, setup, 0, unroll=True)

    def operate(x_ref, c, k, diffs=None):
        x = x_ref[c, k]
        above = x_ref[c, jnp.minimum(k + 1, levels - 1)]
        below = x_ref[c, jnp.maximum(k - 1, 0)]
        d_east = roll(x, -1, 1) - x
        d_north = roll(x, -1, 0) - x
        if diffs is not None:
            diffs[0][c, k] = d_east[:ny, :width]
            diffs[1][c, k] = d_north[:ny, :width]
        east = ce_ref[k] * d_east
        north = cn_ref[k] * d_north
        change = (east - roll(east, 1, 1)) + (north - roll(north, 1, 0))
        change = change + (cz_ref[k + 1] * (above - x) - cz_ref[k] * (x - below))
        return x, change

    def forward_first(ck, carry):
        c = ck // levels
        k = ck % levels
        x, change = operate(ue_ref, c, k, (du0e_ref, du0n_ref))
        heat = jnp.where(c == 0, 1.0, 0.0)
        u1_ref[c, k] = wet_ref[k] * (x + change + heat * src_ref[k])
        return carry

    lax.fori_loop(0, planes, forward_first, 0, unroll=8)

    def forward_second(ck, carry):
        c = ck // levels
        k = ck % levels
        x, change = operate(u1_ref, c, k, (du1e_ref, du1n_ref))
        heat = jnp.where(c == 0, 1.0, 0.0)
        out = wet_ref[k] * (x + change + heat * src_ref[k])
        fin_ref[c, k] = out[:ny, :width]
        return carry

    lax.fori_loop(0, planes, forward_second, 0, unroll=8)

    def backward_second(ck, carry):
        c = ck // levels
        k = ck % levels
        x, change = operate(a_ref, c, k, (dv2e_ref, dv2n_ref))
        b_ref[c, k] = wet_ref[k] * (x + change)
        return carry

    lax.fori_loop(0, planes, backward_second, 0, unroll=8)

    def backward_first(ck, carry):
        c = ck // levels
        k = ck % levels
        x, change = operate(b_ref, c, k, (dv1e_ref, dv1n_ref))
        adj_ref[c, k] = (x + change)[:ny, :width]
        return carry

    lax.fori_loop(0, planes, backward_first, 0, unroll=8)

    def gradient(k, carry):
        g_east = jnp.zeros((ny, width), jnp.float32)
        g_north = jnp.zeros((ny, width), jnp.float32)
        for c in range(chans):
            g_east = g_east - du0e_ref[c, k] * dv1e_ref[c, k] - du1e_ref[c, k] * dv2e_ref[c, k]
            g_north = g_north - du0n_ref[c, k] * dv1n_ref[c, k] - du1n_ref[c, k] * dv2n_ref[c, k]
        grad_ref[0, k] = gem_ref[k] * g_east
        grad_ref[1, k] = gnm_ref[k] * g_north
        return carry

    lax.fori_loop(0, levels, gradient, 0, unroll=True)


def on_device(tracers, diffusivity, level_count, shelf_mask, cotangent):
    _, chans, levels, ny, width = tracers.shape
    lanes = width + 128
    rows = -(-(ny + 2) // 8) * 8
    early = jnp.concatenate(
        [
            tracers[0].reshape(chans * levels, ny, width),
            cotangent[0].reshape(chans * levels, ny, width),
        ]
    )
    early_ghost = mirrored_rows(early)
    full_kappa = gathered_over_scen(diffusivity)
    late = jnp.concatenate(
        [
            full_kappa.reshape(2 * levels, ny, width),
            level_count.astype(jnp.float32)[None],
            shelf_mask.astype(jnp.float32)[None],
        ]
    )
    ghost = jnp.concatenate([early_ghost, mirrored_rows(late)])
    ext = extended(jnp.concatenate([early, late]), lanes, rows, ghost)
    field = jax.ShapeDtypeStruct((chans, levels, ny, width), jnp.float32)
    plane = pltpu.VMEM((levels, rows, lanes), jnp.float32)
    planes_c = pltpu.VMEM((chans, levels, rows, lanes), jnp.float32)
    diff = pltpu.VMEM((chans, levels, ny, width), jnp.float32)
    mask = pltpu.VMEM((levels, ny, width), jnp.float32)
    final, adjoint, grad = pl.pallas_call(
        diffusion_kernel,
        out_shape=(field, field, jax.ShapeDtypeStruct((2, levels, ny, width), jnp.float32)),
        scratch_shapes=[
            plane,
            plane,
            plane,
            pltpu.VMEM((levels + 1, rows, lanes), jnp.float32),
            plane,
            mask,
            mask,
            planes_c,
            planes_c,
            planes_c,
        ]
        + [diff] * 8,
        compiler_params=pltpu.CompilerParams(vmem_limit_bytes=48 * 1024 * 1024),
        interpret=INTERPRET,
    )(ext)
    kappa_grad = summed_over_scen(grad)
    return (final[None], adjoint[None], kappa_grad)


def gathered_over_scen(block):
    parts = lax.axis_size("scen")
    if parts % 2:
        return lax.all_gather(block, "scen", axis=2, tiled=True)
    kinds, levels, rows, width = block.shape
    me = lax.axis_index("scen")
    core = me % 2
    chip = me // 2
    chips = parts // 2
    got = [block]
    for step in range(1, chips):
        got.append(
            lax.ppermute(block, "scen", [(q, ((q // 2 + step) % chips) * 2 + q % 2) for q in range(parts)])
        )
    same = jnp.stack(got)
    other = lax.ppermute(same, "scen", [(q, q ^ 1) for q in range(parts)])
    by_core = jnp.where(core == 0, jnp.stack([same, other], axis=1), jnp.stack([other, same], axis=1))
    order = (chip - jnp.arange(chips)) % chips
    by_chip = jnp.take(by_core, order, axis=0)
    return by_chip.transpose(2, 3, 0, 1, 4, 5).reshape(kinds, levels, parts * rows, width)


def summed_over_scen(grad):
    parts = lax.axis_size("scen")
    kinds, levels, ny, width = grad.shape
    if parts % 2:
        split = grad.reshape(kinds, levels, parts, ny // parts, width)
        return lax.all_to_all(split, "scen", 2, 2, tiled=True).sum(axis=2)
    me = lax.axis_index("scen")
    core = me % 2
    chip = me // 2
    chips = parts // 2
    split = grad.reshape(kinds, levels, chips, 2, ny // parts, width)
    mine = lax.dynamic_index_in_dim(split, core, axis=3, keepdims=False)
    other = lax.dynamic_index_in_dim(split, 1 - core, axis=3, keepdims=False)
    pair = lax.ppermute(other, "scen", [(q, q ^ 1) for q in range(parts)])
    chip_sum = mine + pair
    total = lax.dynamic_index_in_dim(chip_sum, chip, axis=2, keepdims=False)
    for step in range(1, chips):
        send = lax.dynamic_index_in_dim(chip_sum, (chip + step) % chips, axis=2, keepdims=False)
        total = total + lax.ppermute(
            send, "scen", [(q, ((q // 2 + step) % chips) * 2 + q % 2) for q in range(parts)]
        )
    return total


def solution(mesh):
    placed = (
        P("scen", None, None, None, "space"),
        P(None, None, "scen", "space"),
        P(None, "space"),
        P(None, "space"),
        P("scen", None, None, None, "space"),
    )
    return jax.shard_map(
        on_device,
        mesh=mesh,
        in_specs=placed,
        out_specs=(
            P("scen", None, None, None, "space"),
            P("scen", None, None, None, "space"),
            P(None, None, "scen", "space"),
        ),
        check_vma=False,
    )
```

```python
import functools

import jax
import jax.numpy as jnp
from jax import lax
from jax.experimental import pallas as pl
from jax.experimental.pallas import tpu as pltpu
from jax.sharding import PartitionSpec as P

STEPS = 2
HALO = 2

vertical_rate = 0.1
thaw_rate = 0.3

INTERPRET = False


def shifted(x, perm):
    return lax.ppermute(x, "space", perm)


def picker(size, positions):
    where = lax.broadcasted_iota(jnp.int32, (size, len(positions)), 0)
    slot = lax.broadcasted_iota(jnp.int32, (size, len(positions)), 1)
    hit = jnp.zeros((size, len(positions)), jnp.bool_)
    for p, at in enumerate(positions):
        hit = hit | ((slot == p) & (where == at))
    return hit.astype(jnp.float32)


def contract(a, b, dims):
    return lax.dot_general(
        a, b, (dims, ((), ())), precision=lax.Precision.HIGHEST, preferred_element_type=jnp.float32
    )


def extended(fields, lanes, rows):
    n = lax.axis_size("space")
    count, ny, width = fields.shape
    spare = lanes - width
    flat = fields.reshape(count * ny, width)
    edges = contract(picker(width, [width - 2, width - 1, 0, 1]), flat, ((0,), (1,)))
    west = shifted(edges[0:2], [(q, (q + 1) % n) for q in range(n)])
    east = shifted(edges[2:4], [(q, (q - 1) % n) for q in range(n)])
    mirrored = fields[:, ny - 1:ny - 3:-1, ::-1]
    ghost = shifted(mirrored, [(q, n - 1 - q) for q in range(n)])
    top_edges = edges.reshape(4, count, ny)[:, :, ny - 1:ny - 3:-1]
    ghost_east = shifted(top_edges[1::-1], [(q, (n - 2 - q) % n) for q in range(n)])
    ghost_west = shifted(top_edges[3:1:-1], [(q, (n - q) % n) for q in range(n)])
    place = picker(spare, [0, 1, spare - 2, spare - 1]).T
    side = contract(jnp.concatenate([east, west]), place, ((0,), (0,))).reshape(count, ny, spare)
    ghost_halo = jnp.concatenate([ghost_east, ghost_west]).reshape(4, count * 2)
    ghost_side = contract(ghost_halo, place, ((0,), (0,))).reshape(count, 2, spare)
    top = jnp.concatenate([fields, side], axis=-1)
    folded = jnp.concatenate([ghost, ghost_side], axis=-1)
    pad = jnp.zeros((count, rows - ny - 2, lanes), fields.dtype)
    return jnp.concatenate([top, folded, pad], axis=1)


def roll(x, shift, axis):
    return pltpu.roll(x, shift % x.shape[axis], axis)


class Planes:
    def __init__(self, ref, start, levels):
        self.ref = ref
        self.start = start
        self.levels = levels

    def __getitem__(self, index):
        c, k = index
        return self.ref[self.start + c * self.levels + k]


def diffusion_kernel(
    x_ref,
    fin_ref, adj_ref, grad_ref,
    wet_ref, ce_ref, cn_ref, cz_ref, src_ref, gem_ref, gnm_ref, u1_ref, a_ref, b_ref,
    du0e_ref, du0n_ref, du1e_ref, du1n_ref, dv1e_ref, dv1n_ref, dv2e_ref, dv2n_ref,
):
    levels, rows, lanes = wet_ref.shape
    chans, _, ny, width = fin_ref.shape
    row = lax.broadcasted_iota(jnp.int32, (rows, lanes), 0)
    lane = lax.broadcasted_iota(jnp.int32, (rows, lanes), 1)
    planes = chans * levels
    ue_ref = Planes(x_ref, 0, levels)
    ve_ref = Planes(x_ref, planes, levels)
    ke_ref = Planes(x_ref, 2 * planes, levels)
    lev = x_ref[2 * planes + 2 * levels]
    shelf = x_ref[2 * planes + 2 * levels + 1]

    def wet_of(k):
        return (lev > k.astype(jnp.float32)).astype(jnp.float32)

    cz_ref[0] = jnp.zeros((rows, lanes), jnp.float32)

    def setup(k, carry):
        w = wet_of(k)
        w_next = jnp.where(k + 1 < levels, wet_of(k + 1), 0.0)
        w_east = roll(w, -1, 1)
        w_north = roll(w, -1, 0)
        ke = ke_ref[0, k]
        ke_sel = jnp.where(row >= ny, roll(ke, -1, 1), ke)
        east_mask = w * w_east
        ce_ref[k] = ke_sel * east_mask
        kn = ke_ref[1, k]
        kn_up = roll(kn, -1, 0)
        kn_sel = jnp.where(
            row < ny - 1, kn, jnp.where(row == ny - 1, 0.5 * (kn + kn_up), jnp.where(row == ny, kn_up, 0.0))
        )
        north_mask = w * w_north
        cn_ref[k] = kn_sel * north_mask
        cz_ref[k + 1] = vertical_rate * w * w_next
        src_ref[k] = thaw_rate * shelf * w * (1.0 - w_next)
        wet_ref[k] = w
        gem_ref[k] = east_mask[:ny, :width]
        gnm_ref[k] = jnp.where(row < ny - 1, north_mask, 0.5 * north_mask)[:ny, :width]
        for c in range(chans):
            a_ref[c, k] = w * ve_ref[c, k]
        return carry

    lax.fori_loop(0, levels, setup, 0, unroll=True)

    def operate(x_ref, c, k, diffs=None):
        x = x_ref[c, k]
        above = x_ref[c, jnp.minimum(k + 1, levels - 1)]
        below = x_ref[c, jnp.maximum(k - 1, 0)]
        d_east = roll(x, -1, 1) - x
        d_north = roll(x, -1, 0) - x
        if diffs is not None:
            diffs[0][c, k] = d_east[:ny, :width]
            diffs[1][c, k] = d_north[:ny, :width]
        east = ce_ref[k] * d_east
        north = cn_ref[k] * d_north
        change = (east - roll(east, 1, 1)) + (north - roll(north, 1, 0))
        change = change + (cz_ref[k + 1] * (above - x) - cz_ref[k] * (x - below))
        return x, change

    def forward_first(c, k, carry):
        x, change = operate(ue_ref, c, k, (du0e_ref, du0n_ref))
        if c == 0:
            change = change + src_ref[k]
        u1_ref[c, k] = wet_ref[k] * (x + change)
        return carry

    for c in range(chans):
        lax.fori_loop(0, levels, functools.partial(forward_first, c), 0, unroll=10)

    def forward_second(c, k, carry):
        x, change = operate(u1_ref, c, k, (du1e_ref, du1n_ref))
        if c == 0:
            change = change + src_ref[k]
        out = wet_ref[k] * (x + change)
        fin_ref[c, k] = out[:ny, :width]
        return carry

    for c in range(chans):
        lax.fori_loop(0, levels, functools.partial(forward_second, c), 0, unroll=10)

    def backward_second(c, k, carry):
        x, change = operate(a_ref, c, k, (dv2e_ref, dv2n_ref))
        b_ref[c, k] = wet_ref[k] * (x + change)
        return carry

    for c in range(chans):
        lax.fori_loop(0, levels, functools.partial(backward_second, c), 0, unroll=10)

    def backward_first(c, k, carry):
        x, change = operate(b_ref, c, k, (dv1e_ref, dv1n_ref))
        adj_ref[c, k] = (x + change)[:ny, :width]
        return carry

    for c in range(chans):
        lax.fori_loop(0, levels, functools.partial(backward_first, c), 0, unroll=10)

    def gradient(k, carry):
        g_east = jnp.zeros((ny, width), jnp.float32)
        g_north = jnp.zeros((ny, width), jnp.float32)
        for c in range(chans):
            g_east = g_east - du0e_ref[c, k] * dv1e_ref[c, k] - du1e_ref[c, k] * dv2e_ref[c, k]
            g_north = g_north - du0n_ref[c, k] * dv1n_ref[c, k] - du1n_ref[c, k] * dv2n_ref[c, k]
        grad_ref[0, k] = gem_ref[k] * g_east
        grad_ref[1, k] = gnm_ref[k] * g_north
        return carry

    lax.fori_loop(0, levels, gradient, 0, unroll=True)


def on_device(tracers, diffusivity, level_count, shelf_mask, cotangent):
    _, chans, levels, ny, width = tracers.shape
    lanes = width + 128
    rows = -(-(ny + 2) // 8) * 8
    full_kappa = gathered_over_scen(diffusivity)
    fields = jnp.concatenate(
        [
            tracers[0].reshape(chans * levels, ny, width),
            cotangent[0].reshape(chans * levels, ny, width),
            full_kappa.reshape(2 * levels, ny, width),
            level_count.astype(jnp.float32)[None],
            shelf_mask.astype(jnp.float32)[None],
        ]
    )
    ext = extended(fields, lanes, rows)
    field = jax.ShapeDtypeStruct((chans, levels, ny, width), jnp.float32)
    plane = pltpu.VMEM((levels, rows, lanes), jnp.float32)
    planes_c = pltpu.VMEM((chans, levels, rows, lanes), jnp.float32)
    diff = pltpu.VMEM((chans, levels, ny, width), jnp.float32)
    mask = pltpu.VMEM((levels, ny, width), jnp.float32)
    final, adjoint, grad = pl.pallas_call(
        diffusion_kernel,
        out_shape=(field, field, jax.ShapeDtypeStruct((2, levels, ny, width), jnp.float32)),
        scratch_shapes=[
            plane,
            plane,
            plane,
            pltpu.VMEM((levels + 1, rows, lanes), jnp.float32),
            plane,
            mask,
            mask,
            planes_c,
            planes_c,
            planes_c,
        ]
        + [diff] * 8,
        compiler_params=pltpu.CompilerParams(vmem_limit_bytes=48 * 1024 * 1024),
        interpret=INTERPRET,
    )(ext)
    kappa_grad = summed_over_scen(grad)
    return (final[None], adjoint[None], kappa_grad)


def gathered_over_scen(block):
    parts = lax.axis_size("scen")
    if parts % 2:
        return lax.all_gather(block, "scen", axis=2, tiled=True)
    kinds, levels, rows, width = block.shape
    me = lax.axis_index("scen")
    core = me % 2
    chip = me // 2
    chips = parts // 2
    got = [block]
    for step in range(1, chips):
        got.append(
            lax.ppermute(block, "scen", [(q, ((q // 2 + step) % chips) * 2 + q % 2) for q in range(parts)])
        )
    same = jnp.stack(got)
    other = lax.ppermute(same, "scen", [(q, q ^ 1) for q in range(parts)])
    by_core = jnp.where(core == 0, jnp.stack([same, other], axis=1), jnp.stack([other, same], axis=1))
    order = (chip - jnp.arange(chips)) % chips
    by_chip = jnp.take(by_core, order, axis=0)
    return by_chip.transpose(2, 3, 0, 1, 4, 5).reshape(kinds, levels, parts * rows, width)


def summed_over_scen(grad):
    parts = lax.axis_size("scen")
    kinds, levels, ny, width = grad.shape
    if parts % 2:
        split = grad.reshape(kinds, levels, parts, ny // parts, width)
        return lax.all_to_all(split, "scen", 2, 2, tiled=True).sum(axis=2)
    me = lax.axis_index("scen")
    core = me % 2
    chip = me // 2
    chips = parts // 2
    split = grad.reshape(kinds, levels, chips, 2, ny // parts, width)
    mine = lax.dynamic_index_in_dim(split, core, axis=3, keepdims=False)
    other = lax.dynamic_index_in_dim(split, 1 - core, axis=3, keepdims=False)
    pair = lax.ppermute(other, "scen", [(q, q ^ 1) for q in range(parts)])
    chip_sum = mine + pair
    total = lax.dynamic_index_in_dim(chip_sum, chip, axis=2, keepdims=False)
    for step in range(1, chips):
        send = lax.dynamic_index_in_dim(chip_sum, (chip + step) % chips, axis=2, keepdims=False)
        total = total + lax.ppermute(
            send, "scen", [(q, ((q // 2 + step) % chips) * 2 + q % 2) for q in range(parts)]
        )
    return total


def solution(mesh):
    placed = (
        P("scen", None, None, None, "space"),
        P(None, None, "scen", "space"),
        P(None, "space"),
        P(None, "space"),
        P("scen", None, None, None, "space"),
    )
    return jax.shard_map(
        on_device,
        mesh=mesh,
        in_specs=placed,
        out_specs=(
            P("scen", None, None, None, "space"),
            P("scen", None, None, None, "space"),
            P(None, None, "scen", "space"),
        ),
        check_vma=False,
    )
```

```python
import jax
import jax.numpy as jnp
from jax import lax
from jax.experimental import pallas as pl
from jax.experimental.pallas import tpu as pltpu
from jax.sharding import PartitionSpec as P

STEPS = 2
HALO = 2

vertical_rate = 0.1
thaw_rate = 0.3

INTERPRET = False


def shifted(x, perm):
    return lax.ppermute(x, "space", perm)


def picker(size, positions):
    where = lax.broadcasted_iota(jnp.int32, (size, len(positions)), 0)
    slot = lax.broadcasted_iota(jnp.int32, (size, len(positions)), 1)
    hit = jnp.zeros((size, len(positions)), jnp.bool_)
    for p, at in enumerate(positions):
        hit = hit | ((slot == p) & (where == at))
    return hit.astype(jnp.float32)


def contract(a, b, dims):
    return lax.dot_general(
        a, b, (dims, ((), ())), precision=lax.Precision.HIGHEST, preferred_element_type=jnp.float32
    )


def extended(fields, lanes, rows):
    n = lax.axis_size("space")
    count, ny, width = fields.shape
    spare = lanes - width
    flat = fields.reshape(count * ny, width)
    edges = contract(picker(width, [width - 2, width - 1, 0, 1]), flat, ((0,), (1,)))
    west = shifted(edges[0:2], [(q, (q + 1) % n) for q in range(n)])
    east = shifted(edges[2:4], [(q, (q - 1) % n) for q in range(n)])
    mirrored = fields[:, ny - 1:ny - 3:-1, ::-1]
    ghost = shifted(mirrored, [(q, n - 1 - q) for q in range(n)])
    top_edges = edges.reshape(4, count, ny)[:, :, ny - 1:ny - 3:-1]
    ghost_east = shifted(top_edges[1::-1], [(q, (n - 2 - q) % n) for q in range(n)])
    ghost_west = shifted(top_edges[3:1:-1], [(q, (n - q) % n) for q in range(n)])
    place = picker(spare, [0, 1, spare - 2, spare - 1]).T
    side = contract(jnp.concatenate([east, west]), place, ((0,), (0,))).reshape(count, ny, spare)
    ghost_halo = jnp.concatenate([ghost_east, ghost_west]).reshape(4, count * 2)
    ghost_side = contract(ghost_halo, place, ((0,), (0,))).reshape(count, 2, spare)
    top = jnp.concatenate([fields, side], axis=-1)
    folded = jnp.concatenate([ghost, ghost_side], axis=-1)
    pad = jnp.zeros((count, rows - ny - 2, lanes), fields.dtype)
    return jnp.concatenate([top, folded, pad], axis=1)


def roll(x, shift, axis):
    return pltpu.roll(x, shift % x.shape[axis], axis)


class Planes:
    def __init__(self, ref, start, levels):
        self.ref = ref
        self.start = start
        self.levels = levels

    def __getitem__(self, index):
        c, k = index
        return self.ref[self.start + c * self.levels + k]


def diffusion_kernel(
    x_ref,
    fin_ref, adj_ref, grad_ref,
    wet_ref, ce_ref, cn_ref, cz_ref, src_ref, gem_ref, gnm_ref, u1_ref, a_ref, b_ref,
    du0e_ref, du0n_ref, du1e_ref, du1n_ref, dv1e_ref, dv1n_ref, dv2e_ref, dv2n_ref,
):
    levels, rows, lanes = wet_ref.shape
    chans, _, ny, width = fin_ref.shape
    row = lax.broadcasted_iota(jnp.int32, (rows, lanes), 0)
    lane = lax.broadcasted_iota(jnp.int32, (rows, lanes), 1)
    planes = chans * levels
    ue_ref = Planes(x_ref, 0, levels)
    ve_ref = Planes(x_ref, planes, levels)
    ke_ref = Planes(x_ref, 2 * planes, levels)
    lev = x_ref[2 * planes + 2 * levels]
    shelf = x_ref[2 * planes + 2 * levels + 1]

    def wet_of(k):
        return (lev > k.astype(jnp.float32)).astype(jnp.float32)

    cz_ref[0] = jnp.zeros((rows, lanes), jnp.float32)

    def setup(k, carry):
        w = wet_of(k)
        w_next = jnp.where(k + 1 < levels, wet_of(k + 1), 0.0)
        w_east = roll(w, -1, 1)
        w_north = roll(w, -1, 0)
        ke = ke_ref[0, k]
        ke_sel = jnp.where(row >= ny, roll(ke, -1, 1), ke)
        east_mask = w * w_east
        ce_ref[k] = ke_sel * east_mask
        kn = ke_ref[1, k]
        kn_up = roll(kn, -1, 0)
        kn_sel = jnp.where(
            row < ny - 1, kn, jnp.where(row == ny - 1, 0.5 * (kn + kn_up), jnp.where(row == ny, kn_up, 0.0))
        )
        north_mask = w * w_north
        cn_ref[k] = kn_sel * north_mask
        cz_ref[k + 1] = vertical_rate * w * w_next
        src_ref[k] = thaw_rate * shelf * w * (1.0 - w_next)
        wet_ref[k] = w
        gem_ref[k] = east_mask[:ny, :width]
        gnm_ref[k] = jnp.where(row < ny - 1, north_mask, 0.5 * north_mask)[:ny, :width]
        for c in range(chans):
            a_ref[c, k] = w * ve_ref[c, k]
        return carry

    lax.fori_loop(0, levels, setup, 0, unroll=True)

    def operate(x_ref, c, k, diffs=None):
        x = x_ref[c, k]
        above = x_ref[c, jnp.minimum(k + 1, levels - 1)]
        below = x_ref[c, jnp.maximum(k - 1, 0)]
        d_east = roll(x, -1, 1) - x
        d_north = roll(x, -1, 0) - x
        if diffs is not None:
            diffs[0][c, k] = d_east[:ny, :width]
            diffs[1][c, k] = d_north[:ny, :width]
        east = ce_ref[k] * d_east
        north = cn_ref[k] * d_north
        change = (east - roll(east, 1, 1)) + (north - roll(north, 1, 0))
        change = change + (cz_ref[k + 1] * (above - x) - cz_ref[k] * (x - below))
        return x, change

    def forward_first(ck, carry):
        c = ck // levels
        k = ck % levels
        x, change = operate(ue_ref, c, k, (du0e_ref, du0n_ref))
        heat = jnp.where(c == 0, 1.0, 0.0)
        u1_ref[c, k] = wet_ref[k] * (x + change + heat * src_ref[k])
        return carry


    def forward_second(ck, carry):
        c = ck // levels
        k = ck % levels
        x, change = operate(u1_ref, c, k, (du1e_ref, du1n_ref))
        heat = jnp.where(c == 0, 1.0, 0.0)
        out = wet_ref[k] * (x + change + heat * src_ref[k])
        fin_ref[c, k] = out[:ny, :width]
        return carry


    def backward_second(ck, carry):
        c = ck // levels
        k = ck % levels
        x, change = operate(a_ref, c, k, (dv2e_ref, dv2n_ref))
        b_ref[c, k] = wet_ref[k] * (x + change)
        return carry

    def first_pair(ck, carry):
        forward_first(ck, carry)
        return backward_second(ck, carry)

    lax.fori_loop(0, planes, first_pair, 0, unroll=4)

    def backward_first(ck, carry):
        c = ck // levels
        k = ck % levels
        x, change = operate(b_ref, c, k, (dv1e_ref, dv1n_ref))
        adj_ref[c, k] = (x + change)[:ny, :width]
        return carry

    def second_pair(ck, carry):
        forward_second(ck, carry)
        return backward_first(ck, carry)

    lax.fori_loop(0, planes, second_pair, 0, unroll=4)

    def gradient(k, carry):
        g_east = jnp.zeros((ny, width), jnp.float32)
        g_north = jnp.zeros((ny, width), jnp.float32)
        for c in range(chans):
            g_east = g_east - du0e_ref[c, k] * dv1e_ref[c, k] - du1e_ref[c, k] * dv2e_ref[c, k]
            g_north = g_north - du0n_ref[c, k] * dv1n_ref[c, k] - du1n_ref[c, k] * dv2n_ref[c, k]
        grad_ref[0, k] = gem_ref[k] * g_east
        grad_ref[1, k] = gnm_ref[k] * g_north
        return carry

    lax.fori_loop(0, levels, gradient, 0, unroll=True)


def on_device(tracers, diffusivity, level_count, shelf_mask, cotangent):
    _, chans, levels, ny, width = tracers.shape
    lanes = width + 128
    rows = -(-(ny + 2) // 8) * 8
    full_kappa = gathered_over_scen(diffusivity)
    fields = jnp.concatenate(
        [
            tracers[0].reshape(chans * levels, ny, width),
            cotangent[0].reshape(chans * levels, ny, width),
            full_kappa.reshape(2 * levels, ny, width),
            level_count.astype(jnp.float32)[None],
            shelf_mask.astype(jnp.float32)[None],
        ]
    )
    ext = extended(fields, lanes, rows)
    field = jax.ShapeDtypeStruct((chans, levels, ny, width), jnp.float32)
    plane = pltpu.VMEM((levels, rows, lanes), jnp.float32)
    planes_c = pltpu.VMEM((chans, levels, rows, lanes), jnp.float32)
    diff = pltpu.VMEM((chans, levels, ny, width), jnp.float32)
    mask = pltpu.VMEM((levels, ny, width), jnp.float32)
    final, adjoint, grad = pl.pallas_call(
        diffusion_kernel,
        out_shape=(field, field, jax.ShapeDtypeStruct((2, levels, ny, width), jnp.float32)),
        scratch_shapes=[
            plane,
            plane,
            plane,
            pltpu.VMEM((levels + 1, rows, lanes), jnp.float32),
            plane,
            mask,
            mask,
            planes_c,
            planes_c,
            planes_c,
        ]
        + [diff] * 8,
        compiler_params=pltpu.CompilerParams(vmem_limit_bytes=48 * 1024 * 1024),
        interpret=INTERPRET,
    )(ext)
    kappa_grad = summed_over_scen(grad)
    return (final[None], adjoint[None], kappa_grad)


def gathered_over_scen(block):
    parts = lax.axis_size("scen")
    if parts % 2:
        return lax.all_gather(block, "scen", axis=2, tiled=True)
    kinds, levels, rows, width = block.shape
    me = lax.axis_index("scen")
    core = me % 2
    chip = me // 2
    chips = parts // 2
    got = [block]
    for step in range(1, chips):
        got.append(
            lax.ppermute(block, "scen", [(q, ((q // 2 + step) % chips) * 2 + q % 2) for q in range(parts)])
        )
    same = jnp.stack(got)
    other = lax.ppermute(same, "scen", [(q, q ^ 1) for q in range(parts)])
    by_core = jnp.where(core == 0, jnp.stack([same, other], axis=1), jnp.stack([other, same], axis=1))
    order = (chip - jnp.arange(chips)) % chips
    by_chip = jnp.take(by_core, order, axis=0)
    return by_chip.transpose(2, 3, 0, 1, 4, 5).reshape(kinds, levels, parts * rows, width)


def summed_over_scen(grad):
    parts = lax.axis_size("scen")
    kinds, levels, ny, width = grad.shape
    if parts % 2:
        split = grad.reshape(kinds, levels, parts, ny // parts, width)
        return lax.all_to_all(split, "scen", 2, 2, tiled=True).sum(axis=2)
    me = lax.axis_index("scen")
    core = me % 2
    chip = me // 2
    chips = parts // 2
    split = grad.reshape(kinds, levels, chips, 2, ny // parts, width)
    mine = lax.dynamic_index_in_dim(split, core, axis=3, keepdims=False)
    other = lax.dynamic_index_in_dim(split, 1 - core, axis=3, keepdims=False)
    pair = lax.ppermute(other, "scen", [(q, q ^ 1) for q in range(parts)])
    chip_sum = mine + pair
    total = lax.dynamic_index_in_dim(chip_sum, chip, axis=2, keepdims=False)
    for step in range(1, chips):
        send = lax.dynamic_index_in_dim(chip_sum, (chip + step) % chips, axis=2, keepdims=False)
        total = total + lax.ppermute(
            send, "scen", [(q, ((q // 2 + step) % chips) * 2 + q % 2) for q in range(parts)]
        )
    return total


def solution(mesh):
    placed = (
        P("scen", None, None, None, "space"),
        P(None, None, "scen", "space"),
        P(None, "space"),
        P(None, "space"),
        P("scen", None, None, None, "space"),
    )
    return jax.shard_map(
        on_device,
        mesh=mesh,
        in_specs=placed,
        out_specs=(
            P("scen", None, None, None, "space"),
            P("scen", None, None, None, "space"),
            P(None, None, "scen", "space"),
        ),
        check_vma=False,
    )
```

```python
import jax
import jax.numpy as jnp
from jax import lax
from jax.experimental import pallas as pl
from jax.experimental.pallas import tpu as pltpu
from jax.sharding import PartitionSpec as P

STEPS = 2
HALO = 2

vertical_rate = 0.1
thaw_rate = 0.3

INTERPRET = False


def shifted(x, perm):
    return lax.ppermute(x, "space", perm)


def picker(size, positions):
    where = lax.broadcasted_iota(jnp.int32, (size, len(positions)), 0)
    slot = lax.broadcasted_iota(jnp.int32, (size, len(positions)), 1)
    hit = jnp.zeros((size, len(positions)), jnp.bool_)
    for p, at in enumerate(positions):
        hit = hit | ((slot == p) & (where == at))
    return hit.astype(jnp.float32)


def contract(a, b, dims):
    return lax.dot_general(
        a, b, (dims, ((), ())), precision=lax.Precision.HIGHEST, preferred_element_type=jnp.float32
    )


def extended(fields, lanes, rows):
    n = lax.axis_size("space")
    count, ny, width = fields.shape
    spare = lanes - width
    flat = fields.reshape(count * ny, width)
    edges = contract(picker(width, [width - 2, width - 1, 0, 1]), flat, ((0,), (1,)))
    west = shifted(edges[0:2], [(q, (q + 1) % n) for q in range(n)])
    east = shifted(edges[2:4], [(q, (q - 1) % n) for q in range(n)])
    mirrored = fields[:, ny - 1:ny - 3:-1, ::-1]
    ghost = shifted(mirrored, [(q, n - 1 - q) for q in range(n)])
    top_edges = edges.reshape(4, count, ny)[:, :, ny - 1:ny - 3:-1]
    ghost_east = shifted(top_edges[1::-1], [(q, (n - 2 - q) % n) for q in range(n)])
    ghost_west = shifted(top_edges[3:1:-1], [(q, (n - q) % n) for q in range(n)])
    place = picker(spare, [0, 1, spare - 2, spare - 1]).T
    side = contract(jnp.concatenate([east, west]), place, ((0,), (0,))).reshape(count, ny, spare)
    ghost_halo = jnp.concatenate([ghost_east, ghost_west]).reshape(4, count * 2)
    ghost_side = contract(ghost_halo, place, ((0,), (0,))).reshape(count, 2, spare)
    top = jnp.concatenate([fields, side], axis=-1)
    folded = jnp.concatenate([ghost, ghost_side], axis=-1)
    pad = jnp.zeros((count, rows - ny - 2, lanes), fields.dtype)
    return jnp.concatenate([top, folded, pad], axis=1)


def roll(x, shift, axis):
    return pltpu.roll(x, shift % x.shape[axis], axis)


class Planes:
    def __init__(self, ref, start, levels):
        self.ref = ref
        self.start = start
        self.levels = levels

    def __getitem__(self, index):
        c, k = index
        return self.ref[self.start + c * self.levels + k]


def diffusion_kernel(
    x_ref,
    fin_ref, adj_ref, grad_ref,
    wet_ref, ce_ref, cn_ref, cz_ref, src_ref, gem_ref, gnm_ref, u1_ref, a_ref, b_ref,
    du0e_ref, du0n_ref, du1e_ref, du1n_ref, dv1e_ref, dv1n_ref, dv2e_ref, dv2n_ref,
):
    levels, rows, lanes = wet_ref.shape
    chans, _, ny, width = fin_ref.shape
    row = lax.broadcasted_iota(jnp.int32, (rows, lanes), 0)
    lane = lax.broadcasted_iota(jnp.int32, (rows, lanes), 1)
    planes = chans * levels
    ue_ref = Planes(x_ref, 0, levels)
    ve_ref = Planes(x_ref, planes, levels)
    ke_ref = Planes(x_ref, 2 * planes, levels)
    lev = x_ref[2 * planes + 2 * levels]
    shelf = x_ref[2 * planes + 2 * levels + 1]

    def wet_of(k):
        return (lev > k.astype(jnp.float32)).astype(jnp.float32)

    cz_ref[0] = jnp.zeros((rows, lanes), jnp.float32)

    def setup(k, carry):
        w = wet_of(k)
        w_next = jnp.where(k + 1 < levels, wet_of(k + 1), 0.0)
        w_east = roll(w, -1, 1)
        w_north = roll(w, -1, 0)
        ke = ke_ref[0, k]
        ke_sel = jnp.where(row >= ny, roll(ke, -1, 1), ke)
        east_mask = w * w_east
        ce_ref[k] = ke_sel * east_mask
        kn = ke_ref[1, k]
        kn_up = roll(kn, -1, 0)
        kn_sel = jnp.where(
            row < ny - 1, kn, jnp.where(row == ny - 1, 0.5 * (kn + kn_up), jnp.where(row == ny, kn_up, 0.0))
        )
        north_mask = w * w_north
        cn_ref[k] = kn_sel * north_mask
        cz_ref[k + 1] = vertical_rate * w * w_next
        src_ref[k] = thaw_rate * shelf * w * (1.0 - w_next)
        wet_ref[k] = w
        gem_ref[k] = east_mask[:ny, :width]
        gnm_ref[k] = jnp.where(row < ny - 1, north_mask, 0.5 * north_mask)[:ny, :width]
        for c in range(chans):
            a_ref[c, k] = w * ve_ref[c, k]
        return carry

    lax.fori_loop(0, levels, setup, 0, unroll=True)

    def operate(x_ref, c, k, diffs=None):
        x = x_ref[c, k]
        above = x_ref[c, jnp.minimum(k + 1, levels - 1)]
        below = x_ref[c, jnp.maximum(k - 1, 0)]
        d_east = roll(x, -1, 1) - x
        d_north = roll(x, -1, 0) - x
        if diffs is not None:
            diffs[0][c, k] = d_east[:ny, :width]
            diffs[1][c, k] = d_north[:ny, :width]
        east = ce_ref[k] * d_east
        north = cn_ref[k] * d_north
        change = (east - roll(east, 1, 1)) + (north - roll(north, 1, 0))
        change = change + (cz_ref[k + 1] * (above - x) - cz_ref[k] * (x - below))
        return x, change

    def forward_first(ck, carry):
        c = ck // levels
        k = ck % levels
        x, change = operate(ue_ref, c, k, (du0e_ref, du0n_ref))
        heat = jnp.where(c == 0, 1.0, 0.0)
        u1_ref[c, k] = wet_ref[k] * (x + change + heat * src_ref[k])
        return carry


    def forward_second(ck, carry):
        c = ck // levels
        k = ck % levels
        x, change = operate(u1_ref, c, k, (du1e_ref, du1n_ref))
        heat = jnp.where(c == 0, 1.0, 0.0)
        out = wet_ref[k] * (x + change + heat * src_ref[k])
        fin_ref[c, k] = out[:ny, :width]
        return carry


    def backward_second(ck, carry):
        c = ck // levels
        k = ck % levels
        x, change = operate(a_ref, c, k, (dv2e_ref, dv2n_ref))
        b_ref[c, k] = wet_ref[k] * (x + change)
        return carry

    def first_pair(ck, carry):
        forward_first(ck, carry)
        return backward_second(ck, carry)

    lax.fori_loop(0, planes, first_pair, 0, unroll=8)

    def backward_first(ck, carry):
        c = ck // levels
        k = ck % levels
        x, change = operate(b_ref, c, k, (dv1e_ref, dv1n_ref))
        adj_ref[c, k] = (x + change)[:ny, :width]
        return carry

    def second_pair(ck, carry):
        forward_second(ck, carry)
        return backward_first(ck, carry)

    lax.fori_loop(0, planes, second_pair, 0, unroll=8)

    def gradient(k, carry):
        g_east = jnp.zeros((ny, width), jnp.float32)
        g_north = jnp.zeros((ny, width), jnp.float32)
        for c in range(chans):
            g_east = g_east - du0e_ref[c, k] * dv1e_ref[c, k] - du1e_ref[c, k] * dv2e_ref[c, k]
            g_north = g_north - du0n_ref[c, k] * dv1n_ref[c, k] - du1n_ref[c, k] * dv2n_ref[c, k]
        grad_ref[0, k] = gem_ref[k] * g_east
        grad_ref[1, k] = gnm_ref[k] * g_north
        return carry

    lax.fori_loop(0, levels, gradient, 0, unroll=True)


def on_device(tracers, diffusivity, level_count, shelf_mask, cotangent):
    _, chans, levels, ny, width = tracers.shape
    lanes = width + 128
    rows = -(-(ny + 2) // 8) * 8
    full_kappa = gathered_over_scen(diffusivity)
    fields = jnp.concatenate(
        [
            tracers[0].reshape(chans * levels, ny, width),
            cotangent[0].reshape(chans * levels, ny, width),
            full_kappa.reshape(2 * levels, ny, width),
            level_count.astype(jnp.float32)[None],
            shelf_mask.astype(jnp.float32)[None],
        ]
    )
    ext = extended(fields, lanes, rows)
    field = jax.ShapeDtypeStruct((chans, levels, ny, width), jnp.float32)
    plane = pltpu.VMEM((levels, rows, lanes), jnp.float32)
    planes_c = pltpu.VMEM((chans, levels, rows, lanes), jnp.float32)
    diff = pltpu.VMEM((chans, levels, ny, width), jnp.float32)
    mask = pltpu.VMEM((levels, ny, width), jnp.float32)
    final, adjoint, grad = pl.pallas_call(
        diffusion_kernel,
        out_shape=(field, field, jax.ShapeDtypeStruct((2, levels, ny, width), jnp.float32)),
        scratch_shapes=[
            plane,
            plane,
            plane,
            pltpu.VMEM((levels + 1, rows, lanes), jnp.float32),
            plane,
            mask,
            mask,
            planes_c,
            planes_c,
            planes_c,
        ]
        + [diff] * 8,
        compiler_params=pltpu.CompilerParams(vmem_limit_bytes=48 * 1024 * 1024),
        interpret=INTERPRET,
    )(ext)
    kappa_grad = summed_over_scen(grad)
    return (final[None], adjoint[None], kappa_grad)


def gathered_over_scen(block):
    parts = lax.axis_size("scen")
    if parts % 2:
        return lax.all_gather(block, "scen", axis=2, tiled=True)
    kinds, levels, rows, width = block.shape
    me = lax.axis_index("scen")
    core = me % 2
    chip = me // 2
    chips = parts // 2
    got = [block]
    for step in range(1, chips):
        got.append(
            lax.ppermute(block, "scen", [(q, ((q // 2 + step) % chips) * 2 + q % 2) for q in range(parts)])
        )
    same = jnp.stack(got)
    other = lax.ppermute(same, "scen", [(q, q ^ 1) for q in range(parts)])
    by_core = jnp.where(core == 0, jnp.stack([same, other], axis=1), jnp.stack([other, same], axis=1))
    order = (chip - jnp.arange(chips)) % chips
    by_chip = jnp.take(by_core, order, axis=0)
    return by_chip.transpose(2, 3, 0, 1, 4, 5).reshape(kinds, levels, parts * rows, width)


def summed_over_scen(grad):
    parts = lax.axis_size("scen")
    kinds, levels, ny, width = grad.shape
    if parts % 2:
        split = grad.reshape(kinds, levels, parts, ny // parts, width)
        return lax.all_to_all(split, "scen", 2, 2, tiled=True).sum(axis=2)
    me = lax.axis_index("scen")
    core = me % 2
    chip = me // 2
    chips = parts // 2
    split = grad.reshape(kinds, levels, chips, 2, ny // parts, width)
    mine = lax.dynamic_index_in_dim(split, core, axis=3, keepdims=False)
    other = lax.dynamic_index_in_dim(split, 1 - core, axis=3, keepdims=False)
    pair = lax.ppermute(other, "scen", [(q, q ^ 1) for q in range(parts)])
    chip_sum = mine + pair
    total = lax.dynamic_index_in_dim(chip_sum, chip, axis=2, keepdims=False)
    for step in range(1, chips):
        send = lax.dynamic_index_in_dim(chip_sum, (chip + step) % chips, axis=2, keepdims=False)
        total = total + lax.ppermute(
            send, "scen", [(q, ((q // 2 + step) % chips) * 2 + q % 2) for q in range(parts)]
        )
    return total


def solution(mesh):
    placed = (
        P("scen", None, None, None, "space"),
        P(None, None, "scen", "space"),
        P(None, "space"),
        P(None, "space"),
        P("scen", None, None, None, "space"),
    )
    return jax.shard_map(
        on_device,
        mesh=mesh,
        in_specs=placed,
        out_specs=(
            P("scen", None, None, None, "space"),
            P("scen", None, None, None, "space"),
            P(None, None, "scen", "space"),
        ),
        check_vma=False,
    )
```

```python
import jax
import jax.numpy as jnp
from jax import lax
from jax.experimental import pallas as pl
from jax.experimental.pallas import tpu as pltpu
from jax.sharding import PartitionSpec as P

STEPS = 2
HALO = 2

vertical_rate = 0.1
thaw_rate = 0.3

INTERPRET = False


def shifted(x, perm):
    return lax.ppermute(x, "space", perm)


def picker(size, positions):
    where = lax.broadcasted_iota(jnp.int32, (size, len(positions)), 0)
    slot = lax.broadcasted_iota(jnp.int32, (size, len(positions)), 1)
    hit = jnp.zeros((size, len(positions)), jnp.bool_)
    for p, at in enumerate(positions):
        hit = hit | ((slot == p) & (where == at))
    return hit.astype(jnp.float32)


def contract(a, b, dims):
    return lax.dot_general(
        a, b, (dims, ((), ())), precision=lax.Precision.HIGHEST, preferred_element_type=jnp.float32
    )


def extended(fields, lanes, rows):
    n = lax.axis_size("space")
    count, ny, width = fields.shape
    spare = lanes - width
    flat = fields.reshape(count * ny, width)
    edges = contract(picker(width, [width - 2, width - 1, 0, 1]), flat, ((0,), (1,)))
    west = shifted(edges[0:2], [(q, (q + 1) % n) for q in range(n)])
    east = shifted(edges[2:4], [(q, (q - 1) % n) for q in range(n)])
    mirrored = fields[:, ny - 1:ny - 3:-1, ::-1]
    ghost = shifted(mirrored, [(q, n - 1 - q) for q in range(n)])
    top_edges = edges.reshape(4, count, ny)[:, :, ny - 1:ny - 3:-1]
    ghost_east = shifted(top_edges[1::-1], [(q, (n - 2 - q) % n) for q in range(n)])
    ghost_west = shifted(top_edges[3:1:-1], [(q, (n - q) % n) for q in range(n)])
    place = picker(spare, [0, 1, spare - 2, spare - 1]).T
    side = contract(jnp.concatenate([east, west]), place, ((0,), (0,))).reshape(count, ny, spare)
    ghost_halo = jnp.concatenate([ghost_east, ghost_west]).reshape(4, count * 2)
    ghost_side = contract(ghost_halo, place, ((0,), (0,))).reshape(count, 2, spare)
    top = jnp.concatenate([fields, side], axis=-1)
    folded = jnp.concatenate([ghost, ghost_side], axis=-1)
    pad = jnp.zeros((count, rows - ny - 2, lanes), fields.dtype)
    return jnp.concatenate([top, folded, pad], axis=1)


def roll(x, shift, axis):
    return pltpu.roll(x, shift % x.shape[axis], axis)


class Planes:
    def __init__(self, ref, start, levels):
        self.ref = ref
        self.start = start
        self.levels = levels

    def __getitem__(self, index):
        c, k = index
        return self.ref[self.start + c * self.levels + k]


def diffusion_kernel(
    x_ref,
    fin_ref, adj_ref, grad_ref,
    wet_ref, ce_ref, cn_ref, cz_ref, src_ref, gem_ref, gnm_ref, u1_ref, a_ref, b_ref,
    du0e_ref, du0n_ref, du1e_ref, du1n_ref, dv1e_ref, dv1n_ref, dv2e_ref, dv2n_ref,
):
    levels, rows, lanes = wet_ref.shape
    chans, _, ny, width = fin_ref.shape
    row = lax.broadcasted_iota(jnp.int32, (rows, lanes), 0)
    lane = lax.broadcasted_iota(jnp.int32, (rows, lanes), 1)
    planes = chans * levels
    ue_ref = Planes(x_ref, 0, levels)
    ve_ref = Planes(x_ref, planes, levels)
    ke_ref = Planes(x_ref, 2 * planes, levels)
    lev = x_ref[2 * planes + 2 * levels]
    shelf = x_ref[2 * planes + 2 * levels + 1]

    def wet_of(k):
        return (lev > k.astype(jnp.float32)).astype(jnp.float32)

    cz_ref[0] = jnp.zeros((rows, lanes), jnp.float32)

    def setup(k, carry):
        w = wet_of(k)
        w_next = jnp.where(k + 1 < levels, wet_of(k + 1), 0.0)
        w_east = roll(w, -1, 1)
        w_north = roll(w, -1, 0)
        ke = ke_ref[0, k]
        ke_sel = jnp.where(row >= ny, roll(ke, -1, 1), ke)
        east_mask = w * w_east
        ce_ref[k] = ke_sel * east_mask
        kn = ke_ref[1, k]
        kn_up = roll(kn, -1, 0)
        kn_sel = jnp.where(
            row < ny - 1, kn, jnp.where(row == ny - 1, 0.5 * (kn + kn_up), jnp.where(row == ny, kn_up, 0.0))
        )
        north_mask = w * w_north
        cn_ref[k] = kn_sel * north_mask
        cz_ref[k + 1] = vertical_rate * w * w_next
        src_ref[k] = thaw_rate * shelf * w * (1.0 - w_next)
        wet_ref[k] = w
        gem_ref[k] = east_mask[:ny, :width]
        gnm_ref[k] = jnp.where(row < ny - 1, north_mask, 0.5 * north_mask)[:ny, :width]
        for c in range(chans):
            a_ref[c, k] = w * ve_ref[c, k]
        return carry

    lax.fori_loop(0, levels, setup, 0, unroll=True)

    def operate(x_ref, c, k, diffs=None):
        x = x_ref[c, k]
        above = x_ref[c, jnp.minimum(k + 1, levels - 1)]
        below = x_ref[c, jnp.maximum(k - 1, 0)]
        d_east = roll(x, -1, 1) - x
        d_north = roll(x, -1, 0) - x
        if diffs is not None:
            diffs[0][c, k] = d_east[:ny, :width]
            diffs[1][c, k] = d_north[:ny, :width]
        east = ce_ref[k] * d_east
        north = cn_ref[k] * d_north
        change = (east - roll(east, 1, 1)) + (north - roll(north, 1, 0))
        change = change + (cz_ref[k + 1] * (above - x) - cz_ref[k] * (x - below))
        return x, change

    def forward_first(ck, carry):
        c = ck // levels
        k = ck % levels
        x, change = operate(ue_ref, c, k, (du0e_ref, du0n_ref))
        heat = jnp.where(c == 0, 1.0, 0.0)
        u1_ref[c, k] = wet_ref[k] * (x + change + heat * src_ref[k])
        return carry


    def forward_second(ck, carry):
        c = ck // levels
        k = ck % levels
        x, change = operate(u1_ref, c, k, (du1e_ref, du1n_ref))
        heat = jnp.where(c == 0, 1.0, 0.0)
        out = wet_ref[k] * (x + change + heat * src_ref[k])
        fin_ref[c, k] = out[:ny, :width]
        return carry


    def backward_second(ck, carry):
        c = ck // levels
        k = ck % levels
        x, change = operate(a_ref, c, k, (dv2e_ref, dv2n_ref))
        b_ref[c, k] = wet_ref[k] * (x + change)
        return carry

    def first_pair(ck, carry):
        forward_first(ck, carry)
        return backward_second(ck, carry)

    lax.fori_loop(0, planes, first_pair, 0, unroll=5)

    def backward_first(ck, carry):
        c = ck // levels
        k = ck % levels
        x, change = operate(b_ref, c, k, (dv1e_ref, dv1n_ref))
        adj_ref[c, k] = (x + change)[:ny, :width]
        return carry

    def second_pair(ck, carry):
        forward_second(ck, carry)
        return backward_first(ck, carry)

    lax.fori_loop(0, planes, second_pair, 0, unroll=5)

    def gradient(k, carry):
        g_east = jnp.zeros((ny, width), jnp.float32)
        g_north = jnp.zeros((ny, width), jnp.float32)
        for c in range(chans):
            g_east = g_east - du0e_ref[c, k] * dv1e_ref[c, k] - du1e_ref[c, k] * dv2e_ref[c, k]
            g_north = g_north - du0n_ref[c, k] * dv1n_ref[c, k] - du1n_ref[c, k] * dv2n_ref[c, k]
        grad_ref[0, k] = gem_ref[k] * g_east
        grad_ref[1, k] = gnm_ref[k] * g_north
        return carry

    lax.fori_loop(0, levels, gradient, 0, unroll=True)


def on_device(tracers, diffusivity, level_count, shelf_mask, cotangent):
    _, chans, levels, ny, width = tracers.shape
    lanes = width + 128
    rows = -(-(ny + 2) // 8) * 8
    full_kappa = gathered_over_scen(diffusivity)
    fields = jnp.concatenate(
        [
            tracers[0].reshape(chans * levels, ny, width),
            cotangent[0].reshape(chans * levels, ny, width),
            full_kappa.reshape(2 * levels, ny, width),
            level_count.astype(jnp.float32)[None],
            shelf_mask.astype(jnp.float32)[None],
        ]
    )
    ext = extended(fields, lanes, rows)
    field = jax.ShapeDtypeStruct((chans, levels, ny, width), jnp.float32)
    plane = pltpu.VMEM((levels, rows, lanes), jnp.float32)
    planes_c = pltpu.VMEM((chans, levels, rows, lanes), jnp.float32)
    diff = pltpu.VMEM((chans, levels, ny, width), jnp.float32)
    mask = pltpu.VMEM((levels, ny, width), jnp.float32)
    final, adjoint, grad = pl.pallas_call(
        diffusion_kernel,
        out_shape=(field, field, jax.ShapeDtypeStruct((2, levels, ny, width), jnp.float32)),
        scratch_shapes=[
            plane,
            plane,
            plane,
            pltpu.VMEM((levels + 1, rows, lanes), jnp.float32),
            plane,
            mask,
            mask,
            planes_c,
            planes_c,
            planes_c,
        ]
        + [diff] * 8,
        compiler_params=pltpu.CompilerParams(vmem_limit_bytes=48 * 1024 * 1024),
        interpret=INTERPRET,
    )(ext)
    kappa_grad = summed_over_scen(grad)
    return (final[None], adjoint[None], kappa_grad)


def gathered_over_scen(block):
    parts = lax.axis_size("scen")
    if parts % 2:
        return lax.all_gather(block, "scen", axis=2, tiled=True)
    kinds, levels, rows, width = block.shape
    me = lax.axis_index("scen")
    core = me % 2
    chip = me // 2
    chips = parts // 2
    got = [block]
    for step in range(1, chips):
        got.append(
            lax.ppermute(block, "scen", [(q, ((q // 2 + step) % chips) * 2 + q % 2) for q in range(parts)])
        )
    same = jnp.stack(got)
    other = lax.ppermute(same, "scen", [(q, q ^ 1) for q in range(parts)])
    by_core = jnp.where(core == 0, jnp.stack([same, other], axis=1), jnp.stack([other, same], axis=1))
    order = (chip - jnp.arange(chips)) % chips
    by_chip = jnp.take(by_core, order, axis=0)
    return by_chip.transpose(2, 3, 0, 1, 4, 5).reshape(kinds, levels, parts * rows, width)


def summed_over_scen(grad):
    parts = lax.axis_size("scen")
    kinds, levels, ny, width = grad.shape
    if parts % 2:
        split = grad.reshape(kinds, levels, parts, ny // parts, width)
        return lax.all_to_all(split, "scen", 2, 2, tiled=True).sum(axis=2)
    me = lax.axis_index("scen")
    core = me % 2
    chip = me // 2
    chips = parts // 2
    split = grad.reshape(kinds, levels, chips, 2, ny // parts, width)
    mine = lax.dynamic_index_in_dim(split, core, axis=3, keepdims=False)
    other = lax.dynamic_index_in_dim(split, 1 - core, axis=3, keepdims=False)
    pair = lax.ppermute(other, "scen", [(q, q ^ 1) for q in range(parts)])
    chip_sum = mine + pair
    total = lax.dynamic_index_in_dim(chip_sum, chip, axis=2, keepdims=False)
    for step in range(1, chips):
        send = lax.dynamic_index_in_dim(chip_sum, (chip + step) % chips, axis=2, keepdims=False)
        total = total + lax.ppermute(
            send, "scen", [(q, ((q // 2 + step) % chips) * 2 + q % 2) for q in range(parts)]
        )
    return total


def solution(mesh):
    placed = (
        P("scen", None, None, None, "space"),
        P(None, None, "scen", "space"),
        P(None, "space"),
        P(None, "space"),
        P("scen", None, None, None, "space"),
    )
    return jax.shard_map(
        on_device,
        mesh=mesh,
        in_specs=placed,
        out_specs=(
            P("scen", None, None, None, "space"),
            P("scen", None, None, None, "space"),
            P(None, None, "scen", "space"),
        ),
        check_vma=False,
    )
```

```python
import jax
import jax.numpy as jnp
from jax import lax
from jax.experimental import pallas as pl
from jax.experimental.pallas import tpu as pltpu
from jax.sharding import PartitionSpec as P

STEPS = 2
HALO = 2

vertical_rate = 0.1
thaw_rate = 0.3

INTERPRET = False


def shifted(x, perm):
    return lax.ppermute(x, "space", perm)


def picker(size, positions):
    where = lax.broadcasted_iota(jnp.int32, (size, len(positions)), 0)
    slot = lax.broadcasted_iota(jnp.int32, (size, len(positions)), 1)
    hit = jnp.zeros((size, len(positions)), jnp.bool_)
    for p, at in enumerate(positions):
        hit = hit | ((slot == p) & (where == at))
    return hit.astype(jnp.float32)


def contract(a, b, dims):
    return lax.dot_general(
        a, b, (dims, ((), ())), precision=lax.Precision.HIGHEST, preferred_element_type=jnp.float32
    )


def extended(fields, lanes, rows):
    n = lax.axis_size("space")
    count, ny, width = fields.shape
    spare = lanes - width
    flat = fields.reshape(count * ny, width)
    edges = contract(picker(width, [width - 2, width - 1, 0, 1]), flat, ((0,), (1,)))
    west = shifted(edges[0:2], [(q, (q + 1) % n) for q in range(n)])
    east = shifted(edges[2:4], [(q, (q - 1) % n) for q in range(n)])
    mirrored = fields[:, ny - 1:ny - 3:-1, ::-1]
    ghost = shifted(mirrored, [(q, n - 1 - q) for q in range(n)])
    top_edges = edges.reshape(4, count, ny)[:, :, ny - 1:ny - 3:-1]
    ghost_east = shifted(top_edges[1::-1], [(q, (n - 2 - q) % n) for q in range(n)])
    ghost_west = shifted(top_edges[3:1:-1], [(q, (n - q) % n) for q in range(n)])
    place = picker(spare, [0, 1, spare - 2, spare - 1]).T
    side = contract(jnp.concatenate([east, west]), place, ((0,), (0,))).reshape(count, ny, spare)
    ghost_halo = jnp.concatenate([ghost_east, ghost_west]).reshape(4, count * 2)
    ghost_side = contract(ghost_halo, place, ((0,), (0,))).reshape(count, 2, spare)
    top = jnp.concatenate([fields, side], axis=-1)
    folded = jnp.concatenate([ghost, ghost_side], axis=-1)
    pad = jnp.zeros((count, rows - ny - 2, lanes), fields.dtype)
    return jnp.concatenate([top, folded, pad], axis=1)


def roll(x, shift, axis):
    return pltpu.roll(x, shift % x.shape[axis], axis)


class Planes:
    def __init__(self, ref, start, levels):
        self.ref = ref
        self.start = start
        self.levels = levels

    def __getitem__(self, index):
        c, k = index
        return self.ref[self.start + c * self.levels + k]


def diffusion_kernel(
    x_ref,
    fin_ref, adj_ref, grad_ref,
    wet_ref, ce_ref, cn_ref, cz_ref, src_ref, gem_ref, gnm_ref, u1_ref, a_ref, b_ref,
    du0e_ref, du0n_ref, du1e_ref, du1n_ref, dv1e_ref, dv1n_ref, dv2e_ref, dv2n_ref,
):
    levels, rows, lanes = wet_ref.shape
    chans, _, ny, width = fin_ref.shape
    row = lax.broadcasted_iota(jnp.int32, (rows, lanes), 0)
    lane = lax.broadcasted_iota(jnp.int32, (rows, lanes), 1)
    planes = chans * levels
    ue_ref = Planes(x_ref, 0, levels)
    ve_ref = Planes(x_ref, planes, levels)
    ke_ref = Planes(x_ref, 2 * planes, levels)
    lev = x_ref[2 * planes + 2 * levels]
    shelf = x_ref[2 * planes + 2 * levels + 1]

    def wet_of(k):
        return (lev > k.astype(jnp.float32)).astype(jnp.float32)

    cz_ref[0] = jnp.zeros((rows, lanes), jnp.float32)

    def setup(k, carry):
        w = wet_of(k)
        w_next = jnp.where(k + 1 < levels, wet_of(k + 1), 0.0)
        w_east = roll(w, -1, 1)
        w_north = roll(w, -1, 0)
        ke = ke_ref[0, k]
        ke_sel = jnp.where(row >= ny, roll(ke, -1, 1), ke)
        east_mask = w * w_east
        ce_ref[k] = ke_sel * east_mask
        kn = ke_ref[1, k]
        kn_up = roll(kn, -1, 0)
        kn_sel = jnp.where(
            row < ny - 1, kn, jnp.where(row == ny - 1, 0.5 * (kn + kn_up), jnp.where(row == ny, kn_up, 0.0))
        )
        north_mask = w * w_north
        cn_ref[k] = kn_sel * north_mask
        cz_ref[k + 1] = vertical_rate * w * w_next
        src_ref[k] = thaw_rate * shelf * w * (1.0 - w_next)
        wet_ref[k] = w
        gem_ref[k] = east_mask[:ny, :width]
        gnm_ref[k] = jnp.where(row < ny - 1, north_mask, 0.5 * north_mask)[:ny, :width]
        for c in range(chans):
            a_ref[c, k] = w * ve_ref[c, k]
        return carry

    lax.fori_loop(0, levels, setup, 0, unroll=10)

    def operate(x_ref, c, k, diffs=None):
        x = x_ref[c, k]
        above = x_ref[c, jnp.minimum(k + 1, levels - 1)]
        below = x_ref[c, jnp.maximum(k - 1, 0)]
        d_east = roll(x, -1, 1) - x
        d_north = roll(x, -1, 0) - x
        if diffs is not None:
            diffs[0][c, k] = d_east[:ny, :width]
            diffs[1][c, k] = d_north[:ny, :width]
        east = ce_ref[k] * d_east
        north = cn_ref[k] * d_north
        change = (east - roll(east, 1, 1)) + (north - roll(north, 1, 0))
        change = change + (cz_ref[k + 1] * (above - x) - cz_ref[k] * (x - below))
        return x, change

    def forward_first(ck, carry):
        c = ck // levels
        k = ck % levels
        x, change = operate(ue_ref, c, k, (du0e_ref, du0n_ref))
        heat = jnp.where(c == 0, 1.0, 0.0)
        u1_ref[c, k] = wet_ref[k] * (x + change + heat * src_ref[k])
        return carry


    def forward_second(ck, carry):
        c = ck // levels
        k = ck % levels
        x, change = operate(u1_ref, c, k, (du1e_ref, du1n_ref))
        heat = jnp.where(c == 0, 1.0, 0.0)
        out = wet_ref[k] * (x + change + heat * src_ref[k])
        fin_ref[c, k] = out[:ny, :width]
        return carry


    def backward_second(ck, carry):
        c = ck // levels
        k = ck % levels
        x, change = operate(a_ref, c, k, (dv2e_ref, dv2n_ref))
        b_ref[c, k] = wet_ref[k] * (x + change)
        return carry

    def first_pair(ck, carry):
        forward_first(ck, carry)
        return backward_second(ck, carry)

    lax.fori_loop(0, planes, first_pair, 0, unroll=4)

    def backward_first(ck, carry):
        c = ck // levels
        k = ck % levels
        x, change = operate(b_ref, c, k, (dv1e_ref, dv1n_ref))
        adj_ref[c, k] = (x + change)[:ny, :width]
        return carry

    def second_pair(ck, carry):
        forward_second(ck, carry)
        return backward_first(ck, carry)

    lax.fori_loop(0, planes, second_pair, 0, unroll=4)

    def gradient(k, carry):
        g_east = jnp.zeros((ny, width), jnp.float32)
        g_north = jnp.zeros((ny, width), jnp.float32)
        for c in range(chans):
            g_east = g_east - du0e_ref[c, k] * dv1e_ref[c, k] - du1e_ref[c, k] * dv2e_ref[c, k]
            g_north = g_north - du0n_ref[c, k] * dv1n_ref[c, k] - du1n_ref[c, k] * dv2n_ref[c, k]
        grad_ref[0, k] = gem_ref[k] * g_east
        grad_ref[1, k] = gnm_ref[k] * g_north
        return carry

    lax.fori_loop(0, levels, gradient, 0, unroll=True)


def on_device(tracers, diffusivity, level_count, shelf_mask, cotangent):
    _, chans, levels, ny, width = tracers.shape
    lanes = width + 128
    rows = -(-(ny + 2) // 8) * 8
    full_kappa = gathered_over_scen(diffusivity)
    fields = jnp.concatenate(
        [
            tracers[0].reshape(chans * levels, ny, width),
            cotangent[0].reshape(chans * levels, ny, width),
            full_kappa.reshape(2 * levels, ny, width),
            level_count.astype(jnp.float32)[None],
            shelf_mask.astype(jnp.float32)[None],
        ]
    )
    ext = extended(fields, lanes, rows)
    field = jax.ShapeDtypeStruct((chans, levels, ny, width), jnp.float32)
    plane = pltpu.VMEM((levels, rows, lanes), jnp.float32)
    planes_c = pltpu.VMEM((chans, levels, rows, lanes), jnp.float32)
    diff = pltpu.VMEM((chans, levels, ny, width), jnp.float32)
    mask = pltpu.VMEM((levels, ny, width), jnp.float32)
    final, adjoint, grad = pl.pallas_call(
        diffusion_kernel,
        out_shape=(field, field, jax.ShapeDtypeStruct((2, levels, ny, width), jnp.float32)),
        scratch_shapes=[
            plane,
            plane,
            plane,
            pltpu.VMEM((levels + 1, rows, lanes), jnp.float32),
            plane,
            mask,
            mask,
            planes_c,
            planes_c,
            planes_c,
        ]
        + [diff] * 8,
        compiler_params=pltpu.CompilerParams(vmem_limit_bytes=48 * 1024 * 1024),
        interpret=INTERPRET,
    )(ext)
    kappa_grad = summed_over_scen(grad)
    return (final[None], adjoint[None], kappa_grad)


def gathered_over_scen(block):
    parts = lax.axis_size("scen")
    if parts % 2:
        return lax.all_gather(block, "scen", axis=2, tiled=True)
    kinds, levels, rows, width = block.shape
    me = lax.axis_index("scen")
    core = me % 2
    chip = me // 2
    chips = parts // 2
    got = [block]
    for step in range(1, chips):
        got.append(
            lax.ppermute(block, "scen", [(q, ((q // 2 + step) % chips) * 2 + q % 2) for q in range(parts)])
        )
    same = jnp.stack(got)
    other = lax.ppermute(same, "scen", [(q, q ^ 1) for q in range(parts)])
    by_core = jnp.where(core == 0, jnp.stack([same, other], axis=1), jnp.stack([other, same], axis=1))
    order = (chip - jnp.arange(chips)) % chips
    by_chip = jnp.take(by_core, order, axis=0)
    return by_chip.transpose(2, 3, 0, 1, 4, 5).reshape(kinds, levels, parts * rows, width)


def summed_over_scen(grad):
    parts = lax.axis_size("scen")
    kinds, levels, ny, width = grad.shape
    if parts % 2:
        split = grad.reshape(kinds, levels, parts, ny // parts, width)
        return lax.all_to_all(split, "scen", 2, 2, tiled=True).sum(axis=2)
    me = lax.axis_index("scen")
    core = me % 2
    chip = me // 2
    chips = parts // 2
    split = grad.reshape(kinds, levels, chips, 2, ny // parts, width)
    mine = lax.dynamic_index_in_dim(split, core, axis=3, keepdims=False)
    other = lax.dynamic_index_in_dim(split, 1 - core, axis=3, keepdims=False)
    pair = lax.ppermute(other, "scen", [(q, q ^ 1) for q in range(parts)])
    chip_sum = mine + pair
    total = lax.dynamic_index_in_dim(chip_sum, chip, axis=2, keepdims=False)
    for step in range(1, chips):
        send = lax.dynamic_index_in_dim(chip_sum, (chip + step) % chips, axis=2, keepdims=False)
        total = total + lax.ppermute(
            send, "scen", [(q, ((q // 2 + step) % chips) * 2 + q % 2) for q in range(parts)]
        )
    return total


def solution(mesh):
    placed = (
        P("scen", None, None, None, "space"),
        P(None, None, "scen", "space"),
        P(None, "space"),
        P(None, "space"),
        P("scen", None, None, None, "space"),
    )
    return jax.shard_map(
        on_device,
        mesh=mesh,
        in_specs=placed,
        out_specs=(
            P("scen", None, None, None, "space"),
            P("scen", None, None, None, "space"),
            P(None, None, "scen", "space"),
        ),
        check_vma=False,
    )
```

```python
import jax
import jax.numpy as jnp
from jax import lax
from jax.experimental import pallas as pl
from jax.experimental.pallas import tpu as pltpu
from jax.sharding import PartitionSpec as P

STEPS = 2
HALO = 2

vertical_rate = 0.1
thaw_rate = 0.3

INTERPRET = False


def shifted(x, perm):
    return lax.ppermute(x, "space", perm)


def picker(size, positions):
    where = lax.broadcasted_iota(jnp.int32, (size, len(positions)), 0)
    slot = lax.broadcasted_iota(jnp.int32, (size, len(positions)), 1)
    hit = jnp.zeros((size, len(positions)), jnp.bool_)
    for p, at in enumerate(positions):
        hit = hit | ((slot == p) & (where == at))
    return hit.astype(jnp.float32)


def contract(a, b, dims):
    return lax.dot_general(
        a, b, (dims, ((), ())), precision=lax.Precision.HIGHEST, preferred_element_type=jnp.float32
    )


def extended(fields, lanes, rows):
    n = lax.axis_size("space")
    count, ny, width = fields.shape
    spare = lanes - width
    flat = fields.reshape(count * ny, width)
    edges = contract(picker(width, [width - 2, width - 1, 0, 1]), flat, ((0,), (1,)))
    west = shifted(edges[0:2], [(q, (q + 1) % n) for q in range(n)])
    east = shifted(edges[2:4], [(q, (q - 1) % n) for q in range(n)])
    mirrored = fields[:, ny - 1:ny - 3:-1, ::-1]
    ghost = shifted(mirrored, [(q, n - 1 - q) for q in range(n)])
    top_edges = edges.reshape(4, count, ny)[:, :, ny - 1:ny - 3:-1]
    ghost_east = shifted(top_edges[1::-1], [(q, (n - 2 - q) % n) for q in range(n)])
    ghost_west = shifted(top_edges[3:1:-1], [(q, (n - q) % n) for q in range(n)])
    place = picker(spare, [0, 1, spare - 2, spare - 1]).T
    side = contract(jnp.concatenate([east, west]), place, ((0,), (0,))).reshape(count, ny, spare)
    ghost_halo = jnp.concatenate([ghost_east, ghost_west]).reshape(4, count * 2)
    ghost_side = contract(ghost_halo, place, ((0,), (0,))).reshape(count, 2, spare)
    top = jnp.concatenate([fields, side], axis=-1)
    folded = jnp.concatenate([ghost, ghost_side], axis=-1)
    pad = jnp.zeros((count, rows - ny - 2, lanes), fields.dtype)
    return jnp.concatenate([top, folded, pad], axis=1)


def roll(x, shift, axis):
    return pltpu.roll(x, shift % x.shape[axis], axis)


class Planes:
    def __init__(self, ref, start, levels):
        self.ref = ref
        self.start = start
        self.levels = levels

    def __getitem__(self, index):
        c, k = index
        return self.ref[self.start + c * self.levels + k]


def diffusion_kernel(
    x_ref,
    fin_ref, adj_ref, grad_ref,
    wet_ref, ce_ref, cn_ref, cz_ref, src_ref, gem_ref, gnm_ref, u1_ref, a_ref, b_ref,
    du0e_ref, du0n_ref, du1e_ref, du1n_ref, dv1e_ref, dv1n_ref, dv2e_ref, dv2n_ref,
):
    levels, rows, lanes = wet_ref.shape
    chans, _, ny, width = fin_ref.shape
    row = lax.broadcasted_iota(jnp.int32, (rows, lanes), 0)
    lane = lax.broadcasted_iota(jnp.int32, (rows, lanes), 1)
    planes = chans * levels
    ue_ref = Planes(x_ref, 0, levels)
    ve_ref = Planes(x_ref, planes, levels)
    ke_ref = Planes(x_ref, 2 * planes, levels)
    lev = x_ref[2 * planes + 2 * levels]
    shelf = x_ref[2 * planes + 2 * levels + 1]

    def wet_of(k):
        return (lev > k.astype(jnp.float32)).astype(jnp.float32)

    cz_ref[0] = jnp.zeros((rows, lanes), jnp.float32)

    def setup(k, carry):
        w = wet_of(k)
        w_next = jnp.where(k + 1 < levels, wet_of(k + 1), 0.0)
        w_east = roll(w, -1, 1)
        w_north = roll(w, -1, 0)
        ke = ke_ref[0, k]
        ke_sel = jnp.where(row >= ny, roll(ke, -1, 1), ke)
        east_mask = w * w_east
        ce_ref[k] = ke_sel * east_mask
        kn = ke_ref[1, k]
        kn_up = roll(kn, -1, 0)
        kn_sel = jnp.where(
            row < ny - 1, kn, jnp.where(row == ny - 1, 0.5 * (kn + kn_up), jnp.where(row == ny, kn_up, 0.0))
        )
        north_mask = w * w_north
        cn_ref[k] = kn_sel * north_mask
        cz_ref[k + 1] = vertical_rate * w * w_next
        src_ref[k] = thaw_rate * shelf * w * (1.0 - w_next)
        wet_ref[k] = w
        gem_ref[k] = east_mask[:ny, :width]
        gnm_ref[k] = jnp.where(row < ny - 1, north_mask, 0.5 * north_mask)[:ny, :width]
        for c in range(chans):
            a_ref[c, k] = w * ve_ref[c, k]
        return carry

    lax.fori_loop(0, levels, setup, 0, unroll=10)

    def operate(x_ref, c, k, diffs=None):
        x = x_ref[c, k]
        above = x_ref[c, jnp.minimum(k + 1, levels - 1)]
        below = x_ref[c, jnp.maximum(k - 1, 0)]
        d_east = roll(x, -1, 1) - x
        d_north = roll(x, -1, 0) - x
        if diffs is not None:
            diffs[0][c, k] = d_east[:ny, :width]
            diffs[1][c, k] = d_north[:ny, :width]
        east = ce_ref[k] * d_east
        north = cn_ref[k] * d_north
        change = (east - roll(east, 1, 1)) + (north - roll(north, 1, 0))
        change = change + (cz_ref[k + 1] * (above - x) - cz_ref[k] * (x - below))
        return x, change

    def forward_first(ck, carry):
        c = ck // levels
        k = ck % levels
        x, change = operate(ue_ref, c, k, (du0e_ref, du0n_ref))
        heat = jnp.where(c == 0, 1.0, 0.0)
        u1_ref[c, k] = wet_ref[k] * (x + change + heat * src_ref[k])
        return carry


    def forward_second(ck, carry):
        c = ck // levels
        k = ck % levels
        x, change = operate(u1_ref, c, k, (du1e_ref, du1n_ref))
        heat = jnp.where(c == 0, 1.0, 0.0)
        out = wet_ref[k] * (x + change + heat * src_ref[k])
        fin_ref[c, k] = out[:ny, :width]
        return carry


    def backward_second(ck, carry):
        c = ck // levels
        k = ck % levels
        x, change = operate(a_ref, c, k, (dv2e_ref, dv2n_ref))
        b_ref[c, k] = wet_ref[k] * (x + change)
        return carry

    def first_pair(ck, carry):
        forward_first(ck, carry)
        return backward_second(ck, carry)

    lax.fori_loop(0, planes, first_pair, 0, unroll=4)

    def backward_first(ck, carry):
        c = ck // levels
        k = ck % levels
        x, change = operate(b_ref, c, k, (dv1e_ref, dv1n_ref))
        adj_ref[c, k] = (x + change)[:ny, :width]
        return carry

    def second_pair(ck, carry):
        forward_second(ck, carry)
        return backward_first(ck, carry)

    lax.fori_loop(0, planes, second_pair, 0, unroll=4)

    def gradient(k, carry):
        g_east = jnp.zeros((ny, width), jnp.float32)
        g_north = jnp.zeros((ny, width), jnp.float32)
        for c in range(chans):
            g_east = g_east - du0e_ref[c, k] * dv1e_ref[c, k] - du1e_ref[c, k] * dv2e_ref[c, k]
            g_north = g_north - du0n_ref[c, k] * dv1n_ref[c, k] - du1n_ref[c, k] * dv2n_ref[c, k]
        grad_ref[0, k] = gem_ref[k] * g_east
        grad_ref[1, k] = gnm_ref[k] * g_north
        return carry

    lax.fori_loop(0, levels, gradient, 0, unroll=10)


def on_device(tracers, diffusivity, level_count, shelf_mask, cotangent):
    _, chans, levels, ny, width = tracers.shape
    lanes = width + 128
    rows = -(-(ny + 2) // 8) * 8
    full_kappa = gathered_over_scen(diffusivity)
    fields = jnp.concatenate(
        [
            tracers[0].reshape(chans * levels, ny, width),
            cotangent[0].reshape(chans * levels, ny, width),
            full_kappa.reshape(2 * levels, ny, width),
            level_count.astype(jnp.float32)[None],
            shelf_mask.astype(jnp.float32)[None],
        ]
    )
    ext = extended(fields, lanes, rows)
    field = jax.ShapeDtypeStruct((chans, levels, ny, width), jnp.float32)
    plane = pltpu.VMEM((levels, rows, lanes), jnp.float32)
    planes_c = pltpu.VMEM((chans, levels, rows, lanes), jnp.float32)
    diff = pltpu.VMEM((chans, levels, ny, width), jnp.float32)
    mask = pltpu.VMEM((levels, ny, width), jnp.float32)
    final, adjoint, grad = pl.pallas_call(
        diffusion_kernel,
        out_shape=(field, field, jax.ShapeDtypeStruct((2, levels, ny, width), jnp.float32)),
        scratch_shapes=[
            plane,
            plane,
            plane,
            pltpu.VMEM((levels + 1, rows, lanes), jnp.float32),
            plane,
            mask,
            mask,
            planes_c,
            planes_c,
            planes_c,
        ]
        + [diff] * 8,
        compiler_params=pltpu.CompilerParams(vmem_limit_bytes=48 * 1024 * 1024),
        interpret=INTERPRET,
    )(ext)
    kappa_grad = summed_over_scen(grad)
    return (final[None], adjoint[None], kappa_grad)


def gathered_over_scen(block):
    parts = lax.axis_size("scen")
    if parts % 2:
        return lax.all_gather(block, "scen", axis=2, tiled=True)
    kinds, levels, rows, width = block.shape
    me = lax.axis_index("scen")
    core = me % 2
    chip = me // 2
    chips = parts // 2
    got = [block]
    for step in range(1, chips):
        got.append(
            lax.ppermute(block, "scen", [(q, ((q // 2 + step) % chips) * 2 + q % 2) for q in range(parts)])
        )
    same = jnp.stack(got)
    other = lax.ppermute(same, "scen", [(q, q ^ 1) for q in range(parts)])
    by_core = jnp.where(core == 0, jnp.stack([same, other], axis=1), jnp.stack([other, same], axis=1))
    order = (chip - jnp.arange(chips)) % chips
    by_chip = jnp.take(by_core, order, axis=0)
    return by_chip.transpose(2, 3, 0, 1, 4, 5).reshape(kinds, levels, parts * rows, width)


def summed_over_scen(grad):
    parts = lax.axis_size("scen")
    kinds, levels, ny, width = grad.shape
    if parts % 2:
        split = grad.reshape(kinds, levels, parts, ny // parts, width)
        return lax.all_to_all(split, "scen", 2, 2, tiled=True).sum(axis=2)
    me = lax.axis_index("scen")
    core = me % 2
    chip = me // 2
    chips = parts // 2
    split = grad.reshape(kinds, levels, chips, 2, ny // parts, width)
    mine = lax.dynamic_index_in_dim(split, core, axis=3, keepdims=False)
    other = lax.dynamic_index_in_dim(split, 1 - core, axis=3, keepdims=False)
    pair = lax.ppermute(other, "scen", [(q, q ^ 1) for q in range(parts)])
    chip_sum = mine + pair
    total = lax.dynamic_index_in_dim(chip_sum, chip, axis=2, keepdims=False)
    for step in range(1, chips):
        send = lax.dynamic_index_in_dim(chip_sum, (chip + step) % chips, axis=2, keepdims=False)
        total = total + lax.ppermute(
            send, "scen", [(q, ((q // 2 + step) % chips) * 2 + q % 2) for q in range(parts)]
        )
    return total


def solution(mesh):
    placed = (
        P("scen", None, None, None, "space"),
        P(None, None, "scen", "space"),
        P(None, "space"),
        P(None, "space"),
        P("scen", None, None, None, "space"),
    )
    return jax.shard_map(
        on_device,
        mesh=mesh,
        in_specs=placed,
        out_specs=(
            P("scen", None, None, None, "space"),
            P("scen", None, None, None, "space"),
            P(None, None, "scen", "space"),
        ),
        check_vma=False,
    )
```

```python
import jax
import jax.numpy as jnp
from jax import lax
from jax.experimental import pallas as pl
from jax.experimental.pallas import tpu as pltpu
from jax.sharding import PartitionSpec as P

STEPS = 2
HALO = 2

vertical_rate = 0.1
thaw_rate = 0.3

INTERPRET = False


def shifted(x, perm):
    return lax.ppermute(x, "space", perm)


def picker(size, positions):
    where = lax.broadcasted_iota(jnp.int32, (size, len(positions)), 0)
    slot = lax.broadcasted_iota(jnp.int32, (size, len(positions)), 1)
    hit = jnp.zeros((size, len(positions)), jnp.bool_)
    for p, at in enumerate(positions):
        hit = hit | ((slot == p) & (where == at))
    return hit.astype(jnp.float32)


def contract(a, b, dims):
    return lax.dot_general(
        a, b, (dims, ((), ())), precision=lax.Precision.HIGHEST, preferred_element_type=jnp.float32
    )


def extended(fields, lanes, rows):
    n = lax.axis_size("space")
    count, ny, width = fields.shape
    spare = lanes - width
    flat = fields.reshape(count * ny, width)
    edges = contract(picker(width, [width - 2, width - 1, 0, 1]), flat, ((0,), (1,)))
    west = shifted(edges[0:2], [(q, (q + 1) % n) for q in range(n)])
    east = shifted(edges[2:4], [(q, (q - 1) % n) for q in range(n)])
    mirrored = fields[:, ny - 1:ny - 3:-1, ::-1]
    ghost = shifted(mirrored, [(q, n - 1 - q) for q in range(n)])
    top_edges = edges.reshape(4, count, ny)[:, :, ny - 1:ny - 3:-1]
    ghost_east = shifted(top_edges[1::-1], [(q, (n - 2 - q) % n) for q in range(n)])
    ghost_west = shifted(top_edges[3:1:-1], [(q, (n - q) % n) for q in range(n)])
    place = picker(spare, [0, 1, spare - 2, spare - 1]).T
    side = contract(jnp.concatenate([east, west]), place, ((0,), (0,))).reshape(count, ny, spare)
    ghost_halo = jnp.concatenate([ghost_east, ghost_west]).reshape(4, count * 2)
    ghost_side = contract(ghost_halo, place, ((0,), (0,))).reshape(count, 2, spare)
    top = jnp.concatenate([fields, side], axis=-1)
    folded = jnp.concatenate([ghost, ghost_side], axis=-1)
    pad = jnp.zeros((count, rows - ny - 2, lanes), fields.dtype)
    return jnp.concatenate([top, folded, pad], axis=1)


def roll(x, shift, axis):
    return pltpu.roll(x, shift % x.shape[axis], axis)


class Planes:
    def __init__(self, ref, start, levels):
        self.ref = ref
        self.start = start
        self.levels = levels

    def __getitem__(self, index):
        c, k = index
        return self.ref[self.start + c * self.levels + k]


def diffusion_kernel(
    x_ref,
    fin_ref, adj_ref, grad_ref,
    wet_ref, ce_ref, cn_ref, cz_ref, src_ref, gem_ref, gnm_ref, u1_ref, a_ref, b_ref,
    du0e_ref, du0n_ref, du1e_ref, du1n_ref, dv1e_ref, dv1n_ref, dv2e_ref, dv2n_ref,
):
    levels, rows, lanes = wet_ref.shape
    chans, _, ny, width = fin_ref.shape
    row = lax.broadcasted_iota(jnp.int32, (rows, lanes), 0)
    lane = lax.broadcasted_iota(jnp.int32, (rows, lanes), 1)
    planes = chans * levels
    ue_ref = Planes(x_ref, 0, levels)
    ve_ref = Planes(x_ref, planes, levels)
    ke_ref = Planes(x_ref, 2 * planes, levels)
    lev = x_ref[2 * planes + 2 * levels]
    shelf = x_ref[2 * planes + 2 * levels + 1]

    def wet_of(k):
        return (lev > k.astype(jnp.float32)).astype(jnp.float32)

    cz_ref[0] = jnp.zeros((rows, lanes), jnp.float32)

    def setup(k, carry):
        w = wet_of(k)
        w_next = jnp.where(k + 1 < levels, wet_of(k + 1), 0.0)
        w_east = roll(w, -1, 1)
        w_north = roll(w, -1, 0)
        ke = ke_ref[0, k]
        ke_sel = jnp.where(row >= ny, roll(ke, -1, 1), ke)
        east_mask = w * w_east
        ce_ref[k] = ke_sel * east_mask
        kn = ke_ref[1, k]
        kn_up = roll(kn, -1, 0)
        kn_sel = jnp.where(
            row < ny - 1, kn, jnp.where(row == ny - 1, 0.5 * (kn + kn_up), jnp.where(row == ny, kn_up, 0.0))
        )
        north_mask = w * w_north
        cn_ref[k] = kn_sel * north_mask
        cz_ref[k + 1] = vertical_rate * w * w_next
        src_ref[k] = thaw_rate * shelf * w * (1.0 - w_next)
        wet_ref[k] = w
        gem_ref[k] = east_mask[:ny, :width]
        gnm_ref[k] = jnp.where(row < ny - 1, north_mask, 0.5 * north_mask)[:ny, :width]
        for c in range(chans):
            a_ref[c, k] = w * ve_ref[c, k]
        return carry

    lax.fori_loop(0, levels, setup, 0, unroll=10)

    def operate(x_ref, c, k, diffs=None):
        x = x_ref[c, k]
        above = x_ref[c, jnp.minimum(k + 1, levels - 1)]
        below = x_ref[c, jnp.maximum(k - 1, 0)]
        d_east = roll(x, -1, 1) - x
        d_north = roll(x, -1, 0) - x
        if diffs is not None:
            diffs[0][c, k] = d_east[:ny, :width]
            diffs[1][c, k] = d_north[:ny, :width]
        east = ce_ref[k] * d_east
        north = cn_ref[k] * d_north
        change = (east - roll(east, 1, 1)) + (north - roll(north, 1, 0))
        change = change + (cz_ref[k + 1] * (above - x) - cz_ref[k] * (x - below))
        return x, change

    def forward_first(ck, carry):
        c = ck // levels
        k = ck % levels
        x, change = operate(ue_ref, c, k, (du0e_ref, du0n_ref))
        heat = jnp.where(c == 0, 1.0, 0.0)
        u1_ref[c, k] = wet_ref[k] * (x + change + heat * src_ref[k])
        return carry


    def forward_second(ck, carry):
        c = ck // levels
        k = ck % levels
        x, change = operate(u1_ref, c, k, (du1e_ref, du1n_ref))
        heat = jnp.where(c == 0, 1.0, 0.0)
        out = wet_ref[k] * (x + change + heat * src_ref[k])
        fin_ref[c, k] = out[:ny, :width]
        return carry


    def backward_second(ck, carry):
        c = ck // levels
        k = ck % levels
        x, change = operate(a_ref, c, k, (dv2e_ref, dv2n_ref))
        b_ref[c, k] = wet_ref[k] * (x + change)
        return carry

    def first_pair(ck, carry):
        forward_first(ck, carry)
        return backward_second(ck, carry)

    lax.fori_loop(0, planes, first_pair, 0, unroll=4)

    def backward_first(ck, carry):
        c = ck // levels
        k = ck % levels
        x, change = operate(b_ref, c, k, (dv1e_ref, dv1n_ref))
        adj_ref[c, k] = (x + change)[:ny, :width]
        return carry

    def second_pair(ck, carry):
        forward_second(ck, carry)
        return backward_first(ck, carry)

    lax.fori_loop(0, planes, second_pair, 0, unroll=8)

    def gradient(k, carry):
        g_east = jnp.zeros((ny, width), jnp.float32)
        g_north = jnp.zeros((ny, width), jnp.float32)
        for c in range(chans):
            g_east = g_east - du0e_ref[c, k] * dv1e_ref[c, k] - du1e_ref[c, k] * dv2e_ref[c, k]
            g_north = g_north - du0n_ref[c, k] * dv1n_ref[c, k] - du1n_ref[c, k] * dv2n_ref[c, k]
        grad_ref[0, k] = gem_ref[k] * g_east
        grad_ref[1, k] = gnm_ref[k] * g_north
        return carry

    lax.fori_loop(0, levels, gradient, 0, unroll=True)


def on_device(tracers, diffusivity, level_count, shelf_mask, cotangent):
    _, chans, levels, ny, width = tracers.shape
    lanes = width + 128
    rows = -(-(ny + 2) // 8) * 8
    full_kappa = gathered_over_scen(diffusivity)
    fields = jnp.concatenate(
        [
            tracers[0].reshape(chans * levels, ny, width),
            cotangent[0].reshape(chans * levels, ny, width),
            full_kappa.reshape(2 * levels, ny, width),
            level_count.astype(jnp.float32)[None],
            shelf_mask.astype(jnp.float32)[None],
        ]
    )
    ext = extended(fields, lanes, rows)
    field = jax.ShapeDtypeStruct((chans, levels, ny, width), jnp.float32)
    plane = pltpu.VMEM((levels, rows, lanes), jnp.float32)
    planes_c = pltpu.VMEM((chans, levels, rows, lanes), jnp.float32)
    diff = pltpu.VMEM((chans, levels, ny, width), jnp.float32)
    mask = pltpu.VMEM((levels, ny, width), jnp.float32)
    final, adjoint, grad = pl.pallas_call(
        diffusion_kernel,
        out_shape=(field, field, jax.ShapeDtypeStruct((2, levels, ny, width), jnp.float32)),
        scratch_shapes=[
            plane,
            plane,
            plane,
            pltpu.VMEM((levels + 1, rows, lanes), jnp.float32),
            plane,
            mask,
            mask,
            planes_c,
            planes_c,
            planes_c,
        ]
        + [diff] * 8,
        compiler_params=pltpu.CompilerParams(vmem_limit_bytes=48 * 1024 * 1024),
        interpret=INTERPRET,
    )(ext)
    kappa_grad = summed_over_scen(grad)
    return (final[None], adjoint[None], kappa_grad)


def gathered_over_scen(block):
    parts = lax.axis_size("scen")
    if parts % 2:
        return lax.all_gather(block, "scen", axis=2, tiled=True)
    kinds, levels, rows, width = block.shape
    me = lax.axis_index("scen")
    core = me % 2
    chip = me // 2
    chips = parts // 2
    got = [block]
    for step in range(1, chips):
        got.append(
            lax.ppermute(block, "scen", [(q, ((q // 2 + step) % chips) * 2 + q % 2) for q in range(parts)])
        )
    same = jnp.stack(got)
    other = lax.ppermute(same, "scen", [(q, q ^ 1) for q in range(parts)])
    by_core = jnp.where(core == 0, jnp.stack([same, other], axis=1), jnp.stack([other, same], axis=1))
    order = (chip - jnp.arange(chips)) % chips
    by_chip = jnp.take(by_core, order, axis=0)
    return by_chip.transpose(2, 3, 0, 1, 4, 5).reshape(kinds, levels, parts * rows, width)


def summed_over_scen(grad):
    parts = lax.axis_size("scen")
    kinds, levels, ny, width = grad.shape
    if parts % 2:
        split = grad.reshape(kinds, levels, parts, ny // parts, width)
        return lax.all_to_all(split, "scen", 2, 2, tiled=True).sum(axis=2)
    me = lax.axis_index("scen")
    core = me % 2
    chip = me // 2
    chips = parts // 2
    split = grad.reshape(kinds, levels, chips, 2, ny // parts, width)
    mine = lax.dynamic_index_in_dim(split, core, axis=3, keepdims=False)
    other = lax.dynamic_index_in_dim(split, 1 - core, axis=3, keepdims=False)
    pair = lax.ppermute(other, "scen", [(q, q ^ 1) for q in range(parts)])
    chip_sum = mine + pair
    total = lax.dynamic_index_in_dim(chip_sum, chip, axis=2, keepdims=False)
    for step in range(1, chips):
        send = lax.dynamic_index_in_dim(chip_sum, (chip + step) % chips, axis=2, keepdims=False)
        total = total + lax.ppermute(
            send, "scen", [(q, ((q // 2 + step) % chips) * 2 + q % 2) for q in range(parts)]
        )
    return total


def solution(mesh):
    placed = (
        P("scen", None, None, None, "space"),
        P(None, None, "scen", "space"),
        P(None, "space"),
        P(None, "space"),
        P("scen", None, None, None, "space"),
    )
    return jax.shard_map(
        on_device,
        mesh=mesh,
        in_specs=placed,
        out_specs=(
            P("scen", None, None, None, "space"),
            P("scen", None, None, None, "space"),
            P(None, None, "scen", "space"),
        ),
        check_vma=False,
    )
```
